32 devices in a mesh: ctx: 8 (over y, x, core), uly: 4 (over z).
Axes of the slice: x: 2, y: 2, z: 4, core: 2. Of those that a mesh axis runs over, the one named last changes fastest.
Arguments:
- query_rows: bfloat16 [3072, 6144], P('ctx', 'uly'), may hold values from -150 to 150
- key_rows: bfloat16 [3072, 1024], P('ctx'), may hold values from -7 to 7
- value_rows: bfloat16 [3072, 1024], P('ctx'), may hold values from -6 to 6
- out_grad: bfloat16 [3072, 6144], P('ctx', 'uly'), may hold values from -96 to 96
- block_list: int32 [24, 8], replicated, may hold values from 0 to 23, as said below
Outputs:
- query_grad: bfloat16 [3072, 6144], P(('ctx', 'uly'))
- key_grad: bfloat16 [3072, 1024], P(('ctx', 'uly'))
- value_grad: bfloat16 [3072, 1024], P(('ctx', 'uly'))
The draws below stay inside these ranges and needn't reach their ends.
Inputs may be any that keep to these rules, and one draw needn't show every extreme that they name: `block_list`: row i holds (i - 1) mod 24, i, (i + 1) mod 24 in columns 0 to 2 and 0, 1 in columns 3 and 4. Columns 5 to 7 hold blocks j whose index j // 3 is none of i // 3 and its two cyclic neighbours; the rows of one index name at most 2 blocks of any one other index there, and some index reaches 2.
All inputs are finite; a program needn't handle non-finite values.
Results may differ from the reference program's by a relative error of at most 0.015.
Values may be sent and summed in bfloat16 or wider, within the bound.
No kernel may reach another device: no remote copies, remote signals or barrier semaphores. Data moves between devices by JAX's collectives and lax.ppermute only.
A program may use at most 64 MiB of HBM per device.

```python
import math
import jax
import jax.numpy as jnp
from jax import lax

HD = 128
HEADS = 48
KVH = 8
BLK = 128
QB_DEV = 3
NQB = 24
SEQ = 3072
N_CTX = 8
N_ULY = 4


def key_table(key):
    base = jax.random.fold_in(key, 11)
    first_key = jax.random.fold_in(base, 0)
    table = jnp.clip(jax.random.normal(first_key, (SEQ, KVH, HD), jnp.float32), -6.0, 6.0)
    return table


def draw_key_rows(key, part):
    return key_table(key).reshape(SEQ, KVH * HD).astype(jnp.bfloat16)


def draw_query_rows(key, part):
    first_key = jax.random.fold_in(jax.random.fold_in(key, 23), 0)
    table = jnp.clip(jax.random.normal(first_key, (SEQ, HEADS, HD), jnp.float32), -6.0, 6.0)
    return table.reshape(SEQ, HEADS * HD).astype(jnp.bfloat16)


def draw_block_list(key, part):
    rand_count = 3 * QB_DEV
    others = N_CTX - 3
    base = jax.random.fold_in(key, 7)

    def one_shard(shard_index):
        shard_key = jax.random.fold_in(base, shard_index)
        order_key, spread_key, inside_key = jax.random.split(shard_key, 3)
        order = jax.random.permutation(order_key, others)
        spread = jax.random.permutation(spread_key, rand_count)
        owners = (shard_index + 2 + order[spread % others]) % N_CTX
        inside = jax.random.randint(inside_key, (rand_count,), 0, QB_DEV)
        return (owners * QB_DEV + inside).reshape(QB_DEV, 3)
    random_cols = jax.vmap(one_shard)(jnp.arange(N_CTX, dtype=jnp.int32)).reshape(NQB, 3)
    rows = jnp.arange(NQB, dtype=jnp.int32)
    window = jnp.stack([(rows - 1) % NQB, rows, (rows + 1) % NQB], axis=1)
    globals_cols = jnp.stack([jnp.zeros_like(rows), jnp.ones_like(rows)], axis=1)
    return jnp.concatenate([window, globals_cols, random_cols], axis=1).astype(jnp.int32)


def level_of(rng, extent, cuts, least, top_value):
    def one(axis_at, shards_of):
        draws = jax.random.uniform(jax.random.fold_in(jax.random.fold_in(rng, 6), axis_at), (shards_of,), jnp.float32, least / len(cuts), top_value / len(cuts))
        return jnp.repeat(jnp.exp(draws), extent[axis_at] // shards_of).reshape((-1,) + (1,) * (len(extent) - axis_at - 1))

    loudness = one(*cuts[0])
    for cut in cuts[1:]:
        loudness = loudness * one(*cut)
    return loudness


def scatter_about(stream_key, extent, width, bound, cuts=(), held_as=jnp.bfloat16):
    values = width * jax.random.normal(stream_key, extent, jnp.float32)
    if cuts:
        values = values * level_of(stream_key, extent, cuts, -0.22, 0.18)
    return jnp.clip(values, -bound, bound).astype(held_as)


def setup_inputs(seed: int = 0) -> dict:
    key_of = jax.random.split(jax.random.key(seed), 6)
    return {
        "query_rows": draw_query_rows(jax.random.fold_in(key_of[5], 71), 0),
        "key_rows": draw_key_rows(jax.random.fold_in(key_of[5], 71), 0),
        "value_rows": scatter_about(key_of[2], (SEQ, KVH * HD), 1.0, 6.0, ((0, 8),)),
        "out_grad": scatter_about(key_of[3], (SEQ, HEADS * HD), 16.0, 96.0, ((0, 8), (1, 4))),
        "block_list": draw_block_list(jax.random.fold_in(key_of[5], 71), 0),
    }


def rounded_copy(values_in):
    narrow = lax.optimization_barrier(values_in.astype(jnp.bfloat16))
    return narrow.astype(jnp.float32)

def reference(query_rows, key_rows, value_rows, out_grad, block_list):
    scaling = 1.0 / math.sqrt(HD)
    group_size = HEADS // KVH
    run_size = min(HEADS // N_ULY, group_size)
    run_count = HEADS // run_size
    query_four = query_rows.reshape(NQB, BLK, HEADS, HD)
    key_four = key_rows.reshape(NQB, BLK, KVH, HD)
    value_four = value_rows.reshape(NQB, BLK, KVH, HD)
    grad_four = out_grad.reshape(NQB, BLK, HEADS, HD)
    columns = jnp.arange(8, dtype=jnp.int32)
    global_cols = (columns == 3) | (columns == 4)

    def one_block(totals, block_index):
        key_acc, value_acc = totals
        queries = lax.dynamic_index_in_dim(query_four, block_index, 0, keepdims=False).astype(jnp.float32)
        out_block = lax.dynamic_index_in_dim(grad_four, block_index, 0, keepdims=False).astype(jnp.float32)
        listed = lax.dynamic_index_in_dim(block_list, block_index, 0, keepdims=False).astype(jnp.int32)
        key_sel = jnp.take(key_four, listed, axis=0)
        value_sel = jnp.take(value_four, listed, axis=0)
        key_heads = jnp.repeat(key_sel, group_size, axis=2).reshape(8 * BLK, HEADS, HD).astype(jnp.float32)
        value_heads = jnp.repeat(value_sel, group_size, axis=2).reshape(8 * BLK, HEADS, HD).astype(jnp.float32)
        scores = jnp.einsum('qhd,nhd->hqn', queries, key_heads, precision=lax.Precision.HIGHEST) * scaling
        row_peak = lax.optimization_barrier(jnp.max(scores, axis=-1, keepdims=True))
        lifted = jnp.exp(scores - row_peak)
        weights = lifted / lax.optimization_barrier(jnp.sum(lifted, axis=-1, keepdims=True))
        narrow_weights = rounded_copy(weights)
        attended = jnp.einsum('hqn,nhd->qhd', narrow_weights, value_heads, precision=lax.Precision.HIGHEST)
        row_delta = lax.optimization_barrier(jnp.sum(out_block * attended, axis=-1))
        weight_grad = jnp.einsum('qhd,nhd->hqn', out_block, value_heads, precision=lax.Precision.HIGHEST)
        score_grad = rounded_copy(weights * (weight_grad - jnp.transpose(row_delta)[:, :, None]) * scaling)
        query_part = jnp.einsum('hqn,nhd->qhd', score_grad, key_heads, precision=lax.Precision.HIGHEST)
        key_terms = jnp.einsum('hqn,qhd->nhd', score_grad, queries, precision=lax.Precision.HIGHEST)
        value_terms = jnp.einsum('hqn,qhd->nhd', narrow_weights, out_block, precision=lax.Precision.HIGHEST)
        owners = listed // QB_DEV
        remote = (owners != block_index // QB_DEV) & jnp.logical_not(global_cols)

        def settle(slot_terms):
            run_sums = slot_terms.reshape(8, BLK, run_count, run_size, HD).sum(axis=3)
            run_sums = jnp.where(remote[:, None, None, None], rounded_copy(run_sums), run_sums)
            return run_sums.reshape(8, BLK, KVH, run_count // KVH, HD).sum(axis=3)
        key_acc = key_acc.at[listed].add(settle(key_terms))
        value_acc = value_acc.at[listed].add(settle(value_terms))
        return ((key_acc, value_acc), query_part.astype(jnp.bfloat16))
    zeros_acc = jnp.zeros((NQB, BLK, KVH, HD), jnp.float32)
    sums_out, query_out = lax.scan(one_block, (zeros_acc, zeros_acc), jnp.arange(NQB, dtype=jnp.int32))
    query_grad = query_out.reshape(SEQ, HEADS * HD)
    key_grad = sums_out[0].reshape(SEQ, KVH * HD).astype(jnp.bfloat16)
    value_grad = sums_out[1].reshape(SEQ, KVH * HD).astype(jnp.bfloat16)
    return (query_grad, key_grad, value_grad)
```

```python
import functools
import math

import jax
import jax.numpy as jnp
from jax import lax
from jax.experimental import pallas as pl
from jax.experimental.pallas import tpu as pltpu
from jax.sharding import PartitionSpec as P

HD = 128
KVH = 8
BLK = 128
GROUP = 6
SLOTS = 8


def attention_kernel(
    blk_ref, dst_ref, kind_ref,
    q_ref, do_ref, k_ref, v_ref,
    dq_ref, loc_ref, far_ref,
    kc_ref, vc_ref, loc_acc, far_acc,
    *, hpk, kv_here, nb,
):
    g = pl.program_id(0)
    b = pl.program_id(1)
    scale = 1.0 / math.sqrt(HD)

    @pl.when((g == 0) & (b == 0))
    def _():
        loc_acc[...] = jnp.zeros_like(loc_acc)
        far_acc[...] = jnp.zeros_like(far_acc)

    for s in range(SLOTS):
        row = pl.multiple_of(blk_ref[b * SLOTS + s] * BLK, BLK)
        kc_ref[s * BLK:(s + 1) * BLK, :] = k_ref[pl.ds(row, BLK), :]
        vc_ref[s * BLK:(s + 1) * BLK, :] = v_ref[pl.ds(row, BLK), :]

    kc = kc_ref[...]
    vc = vc_ref[...]
    qs = jnp.concatenate([q_ref[:, h * HD:(h + 1) * HD] for h in range(hpk)], axis=0)
    dos = jnp.concatenate([do_ref[:, h * HD:(h + 1) * HD] for h in range(hpk)], axis=0)
    nt = (((1,), (1,)), ((), ()))
    tn = (((0,), (0,)), ((), ()))
    scores = lax.dot_general(qs, kc, nt, preferred_element_type=jnp.float32) * scale
    peak = jnp.max(scores, axis=1, keepdims=True)
    lifted = jnp.exp(scores - peak)
    probs = lifted / jnp.sum(lifted, axis=1, keepdims=True)
    probs_b = probs.astype(jnp.bfloat16)
    attended = jnp.dot(probs_b, vc, preferred_element_type=jnp.float32)
    delta = jnp.sum(dos.astype(jnp.float32) * attended, axis=1, keepdims=True)
    dprobs = lax.dot_general(dos, vc, nt, preferred_element_type=jnp.float32)
    dscores = (probs * (dprobs - delta) * scale).astype(jnp.bfloat16)
    dq = jnp.dot(dscores, kc, preferred_element_type=jnp.float32)
    for h in range(hpk):
        dq_ref[:, h * HD:(h + 1) * HD] = dq[h * BLK:(h + 1) * BLK].astype(jnp.bfloat16)
    kterm = lax.dot_general(dscores, qs, tn, preferred_element_type=jnp.float32)
    vterm = lax.dot_general(probs_b, dos, tn, preferred_element_type=jnp.float32)

    for s in range(SLOTS):
        kind = kind_ref[b * SLOTS + s]
        row = pl.multiple_of(dst_ref[b * SLOTS + s] * BLK, BLK)
        kt = kterm[s * BLK:(s + 1) * BLK]
        vt = vterm[s * BLK:(s + 1) * BLK]
        rounded = kind == 0
        kt = jnp.where(rounded, kt.astype(jnp.bfloat16).astype(jnp.float32), kt)
        vt = jnp.where(rounded, vt.astype(jnp.bfloat16).astype(jnp.float32), vt)

        @pl.when(kind == 2)
        def _():
            loc_acc[g, pl.ds(row, BLK), :] += kt
            loc_acc[kv_here + g, pl.ds(row, BLK), :] += vt

        @pl.when(kind != 2)
        def _():
            far_acc[g, pl.ds(row, BLK), :] += kt
            far_acc[kv_here + g, pl.ds(row, BLK), :] += vt

    @pl.when((g == kv_here - 1) & (b == nb - 1))
    def _():
        for j in range(2 * kv_here):
            loc_ref[:, j * HD:(j + 1) * HD] = loc_acc[j]
            far_ref[:, j * HD:(j + 1) * HD] = far_acc[j].astype(jnp.bfloat16)


def shards(query_rows, key_rows, value_rows, out_grad, block_list):
    shard_index = lax.axis_index("ctx")
    lane_index = lax.axis_index("uly")
    nb = key_rows.shape[0] // BLK
    seq = block_list.shape[0] * BLK
    heads_here = query_rows.shape[1] // HD
    kv_here = max(1, heads_here // GROUP)
    hpk = heads_here // kv_here
    width = 2 * kv_here * HD
    first_kv = lane_index * heads_here // GROUP
    key_own = lax.dynamic_slice_in_dim(key_rows, first_kv * HD, kv_here * HD, axis=1)
    value_own = lax.dynamic_slice_in_dim(value_rows, first_kv * HD, kv_here * HD, axis=1)
    kv_own = jnp.concatenate([key_own, value_own], axis=1)
    kv_all = lax.all_gather(kv_own, "ctx", axis=0, tiled=True)

    rows = lax.dynamic_slice_in_dim(block_list, shard_index * nb, nb, axis=0).astype(jnp.int32)
    owner = rows // nb
    cols = jnp.arange(SLOTS)[None, :]
    is_global = (cols == 3) | (cols == 4)
    local = owner == shard_index
    remote = jnp.logical_not(local) & jnp.logical_not(is_global)
    kind = jnp.where(local, 2, jnp.where(remote, 0, 1)).astype(jnp.int32).reshape(-1)
    dst = jnp.where(local, rows - shard_index * nb, rows).astype(jnp.int32).reshape(-1)
    blk = rows.reshape(-1)

    kernel = functools.partial(attention_kernel, hpk=hpk, kv_here=kv_here, nb=nb)
    grid_spec = pltpu.PrefetchScalarGridSpec(
        num_scalar_prefetch=3,
        grid=(kv_here, nb),
        in_specs=[
            pl.BlockSpec((BLK, hpk * HD), lambda g, b, *_: (b, g)),
            pl.BlockSpec((BLK, hpk * HD), lambda g, b, *_: (b, g)),
            pl.BlockSpec((seq, HD), lambda g, b, *_: (0, g)),
            pl.BlockSpec((seq, HD), lambda g, b, *_: (0, kv_here + g)),
        ],
        out_specs=[
            pl.BlockSpec((BLK, hpk * HD), lambda g, b, *_: (b, g)),
            pl.BlockSpec((nb * BLK, width), lambda g, b, *_: (0, 0)),
            pl.BlockSpec((seq, width), lambda g, b, *_: (0, 0)),
        ],
        scratch_shapes=[
            pltpu.VMEM((SLOTS * BLK, HD), jnp.bfloat16),
            pltpu.VMEM((SLOTS * BLK, HD), jnp.bfloat16),
            pltpu.VMEM((2 * kv_here, nb * BLK, HD), jnp.float32),
            pltpu.VMEM((2 * kv_here, seq, HD), jnp.float32),
        ],
    )
    dq, loc, far = pl.pallas_call(
        kernel,
        grid_spec=grid_spec,
        out_shape=[
            jax.ShapeDtypeStruct((nb * BLK, heads_here * HD), jnp.bfloat16),
            jax.ShapeDtypeStruct((nb * BLK, width), jnp.float32),
            jax.ShapeDtypeStruct((seq, width), jnp.bfloat16),
        ],
        compiler_params=pltpu.CompilerParams(dimension_semantics=("arbitrary", "arbitrary")),
    )(blk, dst, kind, query_rows, out_grad, kv_all, kv_all)

    got = lax.psum_scatter(far, "ctx", scatter_dimension=0, tiled=True)
    kv_grad = (got.astype(jnp.float32) + loc).astype(jnp.bfloat16)

    query_out = lax.all_to_all(dq, "uly", split_axis=0, concat_axis=1, tiled=True)
    kv_seq = lax.all_to_all(kv_grad, "uly", split_axis=0, concat_axis=1, tiled=True)
    rows_here = kv_seq.shape[0]
    lane_count = kv_seq.shape[1] // width
    spread = kv_seq.reshape(rows_here, lane_count, 2, kv_here * HD)

    def gather_heads(part):
        if heads_here >= GROUP:
            return part.reshape(rows_here, KVH * HD)
        lanes_per = GROUP // heads_here
        merged = part.astype(jnp.float32).reshape(rows_here, KVH, lanes_per, HD).sum(axis=2)
        return merged.reshape(rows_here, KVH * HD).astype(jnp.bfloat16)

    return (query_out, gather_heads(spread[:, :, 0]), gather_heads(spread[:, :, 1]))


def solution(mesh):
    return jax.shard_map(
        shards,
        mesh=mesh,
        in_specs=(P("ctx", "uly"), P("ctx", None), P("ctx", None), P("ctx", "uly"), P()),
        out_specs=(P(("ctx", "uly"), None), P(("ctx", "uly"), None), P(("ctx", "uly"), None)),
        check_vma=False,
    )
```

```python
import functools
import math

import jax
import jax.numpy as jnp
from jax import lax
from jax.experimental import pallas as pl
from jax.experimental.pallas import tpu as pltpu
from jax.sharding import PartitionSpec as P

HD = 128
KVH = 8
BLK = 128
GROUP = 6
SLOTS = 8


def remote_plan(block_list, shard_count, block_count):
    listed = block_list.reshape(shard_count, block_count, SLOTS)
    wanted = jnp.concatenate(
        [
            listed[:, 0, 0:1],
            listed[:, block_count - 1, 2:3],
            listed[:, :, 5:8].reshape(shard_count, 3 * block_count),
        ],
        axis=1,
    )
    owners = wanted // block_count
    inside = wanted - owners * block_count
    slot_count = wanted.shape[1]
    same_owner = owners[:, :, None] == owners[:, None, :]
    earlier = jnp.arange(slot_count)[None, :] < jnp.arange(slot_count)[:, None]
    places = jnp.sum((same_owner & earlier[None]).astype(jnp.int32), axis=2)
    return (owners, inside, places)


def attention_kernel(
    kind_ref, idx_ref,
    q_ref, do_ref, ok_ref, ov_ref, fk_ref, fv_ref, gk_ref, gv_ref,
    dq_ref, loc_ref, back_ref, gsum_ref,
    kc_ref, vc_ref, loc_acc, back_acc, g_acc,
    *, hpk, kv_here, nb,
):
    g = pl.program_id(0)
    b = pl.program_id(1)
    scale = 1.0 / math.sqrt(HD)

    @pl.when((g == 0) & (b == 0))
    def _():
        loc_acc[...] = jnp.zeros_like(loc_acc)
        back_acc[...] = jnp.zeros_like(back_acc)
        g_acc[...] = jnp.zeros_like(g_acc)

    for s in range(SLOTS):
        kind = kind_ref[b * SLOTS + s]
        row = pl.multiple_of(idx_ref[b * SLOTS + s] * BLK, BLK)
        for code, tk, tv in ((2, ok_ref, ov_ref), (0, fk_ref, fv_ref), (1, gk_ref, gv_ref)):
            @pl.when(kind == code)
            def _():
                kc_ref[s * BLK:(s + 1) * BLK, :] = tk[pl.ds(row, BLK), :]
                vc_ref[s * BLK:(s + 1) * BLK, :] = tv[pl.ds(row, BLK), :]

    kc = kc_ref[...]
    vc = vc_ref[...]
    qs = jnp.concatenate([q_ref[:, h * HD:(h + 1) * HD] for h in range(hpk)], axis=0)
    dos = jnp.concatenate([do_ref[:, h * HD:(h + 1) * HD] for h in range(hpk)], axis=0)
    nt = (((1,), (1,)), ((), ()))
    tn = (((0,), (0,)), ((), ()))
    scores = lax.dot_general(qs, kc, nt, preferred_element_type=jnp.float32) * scale
    peak = jnp.max(scores, axis=1, keepdims=True)
    lifted = jnp.exp(scores - peak)
    probs = lifted / jnp.sum(lifted, axis=1, keepdims=True)
    probs_b = probs.astype(jnp.bfloat16)
    attended = jnp.dot(probs_b, vc, preferred_element_type=jnp.float32)
    delta = jnp.sum(dos.astype(jnp.float32) * attended, axis=1, keepdims=True)
    dprobs = lax.dot_general(dos, vc, nt, preferred_element_type=jnp.float32)
    dscores = (probs * (dprobs - delta) * scale).astype(jnp.bfloat16)
    dq = jnp.dot(dscores, kc, preferred_element_type=jnp.float32)
    for h in range(hpk):
        dq_ref[:, h * HD:(h + 1) * HD] = dq[h * BLK:(h + 1) * BLK].astype(jnp.bfloat16)
    kterm = lax.dot_general(dscores, qs, tn, preferred_element_type=jnp.float32)
    vterm = lax.dot_general(probs_b, dos, tn, preferred_element_type=jnp.float32)

    for s in range(SLOTS):
        kind = kind_ref[b * SLOTS + s]
        row = pl.multiple_of(idx_ref[b * SLOTS + s] * BLK, BLK)
        kt = kterm[s * BLK:(s + 1) * BLK]
        vt = vterm[s * BLK:(s + 1) * BLK]

        @pl.when(kind == 2)
        def _():
            loc_acc[g, pl.ds(row, BLK), :] += kt
            loc_acc[kv_here + g, pl.ds(row, BLK), :] += vt

        @pl.when(kind == 1)
        def _():
            g_acc[g, pl.ds(row, BLK), :] += kt
            g_acc[kv_here + g, pl.ds(row, BLK), :] += vt

        @pl.when(kind == 0)
        def _():
            back_acc[g, pl.ds(row, BLK), :] += kt.astype(jnp.bfloat16).astype(jnp.float32)
            back_acc[kv_here + g, pl.ds(row, BLK), :] += vt.astype(jnp.bfloat16).astype(jnp.float32)

    @pl.when((g == kv_here - 1) & (b == nb - 1))
    def _():
        for j in range(2 * kv_here):
            loc_ref[:, j * HD:(j + 1) * HD] = loc_acc[j]
            back_ref[:, j * HD:(j + 1) * HD] = back_acc[j].astype(jnp.bfloat16)
            gsum_ref[:, j * HD:(j + 1) * HD] = g_acc[j].astype(jnp.bfloat16)


def shards(query_rows, key_rows, value_rows, out_grad, block_list):
    shard_index = lax.axis_index("ctx")
    lane_index = lax.axis_index("uly")
    shard_count = lax.axis_size("ctx")
    nb = key_rows.shape[0] // BLK
    heads_here = query_rows.shape[1] // HD
    kv_here = max(1, heads_here // GROUP)
    hpk = heads_here // kv_here
    width = 2 * kv_here * HD
    capacity = (3 * nb + shard_count - 4) // (shard_count - 3)
    far_count = shard_count * capacity
    first_kv = lane_index * heads_here // GROUP
    key_own = lax.dynamic_slice_in_dim(key_rows, first_kv * HD, kv_here * HD, axis=1)
    value_own = lax.dynamic_slice_in_dim(value_rows, first_kv * HD, kv_here * HD, axis=1)
    kv_own = jnp.concatenate([key_own, value_own], axis=1)

    owners, inside, places = remote_plan(block_list, shard_count, nb)
    from_here = owners == shard_index
    send_pick = (
        from_here[:, :, None] & (places[:, :, None] == jnp.arange(capacity)[None, None, :])
    ).astype(jnp.bfloat16)
    send_block = (inside[:, :, None] == jnp.arange(nb)[None, None, :]).astype(jnp.bfloat16)
    selector = jnp.einsum(
        "ric,rib->rcb", send_pick, send_block, preferred_element_type=jnp.float32
    ).astype(jnp.bfloat16).reshape(far_count, nb)
    send = jnp.einsum(
        "kb,btx->ktx", selector, kv_own.reshape(nb, BLK, width),
        preferred_element_type=jnp.float32,
    ).astype(jnp.bfloat16).reshape(far_count * BLK, width)
    got = lax.all_to_all(send, "ctx", split_axis=0, concat_axis=0, tiled=True)
    is_root = shard_index == 0
    heads = lax.psum(jnp.where(is_root, kv_own[0:2 * BLK], jnp.zeros_like(kv_own[0:2 * BLK])), "ctx")

    my_owner = lax.dynamic_index_in_dim(owners, shard_index, 0, keepdims=False)
    my_place = lax.dynamic_index_in_dim(places, shard_index, 0, keepdims=False)
    target = my_owner * capacity + my_place
    rows = lax.dynamic_slice_in_dim(block_list, shard_index * nb, nb, axis=0).astype(jnp.int32)
    local = rows // nb == shard_index
    cols = jnp.arange(SLOTS)[None, :]
    blocks = jnp.arange(nb)[:, None]
    is_global = (cols == 3) | (cols == 4)
    wanted_at = jnp.where(cols == 0, 0, jnp.where(cols == 2, 1, 2 + 3 * blocks + cols - 5))
    wanted_at = jnp.clip(wanted_at, 0, target.shape[0] - 1)
    far_index = jnp.take(target, wanted_at)
    kind = jnp.where(local, 2, jnp.where(is_global, 1, 0)).astype(jnp.int32)
    index = jnp.where(local, rows - shard_index * nb, jnp.where(is_global, rows, far_index))
    index = jnp.clip(index, 0, jnp.where(local, nb - 1, jnp.where(is_global, 1, far_count - 1)))
    kind = kind.reshape(-1)
    index = index.astype(jnp.int32).reshape(-1)

    kernel = functools.partial(attention_kernel, hpk=hpk, kv_here=kv_here, nb=nb)

    def columns(count):
        return [
            pl.BlockSpec((count, HD), lambda g, b, *_: (0, g)),
            pl.BlockSpec((count, HD), lambda g, b, *_: (0, kv_here + g)),
        ]

    grid_spec = pltpu.PrefetchScalarGridSpec(
        num_scalar_prefetch=2,
        grid=(kv_here, nb),
        in_specs=[
            pl.BlockSpec((BLK, hpk * HD), lambda g, b, *_: (b, g)),
            pl.BlockSpec((BLK, hpk * HD), lambda g, b, *_: (b, g)),
        ] + columns(nb * BLK) + columns(far_count * BLK) + columns(2 * BLK),
        out_specs=[
            pl.BlockSpec((BLK, hpk * HD), lambda g, b, *_: (b, g)),
            pl.BlockSpec((nb * BLK, width), lambda g, b, *_: (0, 0)),
            pl.BlockSpec((far_count * BLK, width), lambda g, b, *_: (0, 0)),
            pl.BlockSpec((2 * BLK, width), lambda g, b, *_: (0, 0)),
        ],
        scratch_shapes=[
            pltpu.VMEM((SLOTS * BLK, HD), jnp.bfloat16),
            pltpu.VMEM((SLOTS * BLK, HD), jnp.bfloat16),
            pltpu.VMEM((2 * kv_here, nb * BLK, HD), jnp.float32),
            pltpu.VMEM((2 * kv_here, far_count * BLK, HD), jnp.float32),
            pltpu.VMEM((2 * kv_here, 2 * BLK, HD), jnp.float32),
        ],
    )
    dq, loc, back, gsum = pl.pallas_call(
        kernel,
        grid_spec=grid_spec,
        out_shape=[
            jax.ShapeDtypeStruct((nb * BLK, heads_here * HD), jnp.bfloat16),
            jax.ShapeDtypeStruct((nb * BLK, width), jnp.float32),
            jax.ShapeDtypeStruct((far_count * BLK, width), jnp.bfloat16),
            jax.ShapeDtypeStruct((2 * BLK, width), jnp.bfloat16),
        ],
        compiler_params=pltpu.CompilerParams(dimension_semantics=("arbitrary", "arbitrary")),
    )(kind, index, query_rows, out_grad, kv_own, kv_own, got, got, heads, heads)

    ret = lax.all_to_all(back, "ctx", split_axis=0, concat_axis=0, tiled=True)
    head_sum = lax.psum(gsum, "ctx")
    added = jnp.einsum(
        "kb,ktx->btx", selector, ret.reshape(far_count, BLK, width),
        preferred_element_type=jnp.float32,
    ).reshape(nb * BLK, width)
    root_part = jnp.where(
        is_root, jnp.pad(head_sum.astype(jnp.float32), ((0, (nb - 2) * BLK), (0, 0))), 0.0
    )
    kv_grad = (loc + added + root_part).astype(jnp.bfloat16)

    query_out = lax.all_to_all(dq, "uly", split_axis=0, concat_axis=1, tiled=True)
    kv_seq = lax.all_to_all(kv_grad, "uly", split_axis=0, concat_axis=1, tiled=True)
    rows_here = kv_seq.shape[0]
    lane_count = kv_seq.shape[1] // width
    spread = kv_seq.reshape(rows_here, lane_count, 2, kv_here * HD)

    def gather_heads(part):
        if heads_here >= GROUP:
            return part.reshape(rows_here, KVH * HD)
        lanes_per = GROUP // heads_here
        merged = part.astype(jnp.float32).reshape(rows_here, KVH, lanes_per, HD).sum(axis=2)
        return merged.reshape(rows_here, KVH * HD).astype(jnp.bfloat16)

    return (query_out, gather_heads(spread[:, :, 0]), gather_heads(spread[:, :, 1]))


def solution(mesh):
    return jax.shard_map(
        shards,
        mesh=mesh,
        in_specs=(P("ctx", "uly"), P("ctx", None), P("ctx", None), P("ctx", "uly"), P()),
        out_specs=(P(("ctx", "uly"), None), P(("ctx", "uly"), None), P(("ctx", "uly"), None)),
        check_vma=False,
    )
```

```python
import functools
import math

import jax
import jax.numpy as jnp
from jax import lax
from jax.experimental import pallas as pl
from jax.experimental.pallas import tpu as pltpu
from jax.sharding import PartitionSpec as P

HD = 128
KVH = 8
BLK = 128
GROUP = 6
SLOTS = 8


def remote_plan(block_list, shard_count, block_count):
    listed = block_list.reshape(shard_count, block_count, SLOTS)
    wanted = jnp.concatenate(
        [
            listed[:, 0, 0:1],
            listed[:, block_count - 1, 2:3],
            listed[:, :, 5:8].reshape(shard_count, 3 * block_count),
        ],
        axis=1,
    )
    owners = wanted // block_count
    inside = wanted - owners * block_count
    slot_count = wanted.shape[1]
    same_owner = owners[:, :, None] == owners[:, None, :]
    earlier = jnp.arange(slot_count)[None, :] < jnp.arange(slot_count)[:, None]
    places = jnp.sum((same_owner & earlier[None]).astype(jnp.int32), axis=2)
    return (owners, inside, places)


def attention_kernel(
    kind_ref, idx_ref,
    q_ref, do_ref, ok_ref, ov_ref, fk_ref, fv_ref, gk_ref, gv_ref,
    dq_ref, loc_ref, back_ref, gsum_ref,
    kc_ref, vc_ref, loc_acc, back_acc, g_acc,
    *, hpk, kv_here, nb,
):
    g = pl.program_id(0)
    b = pl.program_id(1)
    scale = 1.0 / math.sqrt(HD)

    @pl.when((g == 0) & (b == 0))
    def _():
        loc_acc[...] = jnp.zeros_like(loc_acc)
        back_acc[...] = jnp.zeros_like(back_acc)
        g_acc[...] = jnp.zeros_like(g_acc)

    for s in range(SLOTS):
        kind = kind_ref[b * SLOTS + s]
        row = pl.multiple_of(idx_ref[b * SLOTS + s] * BLK, BLK)
        for code, tk, tv in ((2, ok_ref, ov_ref), (0, fk_ref, fv_ref), (1, gk_ref, gv_ref)):
            @pl.when(kind == code)
            def _():
                kc_ref[s * BLK:(s + 1) * BLK, :] = tk[pl.ds(row, BLK), :]
                vc_ref[s * BLK:(s + 1) * BLK, :] = tv[pl.ds(row, BLK), :]

    kc = kc_ref[...]
    vc = vc_ref[...]
    qs = jnp.concatenate([q_ref[:, h * HD:(h + 1) * HD] for h in range(hpk)], axis=0)
    dos = jnp.concatenate([do_ref[:, h * HD:(h + 1) * HD] for h in range(hpk)], axis=0)
    nt = (((1,), (1,)), ((), ()))
    tn = (((0,), (0,)), ((), ()))
    scores = lax.dot_general(qs, kc, nt, preferred_element_type=jnp.float32) * scale
    peak = jnp.max(scores, axis=1, keepdims=True)
    lifted = jnp.exp(scores - peak)
    probs = lifted / jnp.sum(lifted, axis=1, keepdims=True)
    probs_b = probs.astype(jnp.bfloat16)
    attended = jnp.dot(probs_b, vc, preferred_element_type=jnp.float32)
    delta = jnp.sum(dos.astype(jnp.float32) * attended, axis=1, keepdims=True)
    dprobs = lax.dot_general(dos, vc, nt, preferred_element_type=jnp.float32)
    dscores = (probs * (dprobs - delta) * scale).astype(jnp.bfloat16)
    dq = jnp.dot(dscores, kc, preferred_element_type=jnp.float32)
    for h in range(hpk):
        dq_ref[:, h * HD:(h + 1) * HD] = dq[h * BLK:(h + 1) * BLK].astype(jnp.bfloat16)
    kterm = lax.dot_general(dscores, qs, tn, preferred_element_type=jnp.float32)
    vterm = lax.dot_general(probs_b, dos, tn, preferred_element_type=jnp.float32)

    for s in range(SLOTS):
        kind = kind_ref[b * SLOTS + s]
        row = pl.multiple_of(idx_ref[b * SLOTS + s] * BLK, BLK)
        kt = kterm[s * BLK:(s + 1) * BLK]
        vt = vterm[s * BLK:(s + 1) * BLK]

        @pl.when(kind == 2)
        def _():
            loc_acc[g, pl.ds(row, BLK), :] += kt
            loc_acc[kv_here + g, pl.ds(row, BLK), :] += vt

        @pl.when(kind == 1)
        def _():
            g_acc[g, pl.ds(row, BLK), :] += kt
            g_acc[kv_here + g, pl.ds(row, BLK), :] += vt

        @pl.when(kind == 0)
        def _():
            back_acc[g, pl.ds(row, BLK), :] += kt.astype(jnp.bfloat16).astype(jnp.float32)
            back_acc[kv_here + g, pl.ds(row, BLK), :] += vt.astype(jnp.bfloat16).astype(jnp.float32)

    @pl.when((g == kv_here - 1) & (b == nb - 1))
    def _():
        for j in range(2 * kv_here):
            loc_ref[:, j * HD:(j + 1) * HD] = loc_acc[j]
            back_ref[:, j * HD:(j + 1) * HD] = back_acc[j].astype(jnp.bfloat16)
            gsum_ref[:, j * HD:(j + 1) * HD] = g_acc[j]


def tree_broadcast(x, shard_index, shard_count):
    step = 1
    while step < shard_count:
        pairs = [(i, i + step) for i in range(step) if i + step < shard_count]
        got = lax.ppermute(x, "ctx", pairs)
        x = jnp.where((shard_index >= step) & (shard_index < 2 * step), got, x)
        step *= 2
    return x


def tree_reduce(x, shard_count):
    steps = []
    step = 1
    while step < shard_count:
        steps.append(step)
        step *= 2
    for step in reversed(steps):
        pairs = [(i + step, i) for i in range(step) if i + step < shard_count]
        x = x + lax.ppermute(x.astype(jnp.bfloat16), "ctx", pairs).astype(jnp.float32)
    return x


def shards(query_rows, key_rows, value_rows, out_grad, block_list):
    shard_index = lax.axis_index("ctx")
    lane_index = lax.axis_index("uly")
    shard_count = lax.axis_size("ctx")
    nb = key_rows.shape[0] // BLK
    heads_here = query_rows.shape[1] // HD
    kv_here = max(1, heads_here // GROUP)
    hpk = heads_here // kv_here
    width = 2 * kv_here * HD
    capacity = (3 * nb + shard_count - 4) // (shard_count - 3)
    shift_caps = [1] + [capacity] * (shard_count - 3) + [1]
    shift_offsets = [sum(shift_caps[:i]) for i in range(shard_count - 1)]
    far_count = sum(shift_caps)
    first_kv = lane_index * heads_here // GROUP
    key_own = lax.dynamic_slice_in_dim(key_rows, first_kv * HD, kv_here * HD, axis=1)
    value_own = lax.dynamic_slice_in_dim(value_rows, first_kv * HD, kv_here * HD, axis=1)
    kv_own = jnp.concatenate([key_own, value_own], axis=1)

    owners, inside, places = remote_plan(block_list, shard_count, nb)
    from_here = owners == shard_index
    send_pick = (
        from_here[:, :, None] & (places[:, :, None] == jnp.arange(capacity)[None, None, :])
    ).astype(jnp.bfloat16)
    send_block = (inside[:, :, None] == jnp.arange(nb)[None, None, :]).astype(jnp.bfloat16)
    selector = jnp.einsum(
        "ric,rib->rcb", send_pick, send_block, preferred_element_type=jnp.float32
    ).astype(jnp.bfloat16)
    send = jnp.einsum(
        "rcb,btx->rctx", selector, kv_own.reshape(nb, BLK, width),
        preferred_element_type=jnp.float32,
    ).astype(jnp.bfloat16)
    got_parts = []
    sel_parts = []
    for d in range(1, shard_count):
        cap_d = shift_caps[d - 1]
        peer = (shard_index + d) % shard_count
        payload = lax.dynamic_index_in_dim(send, peer, 0, keepdims=False)[:cap_d]
        pairs = [(i, (i + d) % shard_count) for i in range(shard_count)]
        got_parts.append(lax.ppermute(payload, "ctx", pairs))
        sel_parts.append(lax.dynamic_index_in_dim(selector, peer, 0, keepdims=False)[:cap_d])
    got = jnp.concatenate(got_parts, axis=0).reshape(far_count * BLK, width)
    back_sel = jnp.concatenate(sel_parts, axis=0)
    is_root = shard_index == 0
    heads = tree_broadcast(kv_own[0:2 * BLK], shard_index, shard_count)

    my_owner = lax.dynamic_index_in_dim(owners, shard_index, 0, keepdims=False)
    my_place = lax.dynamic_index_in_dim(places, shard_index, 0, keepdims=False)
    shift = (shard_index - my_owner) % shard_count
    offsets = jnp.asarray([0] + shift_offsets, jnp.int32)
    target = jnp.take(offsets, jnp.clip(shift, 0, shard_count - 1)) + my_place
    rows = lax.dynamic_slice_in_dim(block_list, shard_index * nb, nb, axis=0).astype(jnp.int32)
    local = rows // nb == shard_index
    cols = jnp.arange(SLOTS)[None, :]
    blocks = jnp.arange(nb)[:, None]
    is_global = (cols == 3) | (cols == 4)
    wanted_at = jnp.where(cols == 0, 0, jnp.where(cols == 2, 1, 2 + 3 * blocks + cols - 5))
    wanted_at = jnp.clip(wanted_at, 0, target.shape[0] - 1)
    far_index = jnp.take(target, wanted_at)
    kind = jnp.where(local, 2, jnp.where(is_global, 1, 0)).astype(jnp.int32)
    index = jnp.where(local, rows - shard_index * nb, jnp.where(is_global, rows, far_index))
    index = jnp.clip(index, 0, jnp.where(local, nb - 1, jnp.where(is_global, 1, far_count - 1)))
    kind = kind.reshape(-1)
    index = index.astype(jnp.int32).reshape(-1)

    kernel = functools.partial(attention_kernel, hpk=hpk, kv_here=kv_here, nb=nb)

    def columns(count):
        return [
            pl.BlockSpec((count, HD), lambda g, b, *_: (0, g)),
            pl.BlockSpec((count, HD), lambda g, b, *_: (0, kv_here + g)),
        ]

    grid_spec = pltpu.PrefetchScalarGridSpec(
        num_scalar_prefetch=2,
        grid=(kv_here, nb),
        in_specs=[
            pl.BlockSpec((BLK, hpk * HD), lambda g, b, *_: (b, g)),
            pl.BlockSpec((BLK, hpk * HD), lambda g, b, *_: (b, g)),
        ] + columns(nb * BLK) + columns(far_count * BLK) + columns(2 * BLK),
        out_specs=[
            pl.BlockSpec((BLK, hpk * HD), lambda g, b, *_: (b, g)),
            pl.BlockSpec((nb * BLK, width), lambda g, b, *_: (0, 0)),
            pl.BlockSpec((far_count * BLK, width), lambda g, b, *_: (0, 0)),
            pl.BlockSpec((2 * BLK, width), lambda g, b, *_: (0, 0)),
        ],
        scratch_shapes=[
            pltpu.VMEM((SLOTS * BLK, HD), jnp.bfloat16),
            pltpu.VMEM((SLOTS * BLK, HD), jnp.bfloat16),
            pltpu.VMEM((2 * kv_here, nb * BLK, HD), jnp.float32),
            pltpu.VMEM((2 * kv_here, far_count * BLK, HD), jnp.float32),
            pltpu.VMEM((2 * kv_here, 2 * BLK, HD), jnp.float32),
        ],
    )
    dq, loc, back, gsum = pl.pallas_call(
        kernel,
        grid_spec=grid_spec,
        out_shape=[
            jax.ShapeDtypeStruct((nb * BLK, heads_here * HD), jnp.bfloat16),
            jax.ShapeDtypeStruct((nb * BLK, width), jnp.float32),
            jax.ShapeDtypeStruct((far_count * BLK, width), jnp.bfloat16),
            jax.ShapeDtypeStruct((2 * BLK, width), jnp.float32),
        ],
        compiler_params=pltpu.CompilerParams(dimension_semantics=("arbitrary", "arbitrary")),
    )(kind, index, query_rows, out_grad, kv_own, kv_own, got, got, heads, heads)

    back = back.reshape(far_count, BLK, width)
    ret_parts = []
    for d in range(1, shard_count):
        lo = shift_offsets[d - 1]
        pairs = [(i, (i - d) % shard_count) for i in range(shard_count)]
        ret_parts.append(lax.ppermute(back[lo:lo + shift_caps[d - 1]], "ctx", pairs))
    ret = jnp.concatenate(ret_parts, axis=0)
    head_sum = tree_reduce(gsum, shard_count)
    added = jnp.einsum(
        "kb,ktx->btx", back_sel, ret, preferred_element_type=jnp.float32,
    ).reshape(nb * BLK, width)
    root_part = jnp.where(is_root, jnp.pad(head_sum, ((0, (nb - 2) * BLK), (0, 0))), 0.0)
    kv_grad = (loc + added + root_part).astype(jnp.bfloat16)

    query_out = lax.all_to_all(dq, "uly", split_axis=0, concat_axis=1, tiled=True)
    kv_seq = lax.all_to_all(kv_grad, "uly", split_axis=0, concat_axis=1, tiled=True)
    rows_here = kv_seq.shape[0]
    lane_count = kv_seq.shape[1] // width
    spread = kv_seq.reshape(rows_here, lane_count, 2, kv_here * HD)

    def gather_heads(part):
        if heads_here >= GROUP:
            return part.reshape(rows_here, KVH * HD)
        lanes_per = GROUP // heads_here
        merged = part.astype(jnp.float32).reshape(rows_here, KVH, lanes_per, HD).sum(axis=2)
        return merged.reshape(rows_here, KVH * HD).astype(jnp.bfloat16)

    return (query_out, gather_heads(spread[:, :, 0]), gather_heads(spread[:, :, 1]))


def solution(mesh):
    return jax.shard_map(
        shards,
        mesh=mesh,
        in_specs=(P("ctx", "uly"), P("ctx", None), P("ctx", None), P("ctx", "uly"), P()),
        out_specs=(P(("ctx", "uly"), None), P(("ctx", "uly"), None), P(("ctx", "uly"), None)),
        check_vma=False,
    )
```

```python
import functools
import math

import jax
import jax.numpy as jnp
from jax import lax
from jax.experimental import pallas as pl
from jax.experimental.pallas import tpu as pltpu
from jax.sharding import PartitionSpec as P

HD = 128
KVH = 8
BLK = 128
GROUP = 6
SLOTS = 8


def remote_plan(block_list, shard_count, block_count):
    listed = block_list.reshape(shard_count, block_count, SLOTS)
    wanted = jnp.concatenate(
        [
            listed[:, 0, 0:1],
            listed[:, block_count - 1, 2:3],
            listed[:, :, 5:8].reshape(shard_count, 3 * block_count),
        ],
        axis=1,
    )
    owners = wanted // block_count
    inside = wanted - owners * block_count
    slot_count = wanted.shape[1]
    same_owner = owners[:, :, None] == owners[:, None, :]
    earlier = jnp.arange(slot_count)[None, :] < jnp.arange(slot_count)[:, None]
    places = jnp.sum((same_owner & earlier[None]).astype(jnp.int32), axis=2)
    return (owners, inside, places)


def attention_kernel(
    kind_ref, idx_ref,
    q_ref, do_ref, ok_ref, ov_ref, fk_ref, fv_ref, gk_ref, gv_ref,
    dq_ref, loc_ref, back_ref, gsum_ref,
    kc_ref, vc_ref, loc_acc, back_acc, g_acc,
    *, hpk, kv_here, nb,
):
    g = pl.program_id(0)
    b = pl.program_id(1)
    scale = 1.0 / math.sqrt(HD)

    @pl.when((g == 0) & (b == 0))
    def _():
        loc_acc[...] = jnp.zeros_like(loc_acc)
        back_acc[...] = jnp.zeros_like(back_acc)
        g_acc[...] = jnp.zeros_like(g_acc)

    for s in range(SLOTS):
        kind = kind_ref[b * SLOTS + s]
        row = pl.multiple_of(idx_ref[b * SLOTS + s] * BLK, BLK)
        for code, tk, tv in ((2, ok_ref, ov_ref), (0, fk_ref, fv_ref), (1, gk_ref, gv_ref)):
            @pl.when(kind == code)
            def _():
                kc_ref[s * BLK:(s + 1) * BLK, :] = tk[pl.ds(row, BLK), :]
                vc_ref[s * BLK:(s + 1) * BLK, :] = tv[pl.ds(row, BLK), :]

    kc = kc_ref[...]
    vc = vc_ref[...]
    qs = jnp.concatenate([q_ref[:, h * HD:(h + 1) * HD] for h in range(hpk)], axis=0)
    dos = jnp.concatenate([do_ref[:, h * HD:(h + 1) * HD] for h in range(hpk)], axis=0)
    nt = (((1,), (1,)), ((), ()))
    tn = (((0,), (0,)), ((), ()))
    scores = lax.dot_general(qs, kc, nt, preferred_element_type=jnp.float32) * scale
    peak = jnp.max(scores, axis=1, keepdims=True)
    lifted = jnp.exp(scores - peak)
    probs = lifted / jnp.sum(lifted, axis=1, keepdims=True)
    probs_b = probs.astype(jnp.bfloat16)
    attended = jnp.dot(probs_b, vc, preferred_element_type=jnp.float32)
    delta = jnp.sum(dos.astype(jnp.float32) * attended, axis=1, keepdims=True)
    dprobs = lax.dot_general(dos, vc, nt, preferred_element_type=jnp.float32)
    dscores = (probs * (dprobs - delta) * scale).astype(jnp.bfloat16)
    dq = jnp.dot(dscores, kc, preferred_element_type=jnp.float32)
    for h in range(hpk):
        dq_ref[:, h * HD:(h + 1) * HD] = dq[h * BLK:(h + 1) * BLK].astype(jnp.bfloat16)
    kterm = lax.dot_general(dscores, qs, tn, preferred_element_type=jnp.float32)
    vterm = lax.dot_general(probs_b, dos, tn, preferred_element_type=jnp.float32)

    for s in range(SLOTS):
        kind = kind_ref[b * SLOTS + s]
        row = pl.multiple_of(idx_ref[b * SLOTS + s] * BLK, BLK)
        kt = kterm[s * BLK:(s + 1) * BLK]
        vt = vterm[s * BLK:(s + 1) * BLK]

        @pl.when(kind == 2)
        def _():
            loc_acc[g, pl.ds(row, BLK), :] += kt
            loc_acc[kv_here + g, pl.ds(row, BLK), :] += vt

        @pl.when(kind == 1)
        def _():
            g_acc[g, pl.ds(row, BLK), :] += kt
            g_acc[kv_here + g, pl.ds(row, BLK), :] += vt

        @pl.when(kind == 0)
        def _():
            back_acc[g, pl.ds(row, BLK), :] += kt.astype(jnp.bfloat16).astype(jnp.float32)
            back_acc[kv_here + g, pl.ds(row, BLK), :] += vt.astype(jnp.bfloat16).astype(jnp.float32)

    @pl.when((g == kv_here - 1) & (b == nb - 1))
    def _():
        for j in range(2 * kv_here):
            loc_ref[:, j * HD:(j + 1) * HD] = loc_acc[j]
            back_ref[:, j * HD:(j + 1) * HD] = back_acc[j].astype(jnp.bfloat16)
            gsum_ref[:, j * HD:(j + 1) * HD] = g_acc[j]


def tree_broadcast(x, shard_index, shard_count):
    step = 1
    while step < shard_count:
        pairs = [(i, i + step) for i in range(step) if i + step < shard_count]
        got = lax.ppermute(x, "ctx", pairs)
        x = jnp.where((shard_index >= step) & (shard_index < 2 * step), got, x)
        step *= 2
    return x


def tree_reduce(x, shard_count):
    steps = []
    step = 1
    while step < shard_count:
        steps.append(step)
        step *= 2
    for step in reversed(steps):
        pairs = [(i + step, i) for i in range(step) if i + step < shard_count]
        x = x + lax.ppermute(x.astype(jnp.bfloat16), "ctx", pairs).astype(jnp.float32)
    return x


def combine_kernel(tb_ref, *refs, caps, far_count):
    parts = refs[:len(caps)]
    loc_ref, hs_ref, out_ref, acc = refs[len(caps):]
    acc[...] = loc_ref[...]

    @pl.when(tb_ref[far_count] == 1)
    def _():
        acc[0:hs_ref.shape[0], :] += hs_ref[...]

    k = 0
    for part, cap in zip(parts, caps):
        for p in range(cap):
            t = tb_ref[k]

            @pl.when(t >= 0)
            def _():
                row = pl.multiple_of(t * BLK, BLK)
                acc[pl.ds(row, BLK), :] += part[p * BLK:(p + 1) * BLK, :].astype(jnp.float32)

            k += 1
    out_ref[...] = acc[...].astype(out_ref.dtype)


def lane_transpose(x, lane, lanes):
    rows = x.shape[0] // lanes
    cols = x.shape[1]
    chunks = x.reshape(lanes, rows, cols)
    out = jnp.zeros((rows, lanes * cols), x.dtype)
    own = lax.dynamic_index_in_dim(chunks, lane, 0, keepdims=False)
    out = lax.dynamic_update_slice(out, own, (0, lane * cols))
    for e in range(1, lanes):
        send = lax.dynamic_index_in_dim(chunks, (lane + e) % lanes, 0, keepdims=False)
        pairs = [(i, (i + e) % lanes) for i in range(lanes)]
        got = lax.ppermute(send, "uly", pairs)
        out = lax.dynamic_update_slice(out, got, (0, ((lane - e) % lanes) * cols))
    return out


def shards(query_rows, key_rows, value_rows, out_grad, block_list):
    shard_index = lax.axis_index("ctx")
    lane_index = lax.axis_index("uly")
    shard_count = lax.axis_size("ctx")
    lane_count_all = lax.axis_size("uly")
    nb = key_rows.shape[0] // BLK
    heads_here = query_rows.shape[1] // HD
    kv_here = max(1, heads_here // GROUP)
    hpk = heads_here // kv_here
    width = 2 * kv_here * HD
    capacity = (3 * nb + shard_count - 4) // (shard_count - 3)
    shift_caps = [1] + [capacity] * (shard_count - 3) + [1]
    shift_offsets = [sum(shift_caps[:i]) for i in range(shard_count - 1)]
    far_count = sum(shift_caps)
    first_kv = lane_index * heads_here // GROUP
    key_own = lax.dynamic_slice_in_dim(key_rows, first_kv * HD, kv_here * HD, axis=1)
    value_own = lax.dynamic_slice_in_dim(value_rows, first_kv * HD, kv_here * HD, axis=1)
    kv_own = jnp.concatenate([key_own, value_own], axis=1)

    owners, inside, places = remote_plan(block_list, shard_count, nb)
    match = (owners == shard_index)[:, :, None] & (
        places[:, :, None] == jnp.arange(capacity)[None, None, :]
    )
    pick = jnp.sum(jnp.where(match, inside[:, :, None], 0), axis=1)
    valid = jnp.any(match, axis=1)
    kv_blocks = kv_own.reshape(nb, BLK, width)
    got_parts = []
    back_targets = []
    for d in range(1, shard_count):
        cap_d = shift_caps[d - 1]
        peer = (shard_index + d) % shard_count
        pick_d = lax.dynamic_index_in_dim(pick, peer, 0, keepdims=False)[:cap_d]
        valid_d = lax.dynamic_index_in_dim(valid, peer, 0, keepdims=False)[:cap_d]
        payload = jnp.take(kv_blocks, pick_d, axis=0, mode="clip")
        pairs = [(i, (i + d) % shard_count) for i in range(shard_count)]
        got_parts.append(lax.ppermute(payload, "ctx", pairs))
        back_targets.append(jnp.where(valid_d, pick_d, -1))
    got = jnp.concatenate(got_parts, axis=0).reshape(far_count * BLK, width)
    is_root = shard_index == 0
    heads = tree_broadcast(kv_own[0:2 * BLK], shard_index, shard_count)

    my_owner = lax.dynamic_index_in_dim(owners, shard_index, 0, keepdims=False)
    my_place = lax.dynamic_index_in_dim(places, shard_index, 0, keepdims=False)
    shift = (shard_index - my_owner) % shard_count
    offsets = jnp.asarray([0] + shift_offsets, jnp.int32)
    target = jnp.take(offsets, jnp.clip(shift, 0, shard_count - 1)) + my_place
    rows = lax.dynamic_slice_in_dim(block_list, shard_index * nb, nb, axis=0).astype(jnp.int32)
    local = rows // nb == shard_index
    cols = jnp.arange(SLOTS)[None, :]
    blocks = jnp.arange(nb)[:, None]
    is_global = (cols == 3) | (cols == 4)
    wanted_at = jnp.where(cols == 0, 0, jnp.where(cols == 2, 1, 2 + 3 * blocks + cols - 5))
    wanted_at = jnp.clip(wanted_at, 0, target.shape[0] - 1)
    far_index = jnp.take(target, wanted_at)
    kind = jnp.where(local, 2, jnp.where(is_global, 1, 0)).astype(jnp.int32)
    index = jnp.where(local, rows - shard_index * nb, jnp.where(is_global, rows, far_index))
    index = jnp.clip(index, 0, jnp.where(local, nb - 1, jnp.where(is_global, 1, far_count - 1)))
    kind = kind.reshape(-1)
    index = index.astype(jnp.int32).reshape(-1)

    kernel = functools.partial(attention_kernel, hpk=hpk, kv_here=kv_here, nb=nb)

    def columns(count):
        return [
            pl.BlockSpec((count, HD), lambda g, b, *_: (0, g)),
            pl.BlockSpec((count, HD), lambda g, b, *_: (0, kv_here + g)),
        ]

    grid_spec = pltpu.PrefetchScalarGridSpec(
        num_scalar_prefetch=2,
        grid=(kv_here, nb),
        in_specs=[
            pl.BlockSpec((BLK, hpk * HD), lambda g, b, *_: (b, g)),
            pl.BlockSpec((BLK, hpk * HD), lambda g, b, *_: (b, g)),
        ] + columns(nb * BLK) + columns(far_count * BLK) + columns(2 * BLK),
        out_specs=[
            pl.BlockSpec((BLK, hpk * HD), lambda g, b, *_: (b, g)),
            pl.BlockSpec((nb * BLK, width), lambda g, b, *_: (0, 0)),
            pl.BlockSpec((far_count * BLK, width), lambda g, b, *_: (0, 0)),
            pl.BlockSpec((2 * BLK, width), lambda g, b, *_: (0, 0)),
        ],
        scratch_shapes=[
            pltpu.VMEM((SLOTS * BLK, HD), jnp.bfloat16),
            pltpu.VMEM((SLOTS * BLK, HD), jnp.bfloat16),
            pltpu.VMEM((2 * kv_here, nb * BLK, HD), jnp.float32),
            pltpu.VMEM((2 * kv_here, far_count * BLK, HD), jnp.float32),
            pltpu.VMEM((2 * kv_here, 2 * BLK, HD), jnp.float32),
        ],
    )
    dq, loc, back, gsum = pl.pallas_call(
        kernel,
        grid_spec=grid_spec,
        out_shape=[
            jax.ShapeDtypeStruct((nb * BLK, heads_here * HD), jnp.bfloat16),
            jax.ShapeDtypeStruct((nb * BLK, width), jnp.float32),
            jax.ShapeDtypeStruct((far_count * BLK, width), jnp.bfloat16),
            jax.ShapeDtypeStruct((2 * BLK, width), jnp.float32),
        ],
        compiler_params=pltpu.CompilerParams(dimension_semantics=("arbitrary", "arbitrary")),
    )(kind, index, query_rows, out_grad, kv_own, kv_own, got, got, heads, heads)

    ret_parts = []
    for d in range(1, shard_count):
        lo = shift_offsets[d - 1] * BLK
        pairs = [(i, (i - d) % shard_count) for i in range(shard_count)]
        ret_parts.append(lax.ppermute(back[lo:lo + shift_caps[d - 1] * BLK], "ctx", pairs))
    head_sum = tree_reduce(gsum, shard_count)
    targets = jnp.concatenate(back_targets + [is_root.astype(jnp.int32)[None]]).astype(jnp.int32)
    part_count = len(ret_parts)
    kv_grad = pl.pallas_call(
        functools.partial(combine_kernel, caps=tuple(shift_caps), far_count=far_count),
        out_shape=jax.ShapeDtypeStruct((nb * BLK, width), jnp.bfloat16),
        in_specs=[pl.BlockSpec(memory_space=pltpu.SMEM)]
        + [pl.BlockSpec(memory_space=pltpu.VMEM)] * (part_count + 2),
        out_specs=pl.BlockSpec(memory_space=pltpu.VMEM),
        scratch_shapes=[pltpu.VMEM((nb * BLK, width), jnp.float32)],
    )(targets, *ret_parts, loc, head_sum)

    query_out = lane_transpose(dq, lane_index, lane_count_all)
    kv_seq = lane_transpose(kv_grad, lane_index, lane_count_all)
    rows_here = kv_seq.shape[0]
    lane_count = kv_seq.shape[1] // width
    spread = kv_seq.reshape(rows_here, lane_count, 2, kv_here * HD)

    def gather_heads(part):
        if heads_here >= GROUP:
            return part.reshape(rows_here, KVH * HD)
        lanes_per = GROUP // heads_here
        merged = part.astype(jnp.float32).reshape(rows_here, KVH, lanes_per, HD).sum(axis=2)
        return merged.reshape(rows_here, KVH * HD).astype(jnp.bfloat16)

    return (query_out, gather_heads(spread[:, :, 0]), gather_heads(spread[:, :, 1]))


def solution(mesh):
    return jax.shard_map(
        shards,
        mesh=mesh,
        in_specs=(P("ctx", "uly"), P("ctx", None), P("ctx", None), P("ctx", "uly"), P()),
        out_specs=(P(("ctx", "uly"), None), P(("ctx", "uly"), None), P(("ctx", "uly"), None)),
        check_vma=False,
    )
```

```python
import functools
import math

import jax
import jax.numpy as jnp
from jax import lax
from jax.experimental import pallas as pl
from jax.experimental.pallas import tpu as pltpu
from jax.sharding import PartitionSpec as P

HD = 128
KVH = 8
BLK = 128
GROUP = 6
SLOTS = 8


def attention_kernel(
    blk_ref, dst_ref, kind_ref,
    q_ref, do_ref, k_ref, v_ref, dq_in,
    dq_ref, loc_ref, far_ref,
    kc_ref, vc_ref, loc_acc, far_acc,
    *, hpk, nb,
):
    b = pl.program_id(0)
    scale = 1.0 / math.sqrt(HD)

    @pl.when(b == 0)
    def _():
        loc_acc[...] = jnp.zeros_like(loc_acc)
        far_acc[...] = jnp.zeros_like(far_acc)

    for s in range(SLOTS):
        row = pl.multiple_of(blk_ref[b * SLOTS + s] * BLK, BLK)
        kc_ref[s * BLK:(s + 1) * BLK, :] = k_ref[pl.ds(row, BLK), :]
        vc_ref[s * BLK:(s + 1) * BLK, :] = v_ref[pl.ds(row, BLK), :]

    kc = kc_ref[...]
    vc = vc_ref[...]
    qs = jnp.concatenate([q_ref[:, h * HD:(h + 1) * HD] for h in range(hpk)], axis=0)
    dos = jnp.concatenate([do_ref[:, h * HD:(h + 1) * HD] for h in range(hpk)], axis=0)
    nt = (((1,), (1,)), ((), ()))
    tn = (((0,), (0,)), ((), ()))
    scores = lax.dot_general(qs, kc, nt, preferred_element_type=jnp.float32) * scale
    peak = jnp.max(scores, axis=1, keepdims=True)
    lifted = jnp.exp(scores - peak)
    probs = lifted * (1.0 / jnp.sum(lifted, axis=1, keepdims=True))
    probs_b = probs.astype(jnp.bfloat16)
    attended = jnp.dot(probs_b, vc, preferred_element_type=jnp.float32)
    delta = jnp.sum(dos.astype(jnp.float32) * attended, axis=1, keepdims=True)
    dprobs = lax.dot_general(dos, vc, nt, preferred_element_type=jnp.float32)
    dscores = (probs * (dprobs - delta) * scale).astype(jnp.bfloat16)
    dq = jnp.dot(dscores, kc, preferred_element_type=jnp.float32)
    for h in range(hpk):
        dq_ref[:, h * HD:(h + 1) * HD] = dq[h * BLK:(h + 1) * BLK].astype(jnp.bfloat16)
    kterm = lax.dot_general(dscores, qs, tn, preferred_element_type=jnp.float32)
    vterm = lax.dot_general(probs_b, dos, tn, preferred_element_type=jnp.float32)

    for s in range(SLOTS):
        kind = kind_ref[b * SLOTS + s]
        row = pl.multiple_of(dst_ref[b * SLOTS + s] * BLK, BLK)
        kt = kterm[s * BLK:(s + 1) * BLK]
        vt = vterm[s * BLK:(s + 1) * BLK]
        rounded = kind == 0
        kt = jnp.where(rounded, kt.astype(jnp.bfloat16).astype(jnp.float32), kt)
        vt = jnp.where(rounded, vt.astype(jnp.bfloat16).astype(jnp.float32), vt)

        @pl.when(kind == 2)
        def _():
            loc_acc[0, pl.ds(row, BLK), :] += kt
            loc_acc[1, pl.ds(row, BLK), :] += vt

        @pl.when(kind != 2)
        def _():
            far_acc[0, pl.ds(row, BLK), :] += kt
            far_acc[1, pl.ds(row, BLK), :] += vt

    @pl.when(b == nb - 1)
    def _():
        for j in range(2):
            loc_ref[:, j * HD:(j + 1) * HD] = loc_acc[j]
            far_ref[:, j * HD:(j + 1) * HD] = far_acc[j].astype(jnp.bfloat16)


def shards(query_rows, key_rows, value_rows, out_grad, block_list):
    shard_index = lax.axis_index("ctx")
    lane_index = lax.axis_index("uly")
    nb = key_rows.shape[0] // BLK
    seq = block_list.shape[0] * BLK
    heads_here = query_rows.shape[1] // HD
    kv_here = max(1, heads_here // GROUP)
    hpk = heads_here // kv_here
    first_kv = lane_index * heads_here // GROUP

    rows = lax.dynamic_slice_in_dim(block_list, shard_index * nb, nb, axis=0).astype(jnp.int32)
    owner = rows // nb
    cols = jnp.arange(SLOTS)[None, :]
    is_global = (cols == 3) | (cols == 4)
    local = owner == shard_index
    remote = jnp.logical_not(local) & jnp.logical_not(is_global)
    kind = jnp.where(local, 2, jnp.where(remote, 0, 1)).astype(jnp.int32).reshape(-1)
    dst = jnp.where(local, rows - shard_index * nb, rows).astype(jnp.int32).reshape(-1)
    blk = rows.reshape(-1)

    kernel = functools.partial(attention_kernel, hpk=hpk, nb=nb)
    dq = jnp.zeros((nb * BLK, heads_here * HD), jnp.bfloat16)
    key_parts = []
    value_parts = []
    for g in range(kv_here):
        col = (first_kv + g) * HD
        kv_own = jnp.concatenate(
            [
                lax.dynamic_slice_in_dim(key_rows, col, HD, axis=1),
                lax.dynamic_slice_in_dim(value_rows, col, HD, axis=1),
            ],
            axis=1,
        )
        kv_all = lax.all_gather(kv_own, "ctx", axis=0, tiled=True)
        grid_spec = pltpu.PrefetchScalarGridSpec(
            num_scalar_prefetch=3,
            grid=(nb,),
            in_specs=[
                pl.BlockSpec((BLK, hpk * HD), lambda b, *_, g=g: (b, g)),
                pl.BlockSpec((BLK, hpk * HD), lambda b, *_, g=g: (b, g)),
                pl.BlockSpec((seq, HD), lambda b, *_: (0, 0)),
                pl.BlockSpec((seq, HD), lambda b, *_: (0, 1)),
                pl.BlockSpec(memory_space=pl.ANY),
            ],
            out_specs=[
                pl.BlockSpec((BLK, hpk * HD), lambda b, *_, g=g: (b, g)),
                pl.BlockSpec((nb * BLK, 2 * HD), lambda b, *_: (0, 0)),
                pl.BlockSpec((seq, 2 * HD), lambda b, *_: (0, 0)),
            ],
            scratch_shapes=[
                pltpu.VMEM((SLOTS * BLK, HD), jnp.bfloat16),
                pltpu.VMEM((SLOTS * BLK, HD), jnp.bfloat16),
                pltpu.VMEM((2, nb * BLK, HD), jnp.float32),
                pltpu.VMEM((2, seq, HD), jnp.float32),
            ],
        )
        dq, loc, far = pl.pallas_call(
            kernel,
            grid_spec=grid_spec,
            out_shape=[
                jax.ShapeDtypeStruct((nb * BLK, heads_here * HD), jnp.bfloat16),
                jax.ShapeDtypeStruct((nb * BLK, 2 * HD), jnp.float32),
                jax.ShapeDtypeStruct((seq, 2 * HD), jnp.bfloat16),
            ],
            input_output_aliases={7: 0},
            compiler_params=pltpu.CompilerParams(dimension_semantics=("arbitrary",)),
        )(blk, dst, kind, query_rows, out_grad, kv_all, kv_all, dq)
        got = lax.psum_scatter(far, "ctx", scatter_dimension=0, tiled=True)
        part = (got.astype(jnp.float32) + loc).astype(jnp.bfloat16)
        key_parts.append(part[:, :HD])
        value_parts.append(part[:, HD:])
    kv_grad = jnp.concatenate(key_parts + value_parts, axis=1)
    width = 2 * kv_here * HD

    query_out = lax.all_to_all(dq, "uly", split_axis=0, concat_axis=1, tiled=True)
    kv_seq = lax.all_to_all(kv_grad, "uly", split_axis=0, concat_axis=1, tiled=True)
    rows_here = kv_seq.shape[0]
    lane_count = kv_seq.shape[1] // width
    spread = kv_seq.reshape(rows_here, lane_count, 2, kv_here * HD)

    def gather_heads(part):
        if heads_here >= GROUP:
            return part.reshape(rows_here, KVH * HD)
        lanes_per = GROUP // heads_here
        merged = part.astype(jnp.float32).reshape(rows_here, KVH, lanes_per, HD).sum(axis=2)
        return merged.reshape(rows_here, KVH * HD).astype(jnp.bfloat16)

    return (query_out, gather_heads(spread[:, :, 0]), gather_heads(spread[:, :, 1]))


def solution(mesh):
    return jax.shard_map(
        shards,
        mesh=mesh,
        in_specs=(P("ctx", "uly"), P("ctx", None), P("ctx", None), P("ctx", "uly"), P()),
        out_specs=(P(("ctx", "uly"), None), P(("ctx", "uly"), None), P(("ctx", "uly"), None)),
        check_vma=False,
    )
```

```python
import functools
import math

import jax
import jax.numpy as jnp
from jax import lax
from jax.experimental import pallas as pl
from jax.experimental.pallas import tpu as pltpu
from jax.sharding import PartitionSpec as P

HD = 128
KVH = 8
BLK = 128
GROUP = 6
SLOTS = 8


def attention_kernel(
    blk_ref, dst_ref, kind_ref,
    q_ref, do_ref, k_ref, v_ref,
    dq_ref, loc_ref, far_ref,
    kc_ref, vc_ref, loc_acc, far_acc,
    *, hpk, kv_here, nb,
):
    g = pl.program_id(0)
    b = pl.program_id(1)
    scale = 1.0 / math.sqrt(HD)

    @pl.when((g == 0) & (b == 0))
    def _():
        loc_acc[...] = jnp.zeros_like(loc_acc)
        far_acc[...] = jnp.zeros_like(far_acc)

    for s in range(SLOTS):
        row = pl.multiple_of(blk_ref[b * SLOTS + s] * BLK, BLK)
        kc_ref[s * BLK:(s + 1) * BLK, :] = k_ref[pl.ds(row, BLK), :]
        vc_ref[s * BLK:(s + 1) * BLK, :] = v_ref[pl.ds(row, BLK), :]

    kc = kc_ref[...]
    vc = vc_ref[...]
    qs = jnp.concatenate([q_ref[:, h * HD:(h + 1) * HD] for h in range(hpk)], axis=0)
    dos = jnp.concatenate([do_ref[:, h * HD:(h + 1) * HD] for h in range(hpk)], axis=0)
    nt = (((1,), (1,)), ((), ()))
    tn = (((0,), (0,)), ((), ()))
    scores = lax.dot_general(qs, kc, nt, preferred_element_type=jnp.float32) * scale
    peak = jnp.max(scores, axis=1, keepdims=True)
    lifted = jnp.exp(scores - peak)
    probs = lifted * (1.0 / jnp.sum(lifted, axis=1, keepdims=True))
    probs_b = probs.astype(jnp.bfloat16)
    attended = jnp.dot(probs_b, vc, preferred_element_type=jnp.float32)
    delta = jnp.sum(dos.astype(jnp.float32) * attended, axis=1, keepdims=True)
    dprobs = lax.dot_general(dos, vc, nt, preferred_element_type=jnp.float32)
    dscores = (probs * (dprobs - delta) * scale).astype(jnp.bfloat16)
    dq = jnp.dot(dscores, kc, preferred_element_type=jnp.float32)
    for h in range(hpk):
        dq_ref[:, h * HD:(h + 1) * HD] = dq[h * BLK:(h + 1) * BLK].astype(jnp.bfloat16)
    kterm = lax.dot_general(qs, dscores, tn, preferred_element_type=jnp.float32)
    vterm = lax.dot_general(dos, probs_b, tn, preferred_element_type=jnp.float32)

    for s in range(SLOTS):
        kind = kind_ref[b * SLOTS + s]
        row = pl.multiple_of(dst_ref[b * SLOTS + s] * BLK, BLK)
        kt = kterm[:, s * BLK:(s + 1) * BLK]
        vt = vterm[:, s * BLK:(s + 1) * BLK]
        rounded = kind == 0
        kt = jnp.where(rounded, kt.astype(jnp.bfloat16).astype(jnp.float32), kt)
        vt = jnp.where(rounded, vt.astype(jnp.bfloat16).astype(jnp.float32), vt)

        @pl.when(kind == 2)
        def _():
            loc_acc[g, pl.ds(row, BLK), :] += kt
            loc_acc[kv_here + g, pl.ds(row, BLK), :] += vt

        @pl.when(kind != 2)
        def _():
            far_acc[g, pl.ds(row, BLK), :] += kt
            far_acc[kv_here + g, pl.ds(row, BLK), :] += vt

    @pl.when((g == kv_here - 1) & (b == nb - 1))
    def _():
        for j in range(2 * kv_here):
            loc_ref[:, j * HD:(j + 1) * HD] = loc_acc[j]
            far_ref[:, j * HD:(j + 1) * HD] = far_acc[j].astype(jnp.bfloat16)


def shards(query_rows, key_rows, value_rows, out_grad, block_list):
    shard_index = lax.axis_index("ctx")
    lane_index = lax.axis_index("uly")
    nb = key_rows.shape[0] // BLK
    seq = block_list.shape[0] * BLK
    heads_here = query_rows.shape[1] // HD
    kv_here = max(1, heads_here // GROUP)
    hpk = heads_here // kv_here
    width = 2 * kv_here * HD
    first_kv = lane_index * heads_here // GROUP
    key_own = lax.dynamic_slice_in_dim(key_rows, first_kv * HD, kv_here * HD, axis=1)
    value_own = lax.dynamic_slice_in_dim(value_rows, first_kv * HD, kv_here * HD, axis=1)
    kv_own = jnp.concatenate([key_own, value_own], axis=1)
    kv_all = lax.all_gather(kv_own, "ctx", axis=0, tiled=True)

    rows = lax.dynamic_slice_in_dim(block_list, shard_index * nb, nb, axis=0).astype(jnp.int32)
    owner = rows // nb
    cols = jnp.arange(SLOTS)[None, :]
    is_global = (cols == 3) | (cols == 4)
    local = owner == shard_index
    remote = jnp.logical_not(local) & jnp.logical_not(is_global)
    kind = jnp.where(local, 2, jnp.where(remote, 0, 1)).astype(jnp.int32).reshape(-1)
    dst = jnp.where(local, rows - shard_index * nb, rows).astype(jnp.int32).reshape(-1)
    blk = rows.reshape(-1)

    kernel = functools.partial(attention_kernel, hpk=hpk, kv_here=kv_here, nb=nb)
    grid_spec = pltpu.PrefetchScalarGridSpec(
        num_scalar_prefetch=3,
        grid=(kv_here, nb),
        in_specs=[
            pl.BlockSpec((BLK, hpk * HD), lambda g, b, *_: (b, g)),
            pl.BlockSpec((BLK, hpk * HD), lambda g, b, *_: (b, g)),
            pl.BlockSpec((seq, HD), lambda g, b, *_: (0, g)),
            pl.BlockSpec((seq, HD), lambda g, b, *_: (0, kv_here + g)),
        ],
        out_specs=[
            pl.BlockSpec((BLK, hpk * HD), lambda g, b, *_: (b, g)),
            pl.BlockSpec((nb * BLK, width), lambda g, b, *_: (0, 0)),
            pl.BlockSpec((seq, width), lambda g, b, *_: (0, 0)),
        ],
        scratch_shapes=[
            pltpu.VMEM((SLOTS * BLK, HD), jnp.bfloat16),
            pltpu.VMEM((SLOTS * BLK, HD), jnp.bfloat16),
            pltpu.VMEM((2 * kv_here, nb * BLK, HD), jnp.float32),
            pltpu.VMEM((2 * kv_here, seq, HD), jnp.float32),
        ],
    )
    dq, loc, far = pl.pallas_call(
        kernel,
        grid_spec=grid_spec,
        out_shape=[
            jax.ShapeDtypeStruct((nb * BLK, heads_here * HD), jnp.bfloat16),
            jax.ShapeDtypeStruct((nb * BLK, width), jnp.float32),
            jax.ShapeDtypeStruct((seq, width), jnp.bfloat16),
        ],
        compiler_params=pltpu.CompilerParams(dimension_semantics=("arbitrary", "arbitrary")),
    )(blk, dst, kind, query_rows, out_grad, kv_all, kv_all)

    got = lax.psum_scatter(far, "ctx", scatter_dimension=0, tiled=True)
    kv_sum = (got.astype(jnp.float32) + loc).reshape(nb, HD, 2 * kv_here, BLK)
    kv_grad = jnp.transpose(kv_sum, (0, 3, 2, 1)).reshape(nb * BLK, width).astype(jnp.bfloat16)

    query_out = lax.all_to_all(dq, "uly", split_axis=0, concat_axis=1, tiled=True)
    kv_seq = lax.all_to_all(kv_grad, "uly", split_axis=0, concat_axis=1, tiled=True)
    rows_here = kv_seq.shape[0]
    lane_count = kv_seq.shape[1] // width
    spread = kv_seq.reshape(rows_here, lane_count, 2, kv_here * HD)

    def gather_heads(part):
        if heads_here >= GROUP:
            return part.reshape(rows_here, KVH * HD)
        lanes_per = GROUP // heads_here
        merged = part.astype(jnp.float32).reshape(rows_here, KVH, lanes_per, HD).sum(axis=2)
        return merged.reshape(rows_here, KVH * HD).astype(jnp.bfloat16)

    return (query_out, gather_heads(spread[:, :, 0]), gather_heads(spread[:, :, 1]))


def solution(mesh):
    return jax.shard_map(
        shards,
        mesh=mesh,
        in_specs=(P("ctx", "uly"), P("ctx", None), P("ctx", None), P("ctx", "uly"), P()),
        out_specs=(P(("ctx", "uly"), None), P(("ctx", "uly"), None), P(("ctx", "uly"), None)),
        check_vma=False,
    )
```

```python
import functools
import math

import jax
import jax.numpy as jnp
from jax import lax
from jax.experimental import pallas as pl
from jax.experimental.pallas import tpu as pltpu
from jax.sharding import PartitionSpec as P

HD = 128
KVH = 8
BLK = 128
GROUP = 6
SLOTS = 8


def attention_kernel(
    blk_ref, side_ref, dst_ref, kind_ref,
    q_ref, do_ref, k_ref, v_ref, ko_ref, vo_ref,
    dq_ref, loc_ref, far_ref, fo_ref,
    kc_ref, vc_ref, loc_acc, far_acc, fo_acc,
    *, hpk, kv_here, nb,
):
    g = pl.program_id(0)
    b = pl.program_id(1)
    scale = 1.0 / math.sqrt(HD)

    @pl.when((g == 0) & (b == 0))
    def _():
        loc_acc[...] = jnp.zeros_like(loc_acc)
        far_acc[...] = jnp.zeros_like(far_acc)
        fo_acc[...] = jnp.zeros_like(fo_acc)

    for s in range(SLOTS):
        row = pl.multiple_of(blk_ref[b * SLOTS + s] * BLK, BLK)
        side = side_ref[b * SLOTS + s]
        for code, tk, tv in ((0, k_ref, v_ref), (1, ko_ref, vo_ref)):
            @pl.when(side == code)
            def _():
                kc_ref[s * BLK:(s + 1) * BLK, :] = tk[pl.ds(row, BLK), :]
                vc_ref[s * BLK:(s + 1) * BLK, :] = tv[pl.ds(row, BLK), :]

    kc = kc_ref[...]
    vc = vc_ref[...]
    qs = jnp.concatenate([q_ref[:, h * HD:(h + 1) * HD] for h in range(hpk)], axis=0)
    dos = jnp.concatenate([do_ref[:, h * HD:(h + 1) * HD] for h in range(hpk)], axis=0)
    nt = (((1,), (1,)), ((), ()))
    tn = (((0,), (0,)), ((), ()))
    scores = lax.dot_general(qs, kc, nt, preferred_element_type=jnp.float32) * scale
    peak = jnp.max(scores, axis=1, keepdims=True)
    lifted = jnp.exp(scores - peak)
    probs = lifted * (1.0 / jnp.sum(lifted, axis=1, keepdims=True))
    probs_b = probs.astype(jnp.bfloat16)
    attended = jnp.dot(probs_b, vc, preferred_element_type=jnp.float32)
    delta = jnp.sum(dos.astype(jnp.float32) * attended, axis=1, keepdims=True)
    dprobs = lax.dot_general(dos, vc, nt, preferred_element_type=jnp.float32)
    dscores = (probs * (dprobs - delta) * scale).astype(jnp.bfloat16)
    dq = jnp.dot(dscores, kc, preferred_element_type=jnp.float32)
    for h in range(hpk):
        dq_ref[:, h * HD:(h + 1) * HD] = dq[h * BLK:(h + 1) * BLK].astype(jnp.bfloat16)
    kterm = lax.dot_general(qs, dscores, tn, preferred_element_type=jnp.float32)
    vterm = lax.dot_general(dos, probs_b, tn, preferred_element_type=jnp.float32)

    for s in range(SLOTS):
        kind = kind_ref[b * SLOTS + s]
        row = pl.multiple_of(dst_ref[b * SLOTS + s] * BLK, BLK)
        kt = kterm[:, s * BLK:(s + 1) * BLK]
        vt = vterm[:, s * BLK:(s + 1) * BLK]
        rounded = kind == 0
        kt = jnp.where(rounded, kt.astype(jnp.bfloat16).astype(jnp.float32), kt)
        vt = jnp.where(rounded, vt.astype(jnp.bfloat16).astype(jnp.float32), vt)

        @pl.when(kind == 2)
        def _():
            loc_acc[g, pl.ds(row, BLK), :] += kt
            loc_acc[kv_here + g, pl.ds(row, BLK), :] += vt

        side = side_ref[b * SLOTS + s]

        @pl.when((kind != 2) & (side == 0))
        def _():
            far_acc[g, pl.ds(row, BLK), :] += kt
            far_acc[kv_here + g, pl.ds(row, BLK), :] += vt

        @pl.when((kind != 2) & (side == 1))
        def _():
            fo_acc[g, pl.ds(row, BLK), :] += kt
            fo_acc[kv_here + g, pl.ds(row, BLK), :] += vt

    @pl.when((g == kv_here - 1) & (b == nb - 1))
    def _():
        for j in range(2 * kv_here):
            loc_ref[:, j * HD:(j + 1) * HD] = loc_acc[j]
            far_ref[:, j * HD:(j + 1) * HD] = far_acc[j].astype(jnp.bfloat16)
            fo_ref[:, j * HD:(j + 1) * HD] = fo_acc[j].astype(jnp.bfloat16)


def shards(query_rows, key_rows, value_rows, out_grad, block_list):
    shard_index = lax.axis_index("ctx")
    lane_index = lax.axis_index("uly")
    nb = key_rows.shape[0] // BLK
    seq = block_list.shape[0] * BLK
    heads_here = query_rows.shape[1] // HD
    kv_here = max(1, heads_here // GROUP)
    hpk = heads_here // kv_here
    width = 2 * kv_here * HD
    first_kv = lane_index * heads_here // GROUP
    key_own = lax.dynamic_slice_in_dim(key_rows, first_kv * HD, kv_here * HD, axis=1)
    value_own = lax.dynamic_slice_in_dim(value_rows, first_kv * HD, kv_here * HD, axis=1)
    kv_own = jnp.concatenate([key_own, value_own], axis=1)
    shard_count = lax.axis_size("ctx")
    groups = [[i for i in range(shard_count) if i % 2 == p] for p in range(2)]
    partner = [(i, i ^ 1) for i in range(shard_count)]
    core = shard_index % 2
    kv_half = lax.all_gather(kv_own, "ctx", axis=0, tiled=True, axis_index_groups=groups)
    kv_other = lax.ppermute(kv_half, "ctx", partner)
    half = seq // 2

    rows = lax.dynamic_slice_in_dim(block_list, shard_index * nb, nb, axis=0).astype(jnp.int32)
    owner = rows // nb
    cols = jnp.arange(SLOTS)[None, :]
    is_global = (cols == 3) | (cols == 4)
    local = owner == shard_index
    remote = jnp.logical_not(local) & jnp.logical_not(is_global)
    kind = jnp.where(local, 2, jnp.where(remote, 0, 1)).astype(jnp.int32).reshape(-1)
    owner_side = (owner % 2 != core).astype(jnp.int32)
    half_row = (owner // 2) * nb + rows % nb
    dst = jnp.where(local, rows - shard_index * nb, half_row).astype(jnp.int32).reshape(-1)
    blk = half_row.astype(jnp.int32).reshape(-1)
    side = owner_side.reshape(-1)

    kernel = functools.partial(attention_kernel, hpk=hpk, kv_here=kv_here, nb=nb)
    grid_spec = pltpu.PrefetchScalarGridSpec(
        num_scalar_prefetch=4,
        grid=(kv_here, nb),
        in_specs=[
            pl.BlockSpec((BLK, hpk * HD), lambda g, b, *_: (b, g)),
            pl.BlockSpec((BLK, hpk * HD), lambda g, b, *_: (b, g)),
            pl.BlockSpec((half, HD), lambda g, b, *_: (0, g)),
            pl.BlockSpec((half, HD), lambda g, b, *_: (0, kv_here + g)),
            pl.BlockSpec((half, HD), lambda g, b, *_: (0, g)),
            pl.BlockSpec((half, HD), lambda g, b, *_: (0, kv_here + g)),
        ],
        out_specs=[
            pl.BlockSpec((BLK, hpk * HD), lambda g, b, *_: (b, g)),
            pl.BlockSpec((nb * BLK, width), lambda g, b, *_: (0, 0)),
            pl.BlockSpec((half, width), lambda g, b, *_: (0, 0)),
            pl.BlockSpec((half, width), lambda g, b, *_: (0, 0)),
        ],
        scratch_shapes=[
            pltpu.VMEM((SLOTS * BLK, HD), jnp.bfloat16),
            pltpu.VMEM((SLOTS * BLK, HD), jnp.bfloat16),
            pltpu.VMEM((2 * kv_here, nb * BLK, HD), jnp.float32),
            pltpu.VMEM((2 * kv_here, half, HD), jnp.float32),
            pltpu.VMEM((2 * kv_here, half, HD), jnp.float32),
        ],
    )
    dq, loc, far, far_other = pl.pallas_call(
        kernel,
        grid_spec=grid_spec,
        out_shape=[
            jax.ShapeDtypeStruct((nb * BLK, heads_here * HD), jnp.bfloat16),
            jax.ShapeDtypeStruct((nb * BLK, width), jnp.float32),
            jax.ShapeDtypeStruct((half, width), jnp.bfloat16),
            jax.ShapeDtypeStruct((half, width), jnp.bfloat16),
        ],
        compiler_params=pltpu.CompilerParams(dimension_semantics=("arbitrary", "arbitrary")),
    )(blk, side, dst, kind, query_rows, out_grad, kv_half, kv_half, kv_other, kv_other)

    from_partner = lax.ppermute(far_other, "ctx", partner)
    mine = (far.astype(jnp.float32) + from_partner.astype(jnp.float32)).astype(jnp.bfloat16)
    got = lax.psum_scatter(
        mine, "ctx", scatter_dimension=0, tiled=True, axis_index_groups=groups
    )
    kv_sum = (got.astype(jnp.float32) + loc).reshape(nb, HD, 2 * kv_here, BLK)
    kv_grad = jnp.transpose(kv_sum, (0, 3, 2, 1)).reshape(nb * BLK, width).astype(jnp.bfloat16)

    query_out = lax.all_to_all(dq, "uly", split_axis=0, concat_axis=1, tiled=True)
    kv_seq = lax.all_to_all(kv_grad, "uly", split_axis=0, concat_axis=1, tiled=True)
    rows_here = kv_seq.shape[0]
    lane_count = kv_seq.shape[1] // width
    spread = kv_seq.reshape(rows_here, lane_count, 2, kv_here * HD)

    def gather_heads(part):
        if heads_here >= GROUP:
            return part.reshape(rows_here, KVH * HD)
        lanes_per = GROUP // heads_here
        merged = part.astype(jnp.float32).reshape(rows_here, KVH, lanes_per, HD).sum(axis=2)
        return merged.reshape(rows_here, KVH * HD).astype(jnp.bfloat16)

    return (query_out, gather_heads(spread[:, :, 0]), gather_heads(spread[:, :, 1]))


def solution(mesh):
    return jax.shard_map(
        shards,
        mesh=mesh,
        in_specs=(P("ctx", "uly"), P("ctx", None), P("ctx", None), P("ctx", "uly"), P()),
        out_specs=(P(("ctx", "uly"), None), P(("ctx", "uly"), None), P(("ctx", "uly"), None)),
        check_vma=False,
    )
```

```python
import functools
import math

import jax
import jax.numpy as jnp
from jax import lax
from jax.experimental import pallas as pl
from jax.experimental.pallas import tpu as pltpu
from jax.sharding import PartitionSpec as P

HD = 128
KVH = 8
BLK = 128
GROUP = 6
SLOTS = 8


def attention_kernel(
    blk_ref, side_ref, dst_ref, kind_ref,
    q_ref, do_ref, k_ref, v_ref, ko_ref, vo_ref,
    dq_ref, loc_ref, far_ref, fo_ref,
    kc_ref, vc_ref, loc_acc, far_acc, fo_acc,
    *, hpk, kv_here, nb,
):
    g = pl.program_id(0)
    b = pl.program_id(1)
    scale = 1.0 / math.sqrt(HD)

    @pl.when((g == 0) & (b == 0))
    def _():
        loc_acc[...] = jnp.zeros_like(loc_acc)
        far_acc[...] = jnp.zeros_like(far_acc)
        fo_acc[...] = jnp.zeros_like(fo_acc)

    for s in range(SLOTS):
        row = pl.multiple_of(blk_ref[b * SLOTS + s] * BLK, BLK)
        side = side_ref[b * SLOTS + s]
        for code, tk, tv in ((0, k_ref, v_ref), (1, ko_ref, vo_ref)):
            @pl.when(side == code)
            def _():
                kc_ref[s * BLK:(s + 1) * BLK, :] = tk[pl.ds(row, BLK), :]
                vc_ref[s * BLK:(s + 1) * BLK, :] = tv[pl.ds(row, BLK), :]

    kc = kc_ref[...]
    vc = vc_ref[...]
    qs = jnp.concatenate([q_ref[:, h * HD:(h + 1) * HD] for h in range(hpk)], axis=0)
    dos = jnp.concatenate([do_ref[:, h * HD:(h + 1) * HD] for h in range(hpk)], axis=0)
    nt = (((1,), (1,)), ((), ()))
    tn = (((0,), (0,)), ((), ()))
    scores = lax.dot_general(qs, kc, nt, preferred_element_type=jnp.float32) * scale
    peak = jnp.max(scores, axis=1, keepdims=True)
    lifted = jnp.exp(scores - peak)
    probs = lifted * (1.0 / jnp.sum(lifted, axis=1, keepdims=True))
    probs_b = probs.astype(jnp.bfloat16)
    attended = jnp.dot(probs_b, vc, preferred_element_type=jnp.float32)
    delta = jnp.sum(dos.astype(jnp.float32) * attended, axis=1, keepdims=True)
    dprobs = lax.dot_general(dos, vc, nt, preferred_element_type=jnp.float32)
    dscores = (probs * (dprobs - delta) * scale).astype(jnp.bfloat16)
    dq = jnp.dot(dscores, kc, preferred_element_type=jnp.float32)
    for h in range(hpk):
        dq_ref[:, h * HD:(h + 1) * HD] = dq[h * BLK:(h + 1) * BLK].astype(jnp.bfloat16)
    kterm = lax.dot_general(qs, dscores, tn, preferred_element_type=jnp.float32)
    vterm = lax.dot_general(dos, probs_b, tn, preferred_element_type=jnp.float32)

    for s in range(SLOTS):
        kind = kind_ref[b * SLOTS + s]
        row = pl.multiple_of(dst_ref[b * SLOTS + s] * BLK, BLK)
        kt = kterm[:, s * BLK:(s + 1) * BLK]
        vt = vterm[:, s * BLK:(s + 1) * BLK]
        rounded = kind == 0
        kt = jnp.where(rounded, kt.astype(jnp.bfloat16).astype(jnp.float32), kt)
        vt = jnp.where(rounded, vt.astype(jnp.bfloat16).astype(jnp.float32), vt)

        @pl.when(kind == 2)
        def _():
            loc_acc[g, pl.ds(row, BLK), :] += kt
            loc_acc[kv_here + g, pl.ds(row, BLK), :] += vt

        side = side_ref[b * SLOTS + s]

        @pl.when((kind != 2) & (side == 0))
        def _():
            far_acc[g, pl.ds(row, BLK), :] += kt
            far_acc[kv_here + g, pl.ds(row, BLK), :] += vt

        @pl.when((kind != 2) & (side == 1))
        def _():
            fo_acc[g, pl.ds(row, BLK), :] += kt
            fo_acc[kv_here + g, pl.ds(row, BLK), :] += vt

    @pl.when((g == kv_here - 1) & (b == nb - 1))
    def _():
        for j in range(2 * kv_here):
            loc_ref[:, j * HD:(j + 1) * HD] = loc_acc[j]
            far_ref[:, j * HD:(j + 1) * HD] = far_acc[j].astype(jnp.bfloat16)
            fo_ref[:, j * HD:(j + 1) * HD] = fo_acc[j].astype(jnp.bfloat16)


def shards(query_rows, key_rows, value_rows, out_grad, block_list):
    shard_index = lax.axis_index("ctx")
    lane_index = lax.axis_index("uly")
    nb = key_rows.shape[0] // BLK
    seq = block_list.shape[0] * BLK
    heads_here = query_rows.shape[1] // HD
    kv_here = max(1, heads_here // GROUP)
    hpk = heads_here // kv_here
    width = 2 * kv_here * HD
    first_kv = lane_index * heads_here // GROUP
    key_own = lax.dynamic_slice_in_dim(key_rows, first_kv * HD, kv_here * HD, axis=1)
    value_own = lax.dynamic_slice_in_dim(value_rows, first_kv * HD, kv_here * HD, axis=1)
    kv_own = jnp.concatenate([key_own, value_own], axis=1)
    shard_count = lax.axis_size("ctx")
    partner = [(i, i ^ 1) for i in range(shard_count)]
    core = shard_index % 2
    members = shard_count // 2
    member = shard_index // 2
    gathered = [kv_own]
    for d in range(1, members):
        pairs = [(i, (i + 2 * d) % shard_count) for i in range(shard_count)]
        gathered.append(lax.ppermute(kv_own, "ctx", pairs))
    kv_half = jnp.concatenate(gathered, axis=0)
    kv_other = lax.ppermute(kv_half, "ctx", partner)
    half = seq // 2

    rows = lax.dynamic_slice_in_dim(block_list, shard_index * nb, nb, axis=0).astype(jnp.int32)
    owner = rows // nb
    cols = jnp.arange(SLOTS)[None, :]
    is_global = (cols == 3) | (cols == 4)
    local = owner == shard_index
    remote = jnp.logical_not(local) & jnp.logical_not(is_global)
    kind = jnp.where(local, 2, jnp.where(remote, 0, 1)).astype(jnp.int32).reshape(-1)
    owner_side = (owner % 2 != core).astype(jnp.int32)
    half_row = ((member - owner // 2) % members) * nb + rows % nb
    dst = jnp.where(local, rows - shard_index * nb, half_row).astype(jnp.int32).reshape(-1)
    blk = half_row.astype(jnp.int32).reshape(-1)
    side = owner_side.reshape(-1)

    kernel = functools.partial(attention_kernel, hpk=hpk, kv_here=kv_here, nb=nb)
    grid_spec = pltpu.PrefetchScalarGridSpec(
        num_scalar_prefetch=4,
        grid=(kv_here, nb),
        in_specs=[
            pl.BlockSpec((BLK, hpk * HD), lambda g, b, *_: (b, g)),
            pl.BlockSpec((BLK, hpk * HD), lambda g, b, *_: (b, g)),
            pl.BlockSpec((half, HD), lambda g, b, *_: (0, g)),
            pl.BlockSpec((half, HD), lambda g, b, *_: (0, kv_here + g)),
            pl.BlockSpec((half, HD), lambda g, b, *_: (0, g)),
            pl.BlockSpec((half, HD), lambda g, b, *_: (0, kv_here + g)),
        ],
        out_specs=[
            pl.BlockSpec((BLK, hpk * HD), lambda g, b, *_: (b, g)),
            pl.BlockSpec((nb * BLK, width), lambda g, b, *_: (0, 0)),
            pl.BlockSpec((half, width), lambda g, b, *_: (0, 0)),
            pl.BlockSpec((half, width), lambda g, b, *_: (0, 0)),
        ],
        scratch_shapes=[
            pltpu.VMEM((SLOTS * BLK, HD), jnp.bfloat16),
            pltpu.VMEM((SLOTS * BLK, HD), jnp.bfloat16),
            pltpu.VMEM((2 * kv_here, nb * BLK, HD), jnp.float32),
            pltpu.VMEM((2 * kv_here, half, HD), jnp.float32),
            pltpu.VMEM((2 * kv_here, half, HD), jnp.float32),
        ],
    )
    dq, loc, far, far_other = pl.pallas_call(
        kernel,
        grid_spec=grid_spec,
        out_shape=[
            jax.ShapeDtypeStruct((nb * BLK, heads_here * HD), jnp.bfloat16),
            jax.ShapeDtypeStruct((nb * BLK, width), jnp.float32),
            jax.ShapeDtypeStruct((half, width), jnp.bfloat16),
            jax.ShapeDtypeStruct((half, width), jnp.bfloat16),
        ],
        compiler_params=pltpu.CompilerParams(dimension_semantics=("arbitrary", "arbitrary")),
    )(blk, side, dst, kind, query_rows, out_grad, kv_half, kv_half, kv_other, kv_other)

    from_partner = lax.ppermute(far_other, "ctx", partner)
    mine = (far.astype(jnp.float32) + from_partner.astype(jnp.float32)).astype(jnp.bfloat16)
    total = far[0:nb * BLK].astype(jnp.float32) + from_partner[0:nb * BLK].astype(jnp.float32)
    for d in range(1, members):
        pairs = [(i, (i - 2 * d) % shard_count) for i in range(shard_count)]
        total = total + lax.ppermute(
            mine[d * nb * BLK:(d + 1) * nb * BLK], "ctx", pairs
        ).astype(jnp.float32)
    kv_sum = (total + loc).reshape(nb, HD, 2 * kv_here, BLK)
    kv_grad = jnp.transpose(kv_sum, (0, 3, 2, 1)).reshape(nb * BLK, width).astype(jnp.bfloat16)

    query_out = lax.all_to_all(dq, "uly", split_axis=0, concat_axis=1, tiled=True)
    kv_seq = lax.all_to_all(kv_grad, "uly", split_axis=0, concat_axis=1, tiled=True)
    rows_here = kv_seq.shape[0]
    lane_count = kv_seq.shape[1] // width
    spread = kv_seq.reshape(rows_here, lane_count, 2, kv_here * HD)

    def gather_heads(part):
        if heads_here >= GROUP:
            return part.reshape(rows_here, KVH * HD)
        lanes_per = GROUP // heads_here
        merged = part.astype(jnp.float32).reshape(rows_here, KVH, lanes_per, HD).sum(axis=2)
        return merged.reshape(rows_here, KVH * HD).astype(jnp.bfloat16)

    return (query_out, gather_heads(spread[:, :, 0]), gather_heads(spread[:, :, 1]))


def solution(mesh):
    return jax.shard_map(
        shards,
        mesh=mesh,
        in_specs=(P("ctx", "uly"), P("ctx", None), P("ctx", None), P("ctx", "uly"), P()),
        out_specs=(P(("ctx", "uly"), None), P(("ctx", "uly"), None), P(("ctx", "uly"), None)),
        check_vma=False,
    )
```

```python
import functools
import math

import jax
import jax.numpy as jnp
from jax import lax
from jax.experimental import pallas as pl
from jax.experimental.pallas import tpu as pltpu
from jax.sharding import PartitionSpec as P

HD = 128
KVH = 8
BLK = 128
GROUP = 6
SLOTS = 8


def attention_kernel(
    tbl_ref,
    q_ref, do_ref, k_ref, v_ref, ko_ref, vo_ref,
    dq_ref, loc_ref, far_ref, fo_ref,
    kc_ref, vc_ref, loc_acc, far_acc, fo_acc,
    *, hpk, kv_here, nb,
):
    g = pl.program_id(0)
    b = pl.program_id(1)
    scale = 1.0 / math.sqrt(HD)
    count = nb * SLOTS

    def blk_ref(i):
        return tbl_ref[i]

    def side_ref(i):
        return tbl_ref[count + i]

    def dst_ref(i):
        return tbl_ref[2 * count + i]

    def kind_ref(i):
        return tbl_ref[3 * count + i]

    @pl.when((g == 0) & (b == 0))
    def _():
        loc_acc[...] = jnp.zeros_like(loc_acc)
        far_acc[...] = jnp.zeros_like(far_acc)
        fo_acc[...] = jnp.zeros_like(fo_acc)

    for s in range(SLOTS):
        row = pl.multiple_of(blk_ref(b * SLOTS + s) * BLK, BLK)
        side = side_ref(b * SLOTS + s)
        for code, tk, tv in ((0, k_ref, v_ref), (1, ko_ref, vo_ref)):
            @pl.when(side == code)
            def _():
                kc_ref[s * BLK:(s + 1) * BLK, :] = tk[pl.ds(row, BLK), :]
                vc_ref[s * BLK:(s + 1) * BLK, :] = tv[pl.ds(row, BLK), :]

    kc = kc_ref[...]
    vc = vc_ref[...]
    qs = jnp.concatenate([q_ref[:, h * HD:(h + 1) * HD] for h in range(hpk)], axis=0)
    dos = jnp.concatenate([do_ref[:, h * HD:(h + 1) * HD] for h in range(hpk)], axis=0)
    nt = (((1,), (1,)), ((), ()))
    tn = (((0,), (0,)), ((), ()))
    scores = lax.dot_general(qs, kc, nt, preferred_element_type=jnp.float32) * scale
    peak = jnp.max(scores, axis=1, keepdims=True)
    lifted = jnp.exp(scores - peak)
    probs = lifted * (1.0 / jnp.sum(lifted, axis=1, keepdims=True))
    probs_b = probs.astype(jnp.bfloat16)
    attended = jnp.dot(probs_b, vc, preferred_element_type=jnp.float32)
    delta = jnp.sum(dos.astype(jnp.float32) * attended, axis=1, keepdims=True)
    dprobs = lax.dot_general(dos, vc, nt, preferred_element_type=jnp.float32)
    dscores = (probs * (dprobs - delta) * scale).astype(jnp.bfloat16)
    dq = jnp.dot(dscores, kc, preferred_element_type=jnp.float32)
    for h in range(hpk):
        dq_ref[:, h * HD:(h + 1) * HD] = dq[h * BLK:(h + 1) * BLK].astype(jnp.bfloat16)
    kterm = lax.dot_general(qs, dscores, tn, preferred_element_type=jnp.float32)
    vterm = lax.dot_general(dos, probs_b, tn, preferred_element_type=jnp.float32)

    for s in range(SLOTS):
        kind = kind_ref(b * SLOTS + s)
        row = pl.multiple_of(dst_ref(b * SLOTS + s) * BLK, BLK)
        kt = kterm[:, s * BLK:(s + 1) * BLK]
        vt = vterm[:, s * BLK:(s + 1) * BLK]
        rounded = kind == 0
        kt = jnp.where(rounded, kt.astype(jnp.bfloat16).astype(jnp.float32), kt)
        vt = jnp.where(rounded, vt.astype(jnp.bfloat16).astype(jnp.float32), vt)

        @pl.when(kind == 2)
        def _():
            loc_acc[g, pl.ds(row, BLK), :] += kt
            loc_acc[kv_here + g, pl.ds(row, BLK), :] += vt

        side = side_ref(b * SLOTS + s)

        @pl.when((kind != 2) & (side == 0))
        def _():
            far_acc[g, pl.ds(row, BLK), :] += kt
            far_acc[kv_here + g, pl.ds(row, BLK), :] += vt

        @pl.when((kind != 2) & (side == 1))
        def _():
            fo_acc[g, pl.ds(row, BLK), :] += kt
            fo_acc[kv_here + g, pl.ds(row, BLK), :] += vt

    @pl.when((g == kv_here - 1) & (b == nb - 1))
    def _():
        for j in range(2 * kv_here):
            loc_ref[:, j * HD:(j + 1) * HD] = loc_acc[j]
            far_ref[:, j * HD:(j + 1) * HD] = far_acc[j].astype(jnp.bfloat16)
            fo_ref[:, j * HD:(j + 1) * HD] = fo_acc[j].astype(jnp.bfloat16)


def shards(query_rows, key_rows, value_rows, out_grad, block_list):
    shard_index = lax.axis_index("ctx")
    lane_index = lax.axis_index("uly")
    nb = key_rows.shape[0] // BLK
    seq = block_list.shape[0] * BLK
    heads_here = query_rows.shape[1] // HD
    kv_here = max(1, heads_here // GROUP)
    hpk = heads_here // kv_here
    width = 2 * kv_here * HD
    first_kv = lane_index * heads_here // GROUP
    key_own = lax.dynamic_slice_in_dim(key_rows, first_kv * HD, kv_here * HD, axis=1)
    value_own = lax.dynamic_slice_in_dim(value_rows, first_kv * HD, kv_here * HD, axis=1)
    kv_own = jnp.concatenate([key_own, value_own], axis=1)
    shard_count = lax.axis_size("ctx")
    partner = [(i, i ^ 1) for i in range(shard_count)]
    core = shard_index % 2
    members = shard_count // 2
    member = shard_index // 2
    gathered = [kv_own]
    for d in range(1, members):
        pairs = [(i, (i + 2 * d) % shard_count) for i in range(shard_count)]
        gathered.append(lax.ppermute(kv_own, "ctx", pairs))
    kv_half = jnp.concatenate(gathered, axis=0)
    kv_other = jnp.concatenate([lax.ppermute(p, "ctx", partner) for p in gathered], axis=0)
    half = seq // 2

    rows = lax.dynamic_slice_in_dim(block_list, shard_index * nb, nb, axis=0).astype(jnp.int32)
    owner = rows // nb
    cols = jnp.arange(SLOTS)[None, :]
    is_global = (cols == 3) | (cols == 4)
    local = owner == shard_index
    remote = jnp.logical_not(local) & jnp.logical_not(is_global)
    kind = jnp.where(local, 2, jnp.where(remote, 0, 1)).astype(jnp.int32).reshape(-1)
    owner_side = (owner % 2 != core).astype(jnp.int32)
    half_row = ((member - owner // 2) % members) * nb + rows % nb
    dst = jnp.where(local, rows - shard_index * nb, half_row).astype(jnp.int32).reshape(-1)
    blk = half_row.astype(jnp.int32).reshape(-1)
    side = owner_side.reshape(-1)
    table = jnp.concatenate([blk, side, dst, kind]).astype(jnp.int32)

    kernel = functools.partial(attention_kernel, hpk=hpk, kv_here=kv_here, nb=nb)
    grid_spec = pltpu.PrefetchScalarGridSpec(
        num_scalar_prefetch=1,
        grid=(kv_here, nb),
        in_specs=[
            pl.BlockSpec((BLK, hpk * HD), lambda g, b, *_: (b, g)),
            pl.BlockSpec((BLK, hpk * HD), lambda g, b, *_: (b, g)),
            pl.BlockSpec((half, HD), lambda g, b, *_: (0, g)),
            pl.BlockSpec((half, HD), lambda g, b, *_: (0, kv_here + g)),
            pl.BlockSpec((half, HD), lambda g, b, *_: (0, g)),
            pl.BlockSpec((half, HD), lambda g, b, *_: (0, kv_here + g)),
        ],
        out_specs=[
            pl.BlockSpec((BLK, hpk * HD), lambda g, b, *_: (b, g)),
            pl.BlockSpec((nb * BLK, width), lambda g, b, *_: (0, 0)),
            pl.BlockSpec((half, width), lambda g, b, *_: (0, 0)),
            pl.BlockSpec((half, width), lambda g, b, *_: (0, 0)),
        ],
        scratch_shapes=[
            pltpu.VMEM((SLOTS * BLK, HD), jnp.bfloat16),
            pltpu.VMEM((SLOTS * BLK, HD), jnp.bfloat16),
            pltpu.VMEM((2 * kv_here, nb * BLK, HD), jnp.float32),
            pltpu.VMEM((2 * kv_here, half, HD), jnp.float32),
            pltpu.VMEM((2 * kv_here, half, HD), jnp.float32),
        ],
    )
    dq, loc, far, far_other = pl.pallas_call(
        kernel,
        grid_spec=grid_spec,
        out_shape=[
            jax.ShapeDtypeStruct((nb * BLK, heads_here * HD), jnp.bfloat16),
            jax.ShapeDtypeStruct((nb * BLK, width), jnp.float32),
            jax.ShapeDtypeStruct((half, width), jnp.bfloat16),
            jax.ShapeDtypeStruct((half, width), jnp.bfloat16),
        ],
        compiler_params=pltpu.CompilerParams(dimension_semantics=("arbitrary", "arbitrary")),
    )(table, query_rows, out_grad, kv_half, kv_half, kv_other, kv_other)

    span = nb * BLK

    def partner_sum(pos):
        swapped = lax.ppermute(far_other[pos * span:(pos + 1) * span], "ctx", partner)
        return far[pos * span:(pos + 1) * span].astype(jnp.float32) + swapped.astype(jnp.float32)

    total = partner_sum(0)
    for d in range(1, members):
        pairs = [(i, (i - 2 * d) % shard_count) for i in range(shard_count)]
        chunk = partner_sum(d).astype(jnp.bfloat16)
        total = total + lax.ppermute(chunk, "ctx", pairs).astype(jnp.float32)
    kv_sum = (total + loc).reshape(nb, HD, 2 * kv_here, BLK)
    kv_grad = jnp.transpose(kv_sum, (0, 3, 2, 1)).reshape(nb * BLK, width).astype(jnp.bfloat16)

    query_out = lax.all_to_all(dq, "uly", split_axis=0, concat_axis=1, tiled=True)
    kv_seq = lax.all_to_all(kv_grad, "uly", split_axis=0, concat_axis=1, tiled=True)
    rows_here = kv_seq.shape[0]
    lane_count = kv_seq.shape[1] // width
    spread = kv_seq.reshape(rows_here, lane_count, 2, kv_here * HD)

    def gather_heads(part):
        if heads_here >= GROUP:
            return part.reshape(rows_here, KVH * HD)
        lanes_per = GROUP // heads_here
        merged = part.astype(jnp.float32).reshape(rows_here, KVH, lanes_per, HD).sum(axis=2)
        return merged.reshape(rows_here, KVH * HD).astype(jnp.bfloat16)

    return (query_out, gather_heads(spread[:, :, 0]), gather_heads(spread[:, :, 1]))


def solution(mesh):
    return jax.shard_map(
        shards,
        mesh=mesh,
        in_specs=(P("ctx", "uly"), P("ctx", None), P("ctx", None), P("ctx", "uly"), P()),
        out_specs=(P(("ctx", "uly"), None), P(("ctx", "uly"), None), P(("ctx", "uly"), None)),
        check_vma=False,
    )
```

```python
import functools
import math

import jax
import jax.numpy as jnp
from jax import lax
from jax.experimental import pallas as pl
from jax.experimental.pallas import tpu as pltpu
from jax.sharding import PartitionSpec as P

HD = 128
KVH = 8
BLK = 128
GROUP = 6
SLOTS = 8


def attention_kernel(
    tbl_ref,
    q_ref, do_ref, k_ref, v_ref, ko_ref, vo_ref,
    dq_ref, loc_ref, far_ref, fo_ref,
    kc_ref, vc_ref, loc_acc, far_acc, fo_acc,
    *, hpk, kv_here, nb,
):
    g = pl.program_id(0)
    b = pl.program_id(1)
    scale = 1.0 / math.sqrt(HD)
    count = nb * SLOTS

    def blk_ref(i):
        return tbl_ref[i]

    def side_ref(i):
        return tbl_ref[count + i]

    def dst_ref(i):
        return tbl_ref[2 * count + i]

    def kind_ref(i):
        return tbl_ref[3 * count + i]

    @pl.when((g == 0) & (b == 0))
    def _():
        loc_acc[...] = jnp.zeros_like(loc_acc)
        far_acc[...] = jnp.zeros_like(far_acc)
        fo_acc[...] = jnp.zeros_like(fo_acc)

    for s in range(SLOTS):
        row = pl.multiple_of(blk_ref(b * SLOTS + s) * BLK, BLK)
        side = side_ref(b * SLOTS + s)
        for code, tk, tv in ((0, k_ref, v_ref), (1, ko_ref, vo_ref)):
            @pl.when(side == code)
            def _():
                kc_ref[s * BLK:(s + 1) * BLK, :] = tk[pl.ds(row, BLK), :]
                vc_ref[s * BLK:(s + 1) * BLK, :] = tv[pl.ds(row, BLK), :]

    kc = kc_ref[...]
    vc = vc_ref[...]
    qs = jnp.concatenate([q_ref[:, h * HD:(h + 1) * HD] for h in range(hpk)], axis=0)
    dos = jnp.concatenate([do_ref[:, h * HD:(h + 1) * HD] for h in range(hpk)], axis=0)
    nt = (((1,), (1,)), ((), ()))
    tn = (((0,), (0,)), ((), ()))
    scores = lax.dot_general(qs, kc, nt, preferred_element_type=jnp.float32) * scale
    peak = jnp.max(scores, axis=1, keepdims=True)
    lifted = jnp.exp(scores - peak)
    probs = lifted * (1.0 / jnp.sum(lifted, axis=1, keepdims=True))
    probs_b = probs.astype(jnp.bfloat16)
    attended = jnp.dot(probs_b, vc, preferred_element_type=jnp.float32)
    delta = jnp.sum(dos.astype(jnp.float32) * attended, axis=1, keepdims=True)
    dprobs = lax.dot_general(dos, vc, nt, preferred_element_type=jnp.float32)
    dscores = (probs * (dprobs - delta) * scale).astype(jnp.bfloat16)
    dq = jnp.dot(dscores, kc, preferred_element_type=jnp.float32)
    for h in range(hpk):
        dq_ref[:, h * HD:(h + 1) * HD] = dq[h * BLK:(h + 1) * BLK].astype(jnp.bfloat16)
    kterm = lax.dot_general(qs, dscores, tn, preferred_element_type=jnp.float32)
    vterm = lax.dot_general(dos, probs_b, tn, preferred_element_type=jnp.float32)

    for s in range(SLOTS):
        kind = kind_ref(b * SLOTS + s)
        row = pl.multiple_of(dst_ref(b * SLOTS + s) * BLK, BLK)
        kt = kterm[:, s * BLK:(s + 1) * BLK]
        vt = vterm[:, s * BLK:(s + 1) * BLK]
        rounded = kind == 0
        kt = jnp.where(rounded, kt.astype(jnp.bfloat16).astype(jnp.float32), kt)
        vt = jnp.where(rounded, vt.astype(jnp.bfloat16).astype(jnp.float32), vt)

        @pl.when(kind == 2)
        def _():
            loc_acc[g, pl.ds(row, BLK), :] += kt
            loc_acc[kv_here + g, pl.ds(row, BLK), :] += vt

        side = side_ref(b * SLOTS + s)

        @pl.when((kind != 2) & (side == 0))
        def _():
            far_acc[g, pl.ds(row, BLK), :] += kt
            far_acc[kv_here + g, pl.ds(row, BLK), :] += vt

        @pl.when((kind != 2) & (side == 1))
        def _():
            fo_acc[g, pl.ds(row, BLK), :] += kt
            fo_acc[kv_here + g, pl.ds(row, BLK), :] += vt

    @pl.when((g == kv_here - 1) & (b == nb - 1))
    def _():
        for j in range(2 * kv_here):
            loc_ref[:, j * HD:(j + 1) * HD] = loc_acc[j]
            far_ref[:, j * HD:(j + 1) * HD] = far_acc[j].astype(jnp.bfloat16)
            fo_ref[:, j * HD:(j + 1) * HD] = fo_acc[j].astype(jnp.bfloat16)


def lane_transpose(x, lane, lanes):
    rows = x.shape[0] // lanes
    cols = x.shape[1]
    chunks = x.reshape(lanes, rows, cols)
    out = jnp.zeros((rows, lanes * cols), x.dtype)
    own = lax.dynamic_index_in_dim(chunks, lane, 0, keepdims=False)
    out = lax.dynamic_update_slice(out, own, (0, lane * cols))
    for e in range(1, lanes):
        send = lax.dynamic_index_in_dim(chunks, (lane + e) % lanes, 0, keepdims=False)
        pairs = [(i, (i + e) % lanes) for i in range(lanes)]
        got = lax.ppermute(send, "uly", pairs)
        out = lax.dynamic_update_slice(out, got, (0, ((lane - e) % lanes) * cols))
    return out


def shards(query_rows, key_rows, value_rows, out_grad, block_list):
    shard_index = lax.axis_index("ctx")
    lane_index = lax.axis_index("uly")
    nb = key_rows.shape[0] // BLK
    seq = block_list.shape[0] * BLK
    heads_here = query_rows.shape[1] // HD
    kv_here = max(1, heads_here // GROUP)
    hpk = heads_here // kv_here
    width = 2 * kv_here * HD
    first_kv = lane_index * heads_here // GROUP
    key_own = lax.dynamic_slice_in_dim(key_rows, first_kv * HD, kv_here * HD, axis=1)
    value_own = lax.dynamic_slice_in_dim(value_rows, first_kv * HD, kv_here * HD, axis=1)
    kv_own = jnp.concatenate([key_own, value_own], axis=1)
    shard_count = lax.axis_size("ctx")
    partner = [(i, i ^ 1) for i in range(shard_count)]
    core = shard_index % 2
    members = shard_count // 2
    member = shard_index // 2
    gathered = [kv_own]
    for d in range(1, members):
        pairs = [(i, (i + 2 * d) % shard_count) for i in range(shard_count)]
        gathered.append(lax.ppermute(kv_own, "ctx", pairs))
    kv_half = jnp.concatenate(gathered, axis=0)
    kv_other = jnp.concatenate([lax.ppermute(p, "ctx", partner) for p in gathered], axis=0)
    half = seq // 2

    rows = lax.dynamic_slice_in_dim(block_list, shard_index * nb, nb, axis=0).astype(jnp.int32)
    owner = rows // nb
    cols = jnp.arange(SLOTS)[None, :]
    is_global = (cols == 3) | (cols == 4)
    local = owner == shard_index
    remote = jnp.logical_not(local) & jnp.logical_not(is_global)
    kind = jnp.where(local, 2, jnp.where(remote, 0, 1)).astype(jnp.int32).reshape(-1)
    owner_side = (owner % 2 != core).astype(jnp.int32)
    half_row = ((member - owner // 2) % members) * nb + rows % nb
    dst = jnp.where(local, rows - shard_index * nb, half_row).astype(jnp.int32).reshape(-1)
    blk = half_row.astype(jnp.int32).reshape(-1)
    side = owner_side.reshape(-1)
    table = jnp.concatenate([blk, side, dst, kind]).astype(jnp.int32)

    kernel = functools.partial(attention_kernel, hpk=hpk, kv_here=kv_here, nb=nb)
    grid_spec = pltpu.PrefetchScalarGridSpec(
        num_scalar_prefetch=1,
        grid=(kv_here, nb),
        in_specs=[
            pl.BlockSpec((BLK, hpk * HD), lambda g, b, *_: (b, g)),
            pl.BlockSpec((BLK, hpk * HD), lambda g, b, *_: (b, g)),
            pl.BlockSpec((half, HD), lambda g, b, *_: (0, g)),
            pl.BlockSpec((half, HD), lambda g, b, *_: (0, kv_here + g)),
            pl.BlockSpec((half, HD), lambda g, b, *_: (0, g)),
            pl.BlockSpec((half, HD), lambda g, b, *_: (0, kv_here + g)),
        ],
        out_specs=[
            pl.BlockSpec((BLK, hpk * HD), lambda g, b, *_: (b, g)),
            pl.BlockSpec((nb * BLK, width), lambda g, b, *_: (0, 0)),
            pl.BlockSpec((half, width), lambda g, b, *_: (0, 0)),
            pl.BlockSpec((half, width), lambda g, b, *_: (0, 0)),
        ],
        scratch_shapes=[
            pltpu.VMEM((SLOTS * BLK, HD), jnp.bfloat16),
            pltpu.VMEM((SLOTS * BLK, HD), jnp.bfloat16),
            pltpu.VMEM((2 * kv_here, nb * BLK, HD), jnp.float32),
            pltpu.VMEM((2 * kv_here, half, HD), jnp.float32),
            pltpu.VMEM((2 * kv_here, half, HD), jnp.float32),
        ],
    )
    dq, loc, far, far_other = pl.pallas_call(
        kernel,
        grid_spec=grid_spec,
        out_shape=[
            jax.ShapeDtypeStruct((nb * BLK, heads_here * HD), jnp.bfloat16),
            jax.ShapeDtypeStruct((nb * BLK, width), jnp.float32),
            jax.ShapeDtypeStruct((half, width), jnp.bfloat16),
            jax.ShapeDtypeStruct((half, width), jnp.bfloat16),
        ],
        compiler_params=pltpu.CompilerParams(dimension_semantics=("arbitrary", "arbitrary")),
    )(table, query_rows, out_grad, kv_half, kv_half, kv_other, kv_other)

    span = nb * BLK

    def partner_sum(pos):
        swapped = lax.ppermute(far_other[pos * span:(pos + 1) * span], "ctx", partner)
        return far[pos * span:(pos + 1) * span].astype(jnp.float32) + swapped.astype(jnp.float32)

    total = partner_sum(0)
    for d in range(1, members):
        pairs = [(i, (i - 2 * d) % shard_count) for i in range(shard_count)]
        chunk = partner_sum(d).astype(jnp.bfloat16)
        total = total + lax.ppermute(chunk, "ctx", pairs).astype(jnp.float32)
    kv_sum = (total + loc).reshape(nb, HD, 2 * kv_here, BLK)
    kv_grad = jnp.transpose(kv_sum, (0, 3, 2, 1)).reshape(nb * BLK, width).astype(jnp.bfloat16)

    lanes = lax.axis_size("uly")
    query_out = lane_transpose(dq, lane_index, lanes)
    kv_seq = lane_transpose(kv_grad, lane_index, lanes)
    rows_here = kv_seq.shape[0]
    lane_count = kv_seq.shape[1] // width
    spread = kv_seq.reshape(rows_here, lane_count, 2, kv_here * HD)

    def gather_heads(part):
        if heads_here >= GROUP:
            return part.reshape(rows_here, KVH * HD)
        lanes_per = GROUP // heads_here
        merged = part.astype(jnp.float32).reshape(rows_here, KVH, lanes_per, HD).sum(axis=2)
        return merged.reshape(rows_here, KVH * HD).astype(jnp.bfloat16)

    return (query_out, gather_heads(spread[:, :, 0]), gather_heads(spread[:, :, 1]))


def solution(mesh):
    return jax.shard_map(
        shards,
        mesh=mesh,
        in_specs=(P("ctx", "uly"), P("ctx", None), P("ctx", None), P("ctx", "uly"), P()),
        out_specs=(P(("ctx", "uly"), None), P(("ctx", "uly"), None), P(("ctx", "uly"), None)),
        check_vma=False,
    )
```

```python
import functools
import math

import jax
import jax.numpy as jnp
from jax import lax
from jax.experimental import pallas as pl
from jax.experimental.pallas import tpu as pltpu
from jax.sharding import PartitionSpec as P

HD = 128
KVH = 8
BLK = 128
GROUP = 6
SLOTS = 8


def attention_kernel(
    tbl_ref,
    q_ref, do_ref, k_ref, v_ref, ko_ref, vo_ref,
    dq_ref, loc_ref, far_ref, fo_ref,
    kc_ref, vc_ref, loc_acc, far_acc, fo_acc,
    *, hpk, kv_here, nb,
):
    g = pl.program_id(0)
    b = pl.program_id(1)
    scale = 1.0 / math.sqrt(HD)
    count = nb * SLOTS

    def blk_ref(i):
        return tbl_ref[i]

    def side_ref(i):
        return tbl_ref[count + i]

    def dst_ref(i):
        return tbl_ref[2 * count + i]

    def kind_ref(i):
        return tbl_ref[3 * count + i]

    @pl.when((g == 0) & (b == 0))
    def _():
        loc_acc[...] = jnp.zeros_like(loc_acc)
        far_acc[...] = jnp.zeros_like(far_acc)
        fo_acc[...] = jnp.zeros_like(fo_acc)

    for s in range(SLOTS):
        row = pl.multiple_of(blk_ref(b * SLOTS + s) * BLK, BLK)
        side = side_ref(b * SLOTS + s)
        for code, tk, tv in ((0, k_ref, v_ref), (1, ko_ref, vo_ref)):
            @pl.when(side == code)
            def _():
                kc_ref[s * BLK:(s + 1) * BLK, :] = tk[pl.ds(row, BLK), :]
                vc_ref[s * BLK:(s + 1) * BLK, :] = tv[pl.ds(row, BLK), :]

    kc = kc_ref[...]
    vc = vc_ref[...]
    qs = jnp.concatenate([q_ref[:, h * HD:(h + 1) * HD] for h in range(hpk)], axis=0)
    dos = jnp.concatenate([do_ref[:, h * HD:(h + 1) * HD] for h in range(hpk)], axis=0)
    nt = (((1,), (1,)), ((), ()))
    tn = (((0,), (0,)), ((), ()))
    scores = lax.dot_general(qs, kc, nt, preferred_element_type=jnp.float32) * scale
    peak = jnp.max(scores, axis=1, keepdims=True)
    lifted = jnp.exp(scores - peak)
    probs = lifted * (1.0 / jnp.sum(lifted, axis=1, keepdims=True))
    probs_b = probs.astype(jnp.bfloat16)
    attended = jnp.dot(probs_b, vc, preferred_element_type=jnp.float32)
    delta = jnp.sum(dos.astype(jnp.float32) * attended, axis=1, keepdims=True)
    dprobs = lax.dot_general(dos, vc, nt, preferred_element_type=jnp.float32)
    dscores = (probs * (dprobs - delta) * scale).astype(jnp.bfloat16)
    dq = jnp.dot(dscores, kc, preferred_element_type=jnp.float32)
    for h in range(hpk):
        dq_ref[:, h * HD:(h + 1) * HD] = dq[h * BLK:(h + 1) * BLK].astype(jnp.bfloat16)
    kterm = lax.dot_general(qs, dscores, tn, preferred_element_type=jnp.float32)
    vterm = lax.dot_general(dos, probs_b, tn, preferred_element_type=jnp.float32)

    for s in range(SLOTS):
        kind = kind_ref(b * SLOTS + s)
        row = pl.multiple_of(dst_ref(b * SLOTS + s) * BLK, BLK)
        kt = kterm[:, s * BLK:(s + 1) * BLK]
        vt = vterm[:, s * BLK:(s + 1) * BLK]
        rounded = kind == 0
        kt = jnp.where(rounded, kt.astype(jnp.bfloat16).astype(jnp.float32), kt)
        vt = jnp.where(rounded, vt.astype(jnp.bfloat16).astype(jnp.float32), vt)

        @pl.when(kind == 2)
        def _():
            loc_acc[g, pl.ds(row, BLK), :] += kt
            loc_acc[kv_here + g, pl.ds(row, BLK), :] += vt

        side = side_ref(b * SLOTS + s)

        @pl.when((kind != 2) & (side == 0))
        def _():
            far_acc[g, pl.ds(row, BLK), :] += kt
            far_acc[kv_here + g, pl.ds(row, BLK), :] += vt

        @pl.when((kind != 2) & (side == 1))
        def _():
            fo_acc[g, pl.ds(row, BLK), :] += kt
            fo_acc[kv_here + g, pl.ds(row, BLK), :] += vt

    @pl.when((g == kv_here - 1) & (b == nb - 1))
    def _():
        for j in range(2 * kv_here):
            loc_ref[:, j * HD:(j + 1) * HD] = loc_acc[j]
            far_ref[:, j * HD:(j + 1) * HD] = far_acc[j].astype(jnp.bfloat16)
            fo_ref[:, j * HD:(j + 1) * HD] = fo_acc[j].astype(jnp.bfloat16)


def shards(query_rows, key_rows, value_rows, out_grad, block_list):
    shard_index = lax.axis_index("ctx")
    lane_index = lax.axis_index("uly")
    nb = key_rows.shape[0] // BLK
    seq = block_list.shape[0] * BLK
    heads_here = query_rows.shape[1] // HD
    kv_here = max(1, heads_here // GROUP)
    hpk = heads_here // kv_here
    width = 2 * kv_here * HD
    first_kv = lane_index * heads_here // GROUP
    key_own = lax.dynamic_slice_in_dim(key_rows, first_kv * HD, kv_here * HD, axis=1)
    value_own = lax.dynamic_slice_in_dim(value_rows, first_kv * HD, kv_here * HD, axis=1)
    kv_own = jnp.concatenate([key_own, value_own], axis=1)
    shard_count = lax.axis_size("ctx")
    partner = [(i, i ^ 1) for i in range(shard_count)]
    core = shard_index % 2
    members = shard_count // 2
    member = shard_index // 2
    gathered = [kv_own]
    for d in range(1, members):
        pairs = [(i, (i + 2 * d) % shard_count) for i in range(shard_count)]
        gathered.append(lax.ppermute(kv_own, "ctx", pairs))
    kv_half = jnp.concatenate(gathered, axis=0)
    kv_other = lax.ppermute(kv_half, "ctx", partner)
    half = seq // 2

    rows = lax.dynamic_slice_in_dim(block_list, shard_index * nb, nb, axis=0).astype(jnp.int32)
    owner = rows // nb
    cols = jnp.arange(SLOTS)[None, :]
    is_global = (cols == 3) | (cols == 4)
    local = owner == shard_index
    remote = jnp.logical_not(local) & jnp.logical_not(is_global)
    kind = jnp.where(local, 2, jnp.where(remote, 0, 1)).astype(jnp.int32).reshape(-1)
    owner_side = (owner % 2 != core).astype(jnp.int32)
    half_row = ((member - owner // 2) % members) * nb + rows % nb
    dst = jnp.where(local, rows - shard_index * nb, half_row).astype(jnp.int32).reshape(-1)
    blk = half_row.astype(jnp.int32).reshape(-1)
    side = owner_side.reshape(-1)
    table = jnp.concatenate([blk, side, dst, kind]).astype(jnp.int32)

    kernel = functools.partial(attention_kernel, hpk=hpk, kv_here=kv_here, nb=nb)
    grid_spec = pltpu.PrefetchScalarGridSpec(
        num_scalar_prefetch=1,
        grid=(kv_here, nb),
        in_specs=[
            pl.BlockSpec((BLK, hpk * HD), lambda g, b, *_: (b, g)),
            pl.BlockSpec((BLK, hpk * HD), lambda g, b, *_: (b, g)),
            pl.BlockSpec((half, HD), lambda g, b, *_: (0, g)),
            pl.BlockSpec((half, HD), lambda g, b, *_: (0, kv_here + g)),
            pl.BlockSpec((half, HD), lambda g, b, *_: (0, g)),
            pl.BlockSpec((half, HD), lambda g, b, *_: (0, kv_here + g)),
        ],
        out_specs=[
            pl.BlockSpec((BLK, hpk * HD), lambda g, b, *_: (b, g)),
            pl.BlockSpec((nb * BLK, width), lambda g, b, *_: (0, 0)),
            pl.BlockSpec((half, width), lambda g, b, *_: (0, 0)),
            pl.BlockSpec((half, width), lambda g, b, *_: (0, 0)),
        ],
        scratch_shapes=[
            pltpu.VMEM((SLOTS * BLK, HD), jnp.bfloat16),
            pltpu.VMEM((SLOTS * BLK, HD), jnp.bfloat16),
            pltpu.VMEM((2 * kv_here, nb * BLK, HD), jnp.float32),
            pltpu.VMEM((2 * kv_here, half, HD), jnp.float32),
            pltpu.VMEM((2 * kv_here, half, HD), jnp.float32),
        ],
    )
    dq, loc, far, far_other = pl.pallas_call(
        kernel,
        grid_spec=grid_spec,
        out_shape=[
            jax.ShapeDtypeStruct((nb * BLK, heads_here * HD), jnp.bfloat16),
            jax.ShapeDtypeStruct((nb * BLK, width), jnp.float32),
            jax.ShapeDtypeStruct((half, width), jnp.bfloat16),
            jax.ShapeDtypeStruct((half, width), jnp.bfloat16),
        ],
        compiler_params=pltpu.CompilerParams(dimension_semantics=("arbitrary", "arbitrary")),
    )(table, query_rows, out_grad, kv_half, kv_half, kv_other, kv_other)

    from_partner = lax.ppermute(far_other, "ctx", partner)
    mine = (far.astype(jnp.float32) + from_partner.astype(jnp.float32)).astype(jnp.bfloat16)
    total = far[0:nb * BLK].astype(jnp.float32) + from_partner[0:nb * BLK].astype(jnp.float32)
    for d in range(1, members):
        pairs = [(i, (i - 2 * d) % shard_count) for i in range(shard_count)]
        total = total + lax.ppermute(
            mine[d * nb * BLK:(d + 1) * nb * BLK], "ctx", pairs
        ).astype(jnp.float32)
    kv_sum = (total + loc).reshape(nb, HD, 2 * kv_here, BLK)
    kv_grad = jnp.transpose(kv_sum, (0, 3, 2, 1)).reshape(nb * BLK, width).astype(jnp.bfloat16)

    query_out = lax.all_to_all(dq, "uly", split_axis=0, concat_axis=1, tiled=True)
    kv_seq = lax.all_to_all(kv_grad, "uly", split_axis=0, concat_axis=1, tiled=True)
    rows_here = kv_seq.shape[0]
    lane_count = kv_seq.shape[1] // width
    spread = kv_seq.reshape(rows_here, lane_count, 2, kv_here * HD)

    def gather_heads(part):
        if heads_here >= GROUP:
            return part.reshape(rows_here, KVH * HD)
        lanes_per = GROUP // heads_here
        merged = part.astype(jnp.float32).reshape(rows_here, KVH, lanes_per, HD).sum(axis=2)
        return merged.reshape(rows_here, KVH * HD).astype(jnp.bfloat16)

    return (query_out, gather_heads(spread[:, :, 0]), gather_heads(spread[:, :, 1]))


def solution(mesh):
    return jax.shard_map(
        shards,
        mesh=mesh,
        in_specs=(P("ctx", "uly"), P("ctx", None), P("ctx", None), P("ctx", "uly"), P()),
        out_specs=(P(("ctx", "uly"), None), P(("ctx", "uly"), None), P(("ctx", "uly"), None)),
        check_vma=False,
    )
```

```python
import functools
import math

import jax
import jax.numpy as jnp
from jax import lax
from jax.experimental import pallas as pl
from jax.experimental.pallas import tpu as pltpu
from jax.sharding import PartitionSpec as P

HD = 128
KVH = 8
BLK = 128
GROUP = 6
SLOTS = 8


def attention_kernel(
    tbl_ref,
    q_ref, do_ref, k_ref, v_ref, ko_ref, vo_ref, dq_in,
    dq_ref, loc_ref, far_ref, fo_ref,
    kc_ref, vc_ref, loc_acc, far_acc, fo_acc,
    *, hpk, kv_here, nb,
):
    g = pl.program_id(0)
    b = pl.program_id(1)
    scale = 1.0 / math.sqrt(HD)
    count = nb * SLOTS

    def blk_ref(i):
        return tbl_ref[i]

    def side_ref(i):
        return tbl_ref[count + i]

    def dst_ref(i):
        return tbl_ref[2 * count + i]

    def kind_ref(i):
        return tbl_ref[3 * count + i]

    @pl.when((g == 0) & (b == 0))
    def _():
        loc_acc[...] = jnp.zeros_like(loc_acc)
        far_acc[...] = jnp.zeros_like(far_acc)
        fo_acc[...] = jnp.zeros_like(fo_acc)

    for s in range(SLOTS):
        row = pl.multiple_of(blk_ref(b * SLOTS + s) * BLK, BLK)
        side = side_ref(b * SLOTS + s)
        for code, tk, tv in ((0, k_ref, v_ref), (1, ko_ref, vo_ref)):
            @pl.when(side == code)
            def _():
                kc_ref[s * BLK:(s + 1) * BLK, :] = tk[pl.ds(row, BLK), :]
                vc_ref[s * BLK:(s + 1) * BLK, :] = tv[pl.ds(row, BLK), :]

    kc = kc_ref[...]
    vc = vc_ref[...]
    qs = jnp.concatenate([q_ref[:, h * HD:(h + 1) * HD] for h in range(hpk)], axis=0)
    dos = jnp.concatenate([do_ref[:, h * HD:(h + 1) * HD] for h in range(hpk)], axis=0)
    nt = (((1,), (1,)), ((), ()))
    tn = (((0,), (0,)), ((), ()))
    scores = lax.dot_general(qs, kc, nt, preferred_element_type=jnp.float32) * scale
    peak = jnp.max(scores, axis=1, keepdims=True)
    lifted = jnp.exp(scores - peak)
    probs = lifted * (1.0 / jnp.sum(lifted, axis=1, keepdims=True))
    probs_b = probs.astype(jnp.bfloat16)
    attended = jnp.dot(probs_b, vc, preferred_element_type=jnp.float32)
    delta = jnp.sum(dos.astype(jnp.float32) * attended, axis=1, keepdims=True)
    dprobs = lax.dot_general(dos, vc, nt, preferred_element_type=jnp.float32)
    dscores = (probs * (dprobs - delta) * scale).astype(jnp.bfloat16)
    dq = jnp.dot(dscores, kc, preferred_element_type=jnp.float32)
    for h in range(hpk):
        dq_ref[:, h * HD:(h + 1) * HD] = dq[h * BLK:(h + 1) * BLK].astype(jnp.bfloat16)
    kterm = lax.dot_general(qs, dscores, tn, preferred_element_type=jnp.float32)
    vterm = lax.dot_general(dos, probs_b, tn, preferred_element_type=jnp.float32)

    for s in range(SLOTS):
        kind = kind_ref(b * SLOTS + s)
        row = pl.multiple_of(dst_ref(b * SLOTS + s) * BLK, BLK)
        kt = kterm[:, s * BLK:(s + 1) * BLK]
        vt = vterm[:, s * BLK:(s + 1) * BLK]
        rounded = kind == 0
        kt = jnp.where(rounded, kt.astype(jnp.bfloat16).astype(jnp.float32), kt)
        vt = jnp.where(rounded, vt.astype(jnp.bfloat16).astype(jnp.float32), vt)

        @pl.when(kind == 2)
        def _():
            loc_acc[g, pl.ds(row, BLK), :] += kt
            loc_acc[kv_here + g, pl.ds(row, BLK), :] += vt

        side = side_ref(b * SLOTS + s)

        @pl.when((kind != 2) & (side == 0))
        def _():
            far_acc[g, pl.ds(row, BLK), :] += kt
            far_acc[kv_here + g, pl.ds(row, BLK), :] += vt

        @pl.when((kind != 2) & (side == 1))
        def _():
            fo_acc[g, pl.ds(row, BLK), :] += kt
            fo_acc[kv_here + g, pl.ds(row, BLK), :] += vt

    @pl.when((g == kv_here - 1) & (b == nb - 1))
    def _():
        for j in range(2 * kv_here):
            loc_ref[:, j * HD:(j + 1) * HD] = loc_acc[j]
            far_ref[:, j * HD:(j + 1) * HD] = far_acc[j].astype(jnp.bfloat16)
            fo_ref[:, j * HD:(j + 1) * HD] = fo_acc[j].astype(jnp.bfloat16)


def shards(query_rows, key_rows, value_rows, out_grad, block_list):
    shard_index = lax.axis_index("ctx")
    lane_index = lax.axis_index("uly")
    nb = key_rows.shape[0] // BLK
    seq = block_list.shape[0] * BLK
    heads_here = query_rows.shape[1] // HD
    kv_here = max(1, heads_here // GROUP)
    hpk = heads_here // kv_here
    width = 2 * kv_here * HD
    first_kv = lane_index * heads_here // GROUP
    shard_count = lax.axis_size("ctx")
    partner = [(i, i ^ 1) for i in range(shard_count)]
    core = shard_index % 2
    members = shard_count // 2
    member = shard_index // 2
    half = seq // 2
    span = nb * BLK

    rows = lax.dynamic_slice_in_dim(block_list, shard_index * nb, nb, axis=0).astype(jnp.int32)
    owner = rows // nb
    cols = jnp.arange(SLOTS)[None, :]
    is_global = (cols == 3) | (cols == 4)
    local = owner == shard_index
    remote = jnp.logical_not(local) & jnp.logical_not(is_global)
    kind = jnp.where(local, 2, jnp.where(remote, 0, 1)).astype(jnp.int32).reshape(-1)
    owner_side = (owner % 2 != core).astype(jnp.int32)
    half_row = ((member - owner // 2) % members) * nb + rows % nb
    dst = jnp.where(local, rows - shard_index * nb, half_row).astype(jnp.int32).reshape(-1)
    blk = half_row.astype(jnp.int32).reshape(-1)
    side = owner_side.reshape(-1)
    table = jnp.concatenate([blk, side, dst, kind]).astype(jnp.int32)

    kernel = functools.partial(attention_kernel, hpk=hpk, kv_here=1, nb=nb)
    dq = jnp.zeros((nb * BLK, heads_here * HD), jnp.bfloat16)
    sums = []
    for g in range(kv_here):
        col = (first_kv + g) * HD
        kv_own = jnp.concatenate(
            [
                lax.dynamic_slice_in_dim(key_rows, col, HD, axis=1),
                lax.dynamic_slice_in_dim(value_rows, col, HD, axis=1),
            ],
            axis=1,
        )
        gathered = [kv_own]
        for d in range(1, members):
            pairs = [(i, (i + 2 * d) % shard_count) for i in range(shard_count)]
            gathered.append(lax.ppermute(kv_own, "ctx", pairs))
        kv_half = jnp.concatenate(gathered, axis=0)
        kv_other = lax.ppermute(kv_half, "ctx", partner)
        grid_spec = pltpu.PrefetchScalarGridSpec(
            num_scalar_prefetch=1,
            grid=(1, nb),
            in_specs=[
                pl.BlockSpec((BLK, hpk * HD), lambda z, b, *_, g=g: (b, g)),
                pl.BlockSpec((BLK, hpk * HD), lambda z, b, *_, g=g: (b, g)),
                pl.BlockSpec((half, HD), lambda z, b, *_: (0, 0)),
                pl.BlockSpec((half, HD), lambda z, b, *_: (0, 1)),
                pl.BlockSpec((half, HD), lambda z, b, *_: (0, 0)),
                pl.BlockSpec((half, HD), lambda z, b, *_: (0, 1)),
                pl.BlockSpec(memory_space=pl.ANY),
            ],
            out_specs=[
                pl.BlockSpec((BLK, hpk * HD), lambda z, b, *_, g=g: (b, g)),
                pl.BlockSpec((span, 2 * HD), lambda z, b, *_: (0, 0)),
                pl.BlockSpec((half, 2 * HD), lambda z, b, *_: (0, 0)),
                pl.BlockSpec((half, 2 * HD), lambda z, b, *_: (0, 0)),
            ],
            scratch_shapes=[
                pltpu.VMEM((SLOTS * BLK, HD), jnp.bfloat16),
                pltpu.VMEM((SLOTS * BLK, HD), jnp.bfloat16),
                pltpu.VMEM((2, span, HD), jnp.float32),
                pltpu.VMEM((2, half, HD), jnp.float32),
                pltpu.VMEM((2, half, HD), jnp.float32),
            ],
        )
        dq, loc, far, far_other = pl.pallas_call(
            kernel,
            grid_spec=grid_spec,
            out_shape=[
                jax.ShapeDtypeStruct((nb * BLK, heads_here * HD), jnp.bfloat16),
                jax.ShapeDtypeStruct((span, 2 * HD), jnp.float32),
                jax.ShapeDtypeStruct((half, 2 * HD), jnp.bfloat16),
                jax.ShapeDtypeStruct((half, 2 * HD), jnp.bfloat16),
            ],
            input_output_aliases={7: 0},
            compiler_params=pltpu.CompilerParams(dimension_semantics=("arbitrary", "arbitrary")),
        )(table, query_rows, out_grad, kv_half, kv_half, kv_other, kv_other, dq)
        from_partner = lax.ppermute(far_other, "ctx", partner)
        mine = (far.astype(jnp.float32) + from_partner.astype(jnp.float32)).astype(jnp.bfloat16)
        total = far[0:span].astype(jnp.float32) + from_partner[0:span].astype(jnp.float32)
        for d in range(1, members):
            pairs = [(i, (i - 2 * d) % shard_count) for i in range(shard_count)]
            total = total + lax.ppermute(
                mine[d * span:(d + 1) * span], "ctx", pairs
            ).astype(jnp.float32)
        sums.append((total + loc).reshape(nb, HD, 2, BLK))
    stacked = jnp.stack([s[:, :, 0] for s in sums] + [s[:, :, 1] for s in sums], axis=2)
    kv_grad = jnp.transpose(stacked, (0, 3, 2, 1)).reshape(span, 2 * kv_here * HD).astype(jnp.bfloat16)
    width = 2 * kv_here * HD

    query_out = lax.all_to_all(dq, "uly", split_axis=0, concat_axis=1, tiled=True)
    kv_seq = lax.all_to_all(kv_grad, "uly", split_axis=0, concat_axis=1, tiled=True)
    rows_here = kv_seq.shape[0]
    lane_count = kv_seq.shape[1] // width
    spread = kv_seq.reshape(rows_here, lane_count, 2, kv_here * HD)

    def gather_heads(part):
        if heads_here >= GROUP:
            return part.reshape(rows_here, KVH * HD)
        lanes_per = GROUP // heads_here
        merged = part.astype(jnp.float32).reshape(rows_here, KVH, lanes_per, HD).sum(axis=2)
        return merged.reshape(rows_here, KVH * HD).astype(jnp.bfloat16)

    return (query_out, gather_heads(spread[:, :, 0]), gather_heads(spread[:, :, 1]))


def solution(mesh):
    return jax.shard_map(
        shards,
        mesh=mesh,
        in_specs=(P("ctx", "uly"), P("ctx", None), P("ctx", None), P("ctx", "uly"), P()),
        out_specs=(P(("ctx", "uly"), None), P(("ctx", "uly"), None), P(("ctx", "uly"), None)),
        check_vma=False,
    )
```

```python
import functools
import math

import jax
import jax.numpy as jnp
from jax import lax
from jax.experimental import pallas as pl
from jax.experimental.pallas import tpu as pltpu
from jax.sharding import PartitionSpec as P

HD = 128
KVH = 8
BLK = 128
GROUP = 6
SLOTS = 8


def attention_kernel(
    tbl_ref,
    q_ref, do_ref, k_ref, v_ref, ko_ref, vo_ref, dq_in,
    dq_ref, loc_ref, far_ref, fo_ref,
    kc_ref, vc_ref, loc_acc, far_acc, fo_acc,
    *, hpk, kv_here, nb,
):
    g = pl.program_id(0)
    b = pl.program_id(1)
    scale = 1.0 / math.sqrt(HD)
    count = nb * SLOTS

    def blk_ref(i):
        return tbl_ref[i]

    def side_ref(i):
        return tbl_ref[count + i]

    def dst_ref(i):
        return tbl_ref[2 * count + i]

    def kind_ref(i):
        return tbl_ref[3 * count + i]

    @pl.when((g == 0) & (b == 0))
    def _():
        loc_acc[...] = jnp.zeros_like(loc_acc)
        far_acc[...] = jnp.zeros_like(far_acc)
        fo_acc[...] = jnp.zeros_like(fo_acc)

    for s in range(SLOTS):
        row = pl.multiple_of(blk_ref(b * SLOTS + s) * BLK, BLK)
        side = side_ref(b * SLOTS + s)
        for code, tk, tv in ((0, k_ref, v_ref), (1, ko_ref, vo_ref)):
            @pl.when(side == code)
            def _():
                kc_ref[s * BLK:(s + 1) * BLK, :] = tk[pl.ds(row, BLK), :]
                vc_ref[s * BLK:(s + 1) * BLK, :] = tv[pl.ds(row, BLK), :]

    kc = kc_ref[...]
    vc = vc_ref[...]
    qs = jnp.concatenate([q_ref[:, h * HD:(h + 1) * HD] for h in range(hpk)], axis=0)
    dos = jnp.concatenate([do_ref[:, h * HD:(h + 1) * HD] for h in range(hpk)], axis=0)
    nt = (((1,), (1,)), ((), ()))
    tn = (((0,), (0,)), ((), ()))
    scores = lax.dot_general(qs, kc, nt, preferred_element_type=jnp.float32) * scale
    peak = jnp.max(scores, axis=1, keepdims=True)
    lifted = jnp.exp(scores - peak)
    probs = lifted * (1.0 / jnp.sum(lifted, axis=1, keepdims=True))
    probs_b = probs.astype(jnp.bfloat16)
    attended = jnp.dot(probs_b, vc, preferred_element_type=jnp.float32)
    delta = jnp.sum(dos.astype(jnp.float32) * attended, axis=1, keepdims=True)
    dprobs = lax.dot_general(dos, vc, nt, preferred_element_type=jnp.float32)
    dscores = (probs * (dprobs - delta) * scale).astype(jnp.bfloat16)
    dq = jnp.dot(dscores, kc, preferred_element_type=jnp.float32)
    for h in range(hpk):
        dq_ref[:, h * HD:(h + 1) * HD] = dq[h * BLK:(h + 1) * BLK].astype(jnp.bfloat16)
    kterm = lax.dot_general(qs, dscores, tn, preferred_element_type=jnp.float32)
    vterm = lax.dot_general(dos, probs_b, tn, preferred_element_type=jnp.float32)

    for s in range(SLOTS):
        kind = kind_ref(b * SLOTS + s)
        row = pl.multiple_of(dst_ref(b * SLOTS + s) * BLK, BLK)
        kt = kterm[:, s * BLK:(s + 1) * BLK]
        vt = vterm[:, s * BLK:(s + 1) * BLK]
        rounded = kind == 0
        kt = jnp.where(rounded, kt.astype(jnp.bfloat16).astype(jnp.float32), kt)
        vt = jnp.where(rounded, vt.astype(jnp.bfloat16).astype(jnp.float32), vt)

        @pl.when(kind == 2)
        def _():
            loc_acc[g, pl.ds(row, BLK), :] += kt
            loc_acc[kv_here + g, pl.ds(row, BLK), :] += vt

        side = side_ref(b * SLOTS + s)

        @pl.when((kind != 2) & (side == 0))
        def _():
            far_acc[g, pl.ds(row, BLK), :] += kt
            far_acc[kv_here + g, pl.ds(row, BLK), :] += vt

        @pl.when((kind != 2) & (side == 1))
        def _():
            fo_acc[g, pl.ds(row, BLK), :] += kt
            fo_acc[kv_here + g, pl.ds(row, BLK), :] += vt

    @pl.when((g == kv_here - 1) & (b == nb - 1))
    def _():
        for j in range(2 * kv_here):
            loc_ref[:, j * HD:(j + 1) * HD] = loc_acc[j]
            far_ref[:, j * HD:(j + 1) * HD] = far_acc[j].astype(jnp.bfloat16)
            fo_ref[:, j * HD:(j + 1) * HD] = fo_acc[j].astype(jnp.bfloat16)


def shards(query_rows, key_rows, value_rows, out_grad, block_list):
    shard_index = lax.axis_index("ctx")
    lane_index = lax.axis_index("uly")
    nb = key_rows.shape[0] // BLK
    seq = block_list.shape[0] * BLK
    heads_here = query_rows.shape[1] // HD
    kv_here = max(1, heads_here // GROUP)
    hpk = heads_here // kv_here
    width = 2 * kv_here * HD
    first_kv = lane_index * heads_here // GROUP
    shard_count = lax.axis_size("ctx")
    partner = [(i, i ^ 1) for i in range(shard_count)]
    core = shard_index % 2
    members = shard_count // 2
    member = shard_index // 2
    half = seq // 2
    span = nb * BLK

    rows = lax.dynamic_slice_in_dim(block_list, shard_index * nb, nb, axis=0).astype(jnp.int32)
    owner = rows // nb
    cols = jnp.arange(SLOTS)[None, :]
    is_global = (cols == 3) | (cols == 4)
    local = owner == shard_index
    remote = jnp.logical_not(local) & jnp.logical_not(is_global)
    kind = jnp.where(local, 2, jnp.where(remote, 0, 1)).astype(jnp.int32).reshape(-1)
    owner_side = (owner % 2 != core).astype(jnp.int32)
    half_row = ((member - owner // 2) % members) * nb + rows % nb
    dst = jnp.where(local, rows - shard_index * nb, half_row).astype(jnp.int32).reshape(-1)
    blk = half_row.astype(jnp.int32).reshape(-1)
    side = owner_side.reshape(-1)
    table = jnp.concatenate([blk, side, dst, kind]).astype(jnp.int32)

    kernel = functools.partial(attention_kernel, hpk=hpk, kv_here=1, nb=nb)
    dq = jnp.zeros((nb * BLK, heads_here * HD), jnp.bfloat16)
    sums = []
    for g in range(kv_here):
        col = (first_kv + g) * HD
        kv_own = jnp.concatenate(
            [
                lax.dynamic_slice_in_dim(key_rows, col, HD, axis=1),
                lax.dynamic_slice_in_dim(value_rows, col, HD, axis=1),
            ],
            axis=1,
        )
        gathered = [kv_own]
        for d in range(1, members):
            pairs = [(i, (i + 2 * d) % shard_count) for i in range(shard_count)]
            gathered.append(lax.ppermute(kv_own, "ctx", pairs))
        kv_half = jnp.concatenate(gathered, axis=0)
        kv_other = lax.ppermute(kv_half, "ctx", partner)
        grid_spec = pltpu.PrefetchScalarGridSpec(
            num_scalar_prefetch=1,
            grid=(1, nb),
            in_specs=[
                pl.BlockSpec((BLK, hpk * HD), lambda z, b, *_, g=g: (b, g)),
                pl.BlockSpec((BLK, hpk * HD), lambda z, b, *_, g=g: (b, g)),
                pl.BlockSpec((half, HD), lambda z, b, *_: (0, 0)),
                pl.BlockSpec((half, HD), lambda z, b, *_: (0, 1)),
                pl.BlockSpec((half, HD), lambda z, b, *_: (0, 0)),
                pl.BlockSpec((half, HD), lambda z, b, *_: (0, 1)),
                pl.BlockSpec(memory_space=pl.ANY),
            ],
            out_specs=[
                pl.BlockSpec((BLK, hpk * HD), lambda z, b, *_, g=g: (b, g)),
                pl.BlockSpec((span, 2 * HD), lambda z, b, *_: (0, 0)),
                pl.BlockSpec((half, 2 * HD), lambda z, b, *_: (0, 0)),
                pl.BlockSpec((half, 2 * HD), lambda z, b, *_: (0, 0)),
            ],
            scratch_shapes=[
                pltpu.VMEM((SLOTS * BLK, HD), jnp.bfloat16),
                pltpu.VMEM((SLOTS * BLK, HD), jnp.bfloat16),
                pltpu.VMEM((2, span, HD), jnp.float32),
                pltpu.VMEM((2, half, HD), jnp.float32),
                pltpu.VMEM((2, half, HD), jnp.float32),
            ],
        )
        dq, loc, far, far_other = pl.pallas_call(
            kernel,
            grid_spec=grid_spec,
            out_shape=[
                jax.ShapeDtypeStruct((nb * BLK, heads_here * HD), jnp.bfloat16),
                jax.ShapeDtypeStruct((span, 2 * HD), jnp.float32),
                jax.ShapeDtypeStruct((half, 2 * HD), jnp.bfloat16),
                jax.ShapeDtypeStruct((half, 2 * HD), jnp.bfloat16),
            ],
            input_output_aliases={7: 0},
            compiler_params=pltpu.CompilerParams(dimension_semantics=("arbitrary", "arbitrary")),
        )(table, query_rows, out_grad, kv_half, kv_half, kv_other, kv_other, dq)
        from_partner = lax.ppermute(far_other, "ctx", partner)
        mine = (far.astype(jnp.float32) + from_partner.astype(jnp.float32)).astype(jnp.bfloat16)
        total = far[0:span].astype(jnp.float32) + from_partner[0:span].astype(jnp.float32)
        for d in range(1, members):
            pairs = [(i, (i - 2 * d) % shard_count) for i in range(shard_count)]
            total = total + lax.ppermute(
                mine[d * span:(d + 1) * span], "ctx", pairs
            ).astype(jnp.float32)
        sums.append((total + loc).reshape(nb, HD, 2, BLK))
    stacked = jnp.stack([s[:, :, 0] for s in sums] + [s[:, :, 1] for s in sums], axis=2)
    kv_grad = jnp.transpose(stacked, (0, 3, 2, 1)).reshape(span, 2 * kv_here * HD).astype(jnp.bfloat16)
    width = 2 * kv_here * HD

    query_out = lax.all_to_all(dq, "uly", split_axis=0, concat_axis=1, tiled=True)
    query_out, kv_grad = lax.optimization_barrier((query_out, kv_grad))
    kv_seq = lax.all_to_all(kv_grad, "uly", split_axis=0, concat_axis=1, tiled=True)
    rows_here = kv_seq.shape[0]
    lane_count = kv_seq.shape[1] // width
    spread = kv_seq.reshape(rows_here, lane_count, 2, kv_here * HD)

    def gather_heads(part):
        if heads_here >= GROUP:
            return part.reshape(rows_here, KVH * HD)
        lanes_per = GROUP // heads_here
        merged = part.astype(jnp.float32).reshape(rows_here, KVH, lanes_per, HD).sum(axis=2)
        return merged.reshape(rows_here, KVH * HD).astype(jnp.bfloat16)

    return (query_out, gather_heads(spread[:, :, 0]), gather_heads(spread[:, :, 1]))


def solution(mesh):
    return jax.shard_map(
        shards,
        mesh=mesh,
        in_specs=(P("ctx", "uly"), P("ctx", None), P("ctx", None), P("ctx", "uly"), P()),
        out_specs=(P(("ctx", "uly"), None), P(("ctx", "uly"), None), P(("ctx", "uly"), None)),
        check_vma=False,
    )
```

```python
import functools
import math

import jax
import jax.numpy as jnp
from jax import lax
from jax.experimental import pallas as pl
from jax.experimental.pallas import tpu as pltpu
from jax.sharding import PartitionSpec as P

HD = 128
KVH = 8
BLK = 128
GROUP = 6
SLOTS = 8


def attention_kernel(
    tbl_ref,
    q_ref, do_ref, k_ref, v_ref, ko_ref, vo_ref, dq_in,
    dq_ref, loc_ref, far_ref, fo_ref,
    kc_ref, vc_ref, loc_acc, far_acc, fo_acc,
    *, hpk, kv_here, nb,
):
    g = pl.program_id(0)
    b = pl.program_id(1)
    scale = 1.0 / math.sqrt(HD)
    count = nb * SLOTS

    def blk_ref(i):
        return tbl_ref[i]

    def side_ref(i):
        return tbl_ref[count + i]

    def dst_ref(i):
        return tbl_ref[2 * count + i]

    def kind_ref(i):
        return tbl_ref[3 * count + i]

    @pl.when((g == 0) & (b == 0))
    def _():
        loc_acc[...] = jnp.zeros_like(loc_acc)
        far_acc[...] = jnp.zeros_like(far_acc)
        fo_acc[...] = jnp.zeros_like(fo_acc)

    for s in range(SLOTS):
        row = pl.multiple_of(blk_ref(b * SLOTS + s) * BLK, BLK)
        side = side_ref(b * SLOTS + s)
        for code, tk, tv in ((0, k_ref, v_ref), (1, ko_ref, vo_ref)):
            @pl.when(side == code)
            def _():
                kc_ref[s * BLK:(s + 1) * BLK, :] = tk[pl.ds(row, BLK), :]
                vc_ref[s * BLK:(s + 1) * BLK, :] = tv[pl.ds(row, BLK), :]

    kc = kc_ref[...]
    vc = vc_ref[...]
    qs = jnp.concatenate([q_ref[:, h * HD:(h + 1) * HD] for h in range(hpk)], axis=0)
    dos = jnp.concatenate([do_ref[:, h * HD:(h + 1) * HD] for h in range(hpk)], axis=0)
    nt = (((1,), (1,)), ((), ()))
    tn = (((0,), (0,)), ((), ()))
    scores = lax.dot_general(qs, kc, nt, preferred_element_type=jnp.float32) * scale
    peak = jnp.max(scores, axis=1, keepdims=True)
    lifted = jnp.exp(scores - peak)
    probs = lifted * (1.0 / jnp.sum(lifted, axis=1, keepdims=True))
    probs_b = probs.astype(jnp.bfloat16)
    attended = jnp.dot(probs_b, vc, preferred_element_type=jnp.float32)
    delta = jnp.sum(dos.astype(jnp.float32) * attended, axis=1, keepdims=True)
    dprobs = lax.dot_general(dos, vc, nt, preferred_element_type=jnp.float32)
    dscores = (probs * (dprobs - delta) * scale).astype(jnp.bfloat16)
    dq = jnp.dot(dscores, kc, preferred_element_type=jnp.float32)
    for h in range(hpk):
        dq_ref[:, h * HD:(h + 1) * HD] = dq[h * BLK:(h + 1) * BLK].astype(jnp.bfloat16)
    kterm = lax.dot_general(qs, dscores, tn, preferred_element_type=jnp.float32)
    vterm = lax.dot_general(dos, probs_b, tn, preferred_element_type=jnp.float32)

    for s in range(SLOTS):
        kind = kind_ref(b * SLOTS + s)
        row = pl.multiple_of(dst_ref(b * SLOTS + s) * BLK, BLK)
        kt = kterm[:, s * BLK:(s + 1) * BLK]
        vt = vterm[:, s * BLK:(s + 1) * BLK]
        rounded = kind == 0
        kt = jnp.where(rounded, kt.astype(jnp.bfloat16).astype(jnp.float32), kt)
        vt = jnp.where(rounded, vt.astype(jnp.bfloat16).astype(jnp.float32), vt)

        @pl.when(kind == 2)
        def _():
            loc_acc[g, pl.ds(row, BLK), :] += kt
            loc_acc[kv_here + g, pl.ds(row, BLK), :] += vt

        side = side_ref(b * SLOTS + s)

        @pl.when((kind != 2) & (side == 0))
        def _():
            far_acc[g, pl.ds(row, BLK), :] += kt
            far_acc[kv_here + g, pl.ds(row, BLK), :] += vt

        @pl.when((kind != 2) & (side == 1))
        def _():
            fo_acc[g, pl.ds(row, BLK), :] += kt
            fo_acc[kv_here + g, pl.ds(row, BLK), :] += vt

    @pl.when((g == kv_here - 1) & (b == nb - 1))
    def _():
        for j in range(2 * kv_here):
            loc_ref[:, j * HD:(j + 1) * HD] = loc_acc[j]
            far_ref[:, j * HD:(j + 1) * HD] = far_acc[j].astype(jnp.bfloat16)
            fo_ref[:, j * HD:(j + 1) * HD] = fo_acc[j].astype(jnp.bfloat16)


def shards(query_rows, key_rows, value_rows, out_grad, block_list):
    shard_index = lax.axis_index("ctx")
    lane_index = lax.axis_index("uly")
    nb = key_rows.shape[0] // BLK
    seq = block_list.shape[0] * BLK
    heads_here = query_rows.shape[1] // HD
    kv_here = max(1, heads_here // GROUP)
    hpk = heads_here // kv_here
    width = 2 * kv_here * HD
    first_kv = lane_index * heads_here // GROUP
    shard_count = lax.axis_size("ctx")
    partner = [(i, i ^ 1) for i in range(shard_count)]
    core = shard_index % 2
    members = shard_count // 2
    member = shard_index // 2
    half = seq // 2
    span = nb * BLK

    rows = lax.dynamic_slice_in_dim(block_list, shard_index * nb, nb, axis=0).astype(jnp.int32)
    owner = rows // nb
    cols = jnp.arange(SLOTS)[None, :]
    is_global = (cols == 3) | (cols == 4)
    local = owner == shard_index
    remote = jnp.logical_not(local) & jnp.logical_not(is_global)
    kind = jnp.where(local, 2, jnp.where(remote, 0, 1)).astype(jnp.int32).reshape(-1)
    owner_side = (owner % 2 != core).astype(jnp.int32)
    half_row = ((member - owner // 2) % members) * nb + rows % nb
    dst = jnp.where(local, rows - shard_index * nb, half_row).astype(jnp.int32).reshape(-1)
    blk = half_row.astype(jnp.int32).reshape(-1)
    side = owner_side.reshape(-1)
    table = jnp.concatenate([blk, side, dst, kind]).astype(jnp.int32)

    kernel = functools.partial(attention_kernel, hpk=hpk, kv_here=1, nb=nb)
    dq = jnp.zeros((nb * BLK, heads_here * HD), jnp.bfloat16)
    sums = []
    for g in range(kv_here):
        col = (first_kv + g) * HD
        kv_own = jnp.concatenate(
            [
                lax.dynamic_slice_in_dim(key_rows, col, HD, axis=1),
                lax.dynamic_slice_in_dim(value_rows, col, HD, axis=1),
            ],
            axis=1,
        )
        gathered = [kv_own]
        for d in range(1, members):
            pairs = [(i, (i + 2 * d) % shard_count) for i in range(shard_count)]
            gathered.append(lax.ppermute(kv_own, "ctx", pairs))
        kv_half = jnp.concatenate(gathered, axis=0)
        kv_other = lax.ppermute(kv_half, "ctx", partner)
        grid_spec = pltpu.PrefetchScalarGridSpec(
            num_scalar_prefetch=1,
            grid=(1, nb),
            in_specs=[
                pl.BlockSpec((BLK, hpk * HD), lambda z, b, *_, g=g: (b, g)),
                pl.BlockSpec((BLK, hpk * HD), lambda z, b, *_, g=g: (b, g)),
                pl.BlockSpec((half, HD), lambda z, b, *_: (0, 0)),
                pl.BlockSpec((half, HD), lambda z, b, *_: (0, 1)),
                pl.BlockSpec((half, HD), lambda z, b, *_: (0, 0)),
                pl.BlockSpec((half, HD), lambda z, b, *_: (0, 1)),
                pl.BlockSpec(memory_space=pl.ANY),
            ],
            out_specs=[
                pl.BlockSpec((BLK, hpk * HD), lambda z, b, *_, g=g: (b, g)),
                pl.BlockSpec((span, 2 * HD), lambda z, b, *_: (0, 0)),
                pl.BlockSpec((half, 2 * HD), lambda z, b, *_: (0, 0)),
                pl.BlockSpec((half, 2 * HD), lambda z, b, *_: (0, 0)),
            ],
            scratch_shapes=[
                pltpu.VMEM((SLOTS * BLK, HD), jnp.bfloat16),
                pltpu.VMEM((SLOTS * BLK, HD), jnp.bfloat16),
                pltpu.VMEM((2, span, HD), jnp.float32),
                pltpu.VMEM((2, half, HD), jnp.float32),
                pltpu.VMEM((2, half, HD), jnp.float32),
            ],
        )
        dq, loc, far, far_other = pl.pallas_call(
            kernel,
            grid_spec=grid_spec,
            out_shape=[
                jax.ShapeDtypeStruct((nb * BLK, heads_here * HD), jnp.bfloat16),
                jax.ShapeDtypeStruct((span, 2 * HD), jnp.float32),
                jax.ShapeDtypeStruct((half, 2 * HD), jnp.bfloat16),
                jax.ShapeDtypeStruct((half, 2 * HD), jnp.bfloat16),
            ],
            input_output_aliases={7: 0},
            cost_estimate=pl.CostEstimate(
                flops=12 * nb * hpk * BLK * SLOTS * BLK * HD,
                transcendentals=nb * hpk * BLK * SLOTS * BLK,
                bytes_accessed=4 * nb * BLK * hpk * HD + 4 * half * HD * 2 + 12 * half * HD,
            ),
            compiler_params=pltpu.CompilerParams(dimension_semantics=("arbitrary", "arbitrary")),
        )(table, query_rows, out_grad, kv_half, kv_half, kv_other, kv_other, dq)
        from_partner = lax.ppermute(far_other, "ctx", partner)
        mine = (far.astype(jnp.float32) + from_partner.astype(jnp.float32)).astype(jnp.bfloat16)
        total = far[0:span].astype(jnp.float32) + from_partner[0:span].astype(jnp.float32)
        for d in range(1, members):
            pairs = [(i, (i - 2 * d) % shard_count) for i in range(shard_count)]
            total = total + lax.ppermute(
                mine[d * span:(d + 1) * span], "ctx", pairs
            ).astype(jnp.float32)
        sums.append((total + loc).reshape(nb, HD, 2, BLK))
    stacked = jnp.stack([s[:, :, 0] for s in sums] + [s[:, :, 1] for s in sums], axis=2)
    kv_grad = jnp.transpose(stacked, (0, 3, 2, 1)).reshape(span, 2 * kv_here * HD).astype(jnp.bfloat16)
    width = 2 * kv_here * HD

    query_out = lax.all_to_all(dq, "uly", split_axis=0, concat_axis=1, tiled=True)
    query_out, kv_grad = lax.optimization_barrier((query_out, kv_grad))
    kv_seq = lax.all_to_all(kv_grad, "uly", split_axis=0, concat_axis=1, tiled=True)
    rows_here = kv_seq.shape[0]
    lane_count = kv_seq.shape[1] // width
    spread = kv_seq.reshape(rows_here, lane_count, 2, kv_here * HD)

    def gather_heads(part):
        if heads_here >= GROUP:
            return part.reshape(rows_here, KVH * HD)
        lanes_per = GROUP // heads_here
        merged = part.astype(jnp.float32).reshape(rows_here, KVH, lanes_per, HD).sum(axis=2)
        return merged.reshape(rows_here, KVH * HD).astype(jnp.bfloat16)

    return (query_out, gather_heads(spread[:, :, 0]), gather_heads(spread[:, :, 1]))


def solution(mesh):
    return jax.shard_map(
        shards,
        mesh=mesh,
        in_specs=(P("ctx", "uly"), P("ctx", None), P("ctx", None), P("ctx", "uly"), P()),
        out_specs=(P(("ctx", "uly"), None), P(("ctx", "uly"), None), P(("ctx", "uly"), None)),
        check_vma=False,
    )
```

```python
import functools
import math

import jax
import jax.numpy as jnp
from jax import lax
from jax.experimental import pallas as pl
from jax.experimental.pallas import tpu as pltpu
from jax.sharding import PartitionSpec as P

HD = 128
KVH = 8
BLK = 128
GROUP = 6
SLOTS = 8


def attention_kernel(
    tbl_ref,
    q_ref, do_ref, k_ref, v_ref, ko_ref, vo_ref, dq_in,
    dq_ref, loc_ref, far_ref, fo_ref,
    kc_ref, vc_ref, loc_acc, far_acc, fo_acc,
    *, hpk, kv_here, nb,
):
    g = pl.program_id(0)
    b = pl.program_id(1)
    scale = 1.0 / math.sqrt(HD)
    count = nb * SLOTS

    def blk_ref(i):
        return tbl_ref[i]

    def side_ref(i):
        return tbl_ref[count + i]

    def dst_ref(i):
        return tbl_ref[2 * count + i]

    def kind_ref(i):
        return tbl_ref[3 * count + i]

    @pl.when((g == 0) & (b == 0))
    def _():
        loc_acc[...] = jnp.zeros_like(loc_acc)
        far_acc[...] = jnp.zeros_like(far_acc)
        fo_acc[...] = jnp.zeros_like(fo_acc)

    for s in range(SLOTS):
        row = pl.multiple_of(blk_ref(b * SLOTS + s) * BLK, BLK)
        side = side_ref(b * SLOTS + s)
        for code, tk, tv in ((0, k_ref, v_ref), (1, ko_ref, vo_ref)):
            @pl.when(side == code)
            def _():
                kc_ref[s * BLK:(s + 1) * BLK, :] = tk[pl.ds(row, BLK), :]
                vc_ref[s * BLK:(s + 1) * BLK, :] = tv[pl.ds(row, BLK), :]

    kc = kc_ref[...]
    vc = vc_ref[...]
    qs = jnp.concatenate([q_ref[:, h * HD:(h + 1) * HD] for h in range(hpk)], axis=0)
    dos = jnp.concatenate([do_ref[:, h * HD:(h + 1) * HD] for h in range(hpk)], axis=0)
    nt = (((1,), (1,)), ((), ()))
    tn = (((0,), (0,)), ((), ()))
    scores = lax.dot_general(qs, kc, nt, preferred_element_type=jnp.float32) * scale
    peak = jnp.max(scores, axis=1, keepdims=True)
    lifted = jnp.exp(scores - peak)
    probs = lifted * (1.0 / jnp.sum(lifted, axis=1, keepdims=True))
    probs_b = probs.astype(jnp.bfloat16)
    attended = jnp.dot(probs_b, vc, preferred_element_type=jnp.float32)
    delta = jnp.sum(dos.astype(jnp.float32) * attended, axis=1, keepdims=True)
    dprobs = lax.dot_general(dos, vc, nt, preferred_element_type=jnp.float32)
    dscores = (probs * (dprobs - delta) * scale).astype(jnp.bfloat16)
    dq = jnp.dot(dscores, kc, preferred_element_type=jnp.float32)
    for h in range(hpk):
        dq_ref[:, h * HD:(h + 1) * HD] = dq[h * BLK:(h + 1) * BLK].astype(jnp.bfloat16)
    kterm = lax.dot_general(qs, dscores, tn, preferred_element_type=jnp.float32)
    vterm = lax.dot_general(dos, probs_b, tn, preferred_element_type=jnp.float32)

    for s in range(SLOTS):
        kind = kind_ref(b * SLOTS + s)
        row = pl.multiple_of(dst_ref(b * SLOTS + s) * BLK, BLK)
        kt = kterm[:, s * BLK:(s + 1) * BLK]
        vt = vterm[:, s * BLK:(s + 1) * BLK]
        rounded = kind == 0
        kt = jnp.where(rounded, kt.astype(jnp.bfloat16).astype(jnp.float32), kt)
        vt = jnp.where(rounded, vt.astype(jnp.bfloat16).astype(jnp.float32), vt)

        @pl.when(kind == 2)
        def _():
            loc_acc[g, pl.ds(row, BLK), :] += kt
            loc_acc[kv_here + g, pl.ds(row, BLK), :] += vt

        side = side_ref(b * SLOTS + s)

        @pl.when((kind != 2) & (side == 0))
        def _():
            far_acc[g, pl.ds(row, BLK), :] += kt
            far_acc[kv_here + g, pl.ds(row, BLK), :] += vt

        @pl.when((kind != 2) & (side == 1))
        def _():
            fo_acc[g, pl.ds(row, BLK), :] += kt
            fo_acc[kv_here + g, pl.ds(row, BLK), :] += vt

    @pl.when((g == kv_here - 1) & (b == nb - 1))
    def _():
        for j in range(2 * kv_here):
            loc_ref[:, j * HD:(j + 1) * HD] = loc_acc[j]
            far_ref[:, j * HD:(j + 1) * HD] = far_acc[j].astype(jnp.bfloat16)
            fo_ref[:, j * HD:(j + 1) * HD] = fo_acc[j].astype(jnp.bfloat16)


def shards(query_rows, key_rows, value_rows, out_grad, block_list):
    shard_index = lax.axis_index("ctx")
    lane_index = lax.axis_index("uly")
    nb = key_rows.shape[0] // BLK
    seq = block_list.shape[0] * BLK
    heads_here = query_rows.shape[1] // HD
    kv_here = max(1, heads_here // GROUP)
    hpk = heads_here // kv_here
    width = 2 * kv_here * HD
    first_kv = lane_index * heads_here // GROUP
    shard_count = lax.axis_size("ctx")
    partner = [(i, i ^ 1) for i in range(shard_count)]
    core = shard_index % 2
    members = shard_count // 2
    member = shard_index // 2
    half = seq // 2
    span = nb * BLK

    rows = lax.dynamic_slice_in_dim(block_list, shard_index * nb, nb, axis=0).astype(jnp.int32)
    owner = rows // nb
    cols = jnp.arange(SLOTS)[None, :]
    is_global = (cols == 3) | (cols == 4)
    local = owner == shard_index
    remote = jnp.logical_not(local) & jnp.logical_not(is_global)
    kind = jnp.where(local, 2, jnp.where(remote, 0, 1)).astype(jnp.int32).reshape(-1)
    owner_side = (owner % 2 != core).astype(jnp.int32)
    half_row = ((member - owner // 2) % members) * nb + rows % nb
    dst = jnp.where(local, rows - shard_index * nb, half_row).astype(jnp.int32).reshape(-1)
    blk = half_row.astype(jnp.int32).reshape(-1)
    side = owner_side.reshape(-1)
    table = jnp.concatenate([blk, side, dst, kind]).astype(jnp.int32)

    kernel = functools.partial(attention_kernel, hpk=hpk, kv_here=1, nb=nb)
    dq = jnp.zeros((nb * BLK, heads_here * HD), jnp.bfloat16)
    sums = []
    for g in range(kv_here):
        col = (first_kv + g) * HD
        kv_own = jnp.concatenate(
            [
                lax.dynamic_slice_in_dim(key_rows, col, HD, axis=1),
                lax.dynamic_slice_in_dim(value_rows, col, HD, axis=1),
            ],
            axis=1,
        )
        gathered = [kv_own]
        for d in range(1, members):
            pairs = [(i, (i + 2 * d) % shard_count) for i in range(shard_count)]
            gathered.append(lax.ppermute(kv_own, "ctx", pairs))
        kv_half = jnp.concatenate(gathered, axis=0)
        kv_other = lax.ppermute(kv_half, "ctx", partner)
        if g > 0:
            kv_half, kv_other, dq = lax.optimization_barrier((kv_half, kv_other, dq))
        grid_spec = pltpu.PrefetchScalarGridSpec(
            num_scalar_prefetch=1,
            grid=(1, nb),
            in_specs=[
                pl.BlockSpec((BLK, hpk * HD), lambda z, b, *_, g=g: (b, g)),
                pl.BlockSpec((BLK, hpk * HD), lambda z, b, *_, g=g: (b, g)),
                pl.BlockSpec((half, HD), lambda z, b, *_: (0, 0)),
                pl.BlockSpec((half, HD), lambda z, b, *_: (0, 1)),
                pl.BlockSpec((half, HD), lambda z, b, *_: (0, 0)),
                pl.BlockSpec((half, HD), lambda z, b, *_: (0, 1)),
                pl.BlockSpec(memory_space=pl.ANY),
            ],
            out_specs=[
                pl.BlockSpec((BLK, hpk * HD), lambda z, b, *_, g=g: (b, g)),
                pl.BlockSpec((span, 2 * HD), lambda z, b, *_: (0, 0)),
                pl.BlockSpec((half, 2 * HD), lambda z, b, *_: (0, 0)),
                pl.BlockSpec((half, 2 * HD), lambda z, b, *_: (0, 0)),
            ],
            scratch_shapes=[
                pltpu.VMEM((SLOTS * BLK, HD), jnp.bfloat16),
                pltpu.VMEM((SLOTS * BLK, HD), jnp.bfloat16),
                pltpu.VMEM((2, span, HD), jnp.float32),
                pltpu.VMEM((2, half, HD), jnp.float32),
                pltpu.VMEM((2, half, HD), jnp.float32),
            ],
        )
        dq, loc, far, far_other = pl.pallas_call(
            kernel,
            grid_spec=grid_spec,
            out_shape=[
                jax.ShapeDtypeStruct((nb * BLK, heads_here * HD), jnp.bfloat16),
                jax.ShapeDtypeStruct((span, 2 * HD), jnp.float32),
                jax.ShapeDtypeStruct((half, 2 * HD), jnp.bfloat16),
                jax.ShapeDtypeStruct((half, 2 * HD), jnp.bfloat16),
            ],
            input_output_aliases={7: 0},
            cost_estimate=pl.CostEstimate(
                flops=12 * nb * hpk * BLK * SLOTS * BLK * HD,
                transcendentals=nb * hpk * BLK * SLOTS * BLK,
                bytes_accessed=4 * nb * BLK * hpk * HD + 4 * half * HD * 2 + 12 * half * HD,
            ),
            compiler_params=pltpu.CompilerParams(dimension_semantics=("arbitrary", "arbitrary")),
        )(table, query_rows, out_grad, kv_half, kv_half, kv_other, kv_other, dq)
        from_partner = lax.ppermute(far_other, "ctx", partner)
        mine = (far.astype(jnp.float32) + from_partner.astype(jnp.float32)).astype(jnp.bfloat16)
        total = far[0:span].astype(jnp.float32) + from_partner[0:span].astype(jnp.float32)
        for d in range(1, members):
            pairs = [(i, (i - 2 * d) % shard_count) for i in range(shard_count)]
            total = total + lax.ppermute(
                mine[d * span:(d + 1) * span], "ctx", pairs
            ).astype(jnp.float32)
        sums.append((total + loc).reshape(nb, HD, 2, BLK))
    stacked = jnp.stack([s[:, :, 0] for s in sums] + [s[:, :, 1] for s in sums], axis=2)
    kv_grad = jnp.transpose(stacked, (0, 3, 2, 1)).reshape(span, 2 * kv_here * HD).astype(jnp.bfloat16)
    width = 2 * kv_here * HD

    query_out = lax.all_to_all(dq, "uly", split_axis=0, concat_axis=1, tiled=True)
    query_out, kv_grad = lax.optimization_barrier((query_out, kv_grad))
    kv_seq = lax.all_to_all(kv_grad, "uly", split_axis=0, concat_axis=1, tiled=True)
    rows_here = kv_seq.shape[0]
    lane_count = kv_seq.shape[1] // width
    spread = kv_seq.reshape(rows_here, lane_count, 2, kv_here * HD)

    def gather_heads(part):
        if heads_here >= GROUP:
            return part.reshape(rows_here, KVH * HD)
        lanes_per = GROUP // heads_here
        merged = part.astype(jnp.float32).reshape(rows_here, KVH, lanes_per, HD).sum(axis=2)
        return merged.reshape(rows_here, KVH * HD).astype(jnp.bfloat16)

    return (query_out, gather_heads(spread[:, :, 0]), gather_heads(spread[:, :, 1]))


def solution(mesh):
    return jax.shard_map(
        shards,
        mesh=mesh,
        in_specs=(P("ctx", "uly"), P("ctx", None), P("ctx", None), P("ctx", "uly"), P()),
        out_specs=(P(("ctx", "uly"), None), P(("ctx", "uly"), None), P(("ctx", "uly"), None)),
        check_vma=False,
    )
```

```python
import functools
import math

import jax
import jax.numpy as jnp
from jax import lax
from jax.experimental import pallas as pl
from jax.experimental.pallas import tpu as pltpu
from jax.sharding import PartitionSpec as P

HD = 128
KVH = 8
BLK = 128
GROUP = 6
SLOTS = 8


def attention_kernel(
    tbl_ref,
    q_ref, do_ref, k_ref, v_ref, ko_ref, vo_ref, dq_in,
    dq_ref, loc_ref, far_ref, fo_ref,
    kc_ref, vc_ref, loc_acc, far_acc, fo_acc, s_ref, p_ref, pb_ref, ds_ref, dl_ref,
    *, hpk, kv_here, nb,
):
    g = pl.program_id(0)
    b = pl.program_id(1)
    scale = 1.0 / math.sqrt(HD)
    count = nb * SLOTS

    def blk_ref(i):
        return tbl_ref[i]

    def side_ref(i):
        return tbl_ref[count + i]

    def dst_ref(i):
        return tbl_ref[2 * count + i]

    def kind_ref(i):
        return tbl_ref[3 * count + i]

    @pl.when((g == 0) & (b == 0))
    def _():
        loc_acc[...] = jnp.zeros_like(loc_acc)
        far_acc[...] = jnp.zeros_like(far_acc)
        fo_acc[...] = jnp.zeros_like(fo_acc)

    for s in range(SLOTS):
        row = pl.multiple_of(blk_ref(b * SLOTS + s) * BLK, BLK)
        side = side_ref(b * SLOTS + s)
        for code, tk, tv in ((0, k_ref, v_ref), (1, ko_ref, vo_ref)):
            @pl.when(side == code)
            def _():
                kc_ref[s * BLK:(s + 1) * BLK, :] = tk[pl.ds(row, BLK), :]
                vc_ref[s * BLK:(s + 1) * BLK, :] = tv[pl.ds(row, BLK), :]

    kc = kc_ref[...]
    vc = vc_ref[...]
    qs = jnp.concatenate([q_ref[:, h * HD:(h + 1) * HD] for h in range(hpk)], axis=0)
    dos = jnp.concatenate([do_ref[:, h * HD:(h + 1) * HD] for h in range(hpk)], axis=0)
    nt = (((1,), (1,)), ((), ()))
    tn = (((0,), (0,)), ((), ()))
    rows = hpk * BLK
    chunk = 16
    s_ref[...] = lax.dot_general(qs, kc, nt, preferred_element_type=jnp.float32)

    def softmax_rows(i, carry):
        r0 = pl.multiple_of(i * chunk, chunk)
        scores = s_ref[pl.ds(r0, chunk), :] * scale
        peak = jnp.max(scores, axis=1, keepdims=True)
        lifted = jnp.exp(scores - peak)
        probs = lifted * (1.0 / jnp.sum(lifted, axis=1, keepdims=True))
        p_ref[pl.ds(r0, chunk), :] = probs
        pb_ref[pl.ds(r0, chunk), :] = probs.astype(jnp.bfloat16)
        return carry

    lax.fori_loop(0, rows // chunk, softmax_rows, 0, unroll=2)
    probs_b = pb_ref[...]
    attended = jnp.dot(probs_b, vc, preferred_element_type=jnp.float32)
    dl_ref[...] = jnp.sum(dos.astype(jnp.float32) * attended, axis=1, keepdims=True)
    s_ref[...] = lax.dot_general(dos, vc, nt, preferred_element_type=jnp.float32)

    def score_grad_rows(i, carry):
        r0 = pl.multiple_of(i * chunk, chunk)
        probs = p_ref[pl.ds(r0, chunk), :]
        dprobs = s_ref[pl.ds(r0, chunk), :]
        delta = dl_ref[pl.ds(r0, chunk), :]
        ds_ref[pl.ds(r0, chunk), :] = (probs * (dprobs - delta) * scale).astype(jnp.bfloat16)
        return carry

    lax.fori_loop(0, rows // chunk, score_grad_rows, 0, unroll=2)
    dscores = ds_ref[...]
    dq = jnp.dot(dscores, kc, preferred_element_type=jnp.float32)
    for h in range(hpk):
        dq_ref[:, h * HD:(h + 1) * HD] = dq[h * BLK:(h + 1) * BLK].astype(jnp.bfloat16)
    kterm = lax.dot_general(qs, dscores, tn, preferred_element_type=jnp.float32)
    vterm = lax.dot_general(dos, probs_b, tn, preferred_element_type=jnp.float32)

    for s in range(SLOTS):
        kind = kind_ref(b * SLOTS + s)
        row = pl.multiple_of(dst_ref(b * SLOTS + s) * BLK, BLK)
        kt = kterm[:, s * BLK:(s + 1) * BLK]
        vt = vterm[:, s * BLK:(s + 1) * BLK]
        rounded = kind == 0
        kt = jnp.where(rounded, kt.astype(jnp.bfloat16).astype(jnp.float32), kt)
        vt = jnp.where(rounded, vt.astype(jnp.bfloat16).astype(jnp.float32), vt)

        @pl.when(kind == 2)
        def _():
            loc_acc[g, pl.ds(row, BLK), :] += kt
            loc_acc[kv_here + g, pl.ds(row, BLK), :] += vt

        side = side_ref(b * SLOTS + s)

        @pl.when((kind != 2) & (side == 0))
        def _():
            far_acc[g, pl.ds(row, BLK), :] += kt
            far_acc[kv_here + g, pl.ds(row, BLK), :] += vt

        @pl.when((kind != 2) & (side == 1))
        def _():
            fo_acc[g, pl.ds(row, BLK), :] += kt
            fo_acc[kv_here + g, pl.ds(row, BLK), :] += vt

    @pl.when((g == kv_here - 1) & (b == nb - 1))
    def _():
        for j in range(2 * kv_here):
            loc_ref[:, j * HD:(j + 1) * HD] = loc_acc[j]
            far_ref[:, j * HD:(j + 1) * HD] = far_acc[j].astype(jnp.bfloat16)
            fo_ref[:, j * HD:(j + 1) * HD] = fo_acc[j].astype(jnp.bfloat16)


def shards(query_rows, key_rows, value_rows, out_grad, block_list):
    shard_index = lax.axis_index("ctx")
    lane_index = lax.axis_index("uly")
    nb = key_rows.shape[0] // BLK
    seq = block_list.shape[0] * BLK
    heads_here = query_rows.shape[1] // HD
    kv_here = max(1, heads_here // GROUP)
    hpk = heads_here // kv_here
    width = 2 * kv_here * HD
    first_kv = lane_index * heads_here // GROUP
    shard_count = lax.axis_size("ctx")
    partner = [(i, i ^ 1) for i in range(shard_count)]
    core = shard_index % 2
    members = shard_count // 2
    member = shard_index // 2
    half = seq // 2
    span = nb * BLK

    rows = lax.dynamic_slice_in_dim(block_list, shard_index * nb, nb, axis=0).astype(jnp.int32)
    owner = rows // nb
    cols = jnp.arange(SLOTS)[None, :]
    is_global = (cols == 3) | (cols == 4)
    local = owner == shard_index
    remote = jnp.logical_not(local) & jnp.logical_not(is_global)
    kind = jnp.where(local, 2, jnp.where(remote, 0, 1)).astype(jnp.int32).reshape(-1)
    owner_side = (owner % 2 != core).astype(jnp.int32)
    half_row = ((member - owner // 2) % members) * nb + rows % nb
    dst = jnp.where(local, rows - shard_index * nb, half_row).astype(jnp.int32).reshape(-1)
    blk = half_row.astype(jnp.int32).reshape(-1)
    side = owner_side.reshape(-1)
    table = jnp.concatenate([blk, side, dst, kind]).astype(jnp.int32)

    kernel = functools.partial(attention_kernel, hpk=hpk, kv_here=1, nb=nb)
    dq = jnp.zeros((nb * BLK, heads_here * HD), jnp.bfloat16)
    sums = []
    for g in range(kv_here):
        col = (first_kv + g) * HD
        kv_own = jnp.concatenate(
            [
                lax.dynamic_slice_in_dim(key_rows, col, HD, axis=1),
                lax.dynamic_slice_in_dim(value_rows, col, HD, axis=1),
            ],
            axis=1,
        )
        gathered = [kv_own]
        for d in range(1, members):
            pairs = [(i, (i + 2 * d) % shard_count) for i in range(shard_count)]
            gathered.append(lax.ppermute(kv_own, "ctx", pairs))
        kv_half = jnp.concatenate(gathered, axis=0)
        kv_other = lax.ppermute(kv_half, "ctx", partner)
        if g > 0:
            kv_half, kv_other, dq = lax.optimization_barrier((kv_half, kv_other, dq))
        grid_spec = pltpu.PrefetchScalarGridSpec(
            num_scalar_prefetch=1,
            grid=(1, nb),
            in_specs=[
                pl.BlockSpec((BLK, hpk * HD), lambda z, b, *_, g=g: (b, g)),
                pl.BlockSpec((BLK, hpk * HD), lambda z, b, *_, g=g: (b, g)),
                pl.BlockSpec((half, HD), lambda z, b, *_: (0, 0)),
                pl.BlockSpec((half, HD), lambda z, b, *_: (0, 1)),
                pl.BlockSpec((half, HD), lambda z, b, *_: (0, 0)),
                pl.BlockSpec((half, HD), lambda z, b, *_: (0, 1)),
                pl.BlockSpec(memory_space=pl.ANY),
            ],
            out_specs=[
                pl.BlockSpec((BLK, hpk * HD), lambda z, b, *_, g=g: (b, g)),
                pl.BlockSpec((span, 2 * HD), lambda z, b, *_: (0, 0)),
                pl.BlockSpec((half, 2 * HD), lambda z, b, *_: (0, 0)),
                pl.BlockSpec((half, 2 * HD), lambda z, b, *_: (0, 0)),
            ],
            scratch_shapes=[
                pltpu.VMEM((SLOTS * BLK, HD), jnp.bfloat16),
                pltpu.VMEM((SLOTS * BLK, HD), jnp.bfloat16),
                pltpu.VMEM((2, span, HD), jnp.float32),
                pltpu.VMEM((2, half, HD), jnp.float32),
                pltpu.VMEM((2, half, HD), jnp.float32),
                pltpu.VMEM((hpk * BLK, SLOTS * BLK), jnp.float32),
                pltpu.VMEM((hpk * BLK, SLOTS * BLK), jnp.float32),
                pltpu.VMEM((hpk * BLK, SLOTS * BLK), jnp.bfloat16),
                pltpu.VMEM((hpk * BLK, SLOTS * BLK), jnp.bfloat16),
                pltpu.VMEM((hpk * BLK, 1), jnp.float32),
            ],
        )
        dq, loc, far, far_other = pl.pallas_call(
            kernel,
            grid_spec=grid_spec,
            out_shape=[
                jax.ShapeDtypeStruct((nb * BLK, heads_here * HD), jnp.bfloat16),
                jax.ShapeDtypeStruct((span, 2 * HD), jnp.float32),
                jax.ShapeDtypeStruct((half, 2 * HD), jnp.bfloat16),
                jax.ShapeDtypeStruct((half, 2 * HD), jnp.bfloat16),
            ],
            input_output_aliases={7: 0},
            cost_estimate=pl.CostEstimate(
                flops=12 * nb * hpk * BLK * SLOTS * BLK * HD,
                transcendentals=nb * hpk * BLK * SLOTS * BLK,
                bytes_accessed=4 * nb * BLK * hpk * HD + 4 * half * HD * 2 + 12 * half * HD,
            ),
            compiler_params=pltpu.CompilerParams(dimension_semantics=("arbitrary", "arbitrary")),
        )(table, query_rows, out_grad, kv_half, kv_half, kv_other, kv_other, dq)
        from_partner = lax.ppermute(far_other, "ctx", partner)
        mine = (far.astype(jnp.float32) + from_partner.astype(jnp.float32)).astype(jnp.bfloat16)
        total = far[0:span].astype(jnp.float32) + from_partner[0:span].astype(jnp.float32)
        for d in range(1, members):
            pairs = [(i, (i - 2 * d) % shard_count) for i in range(shard_count)]
            total = total + lax.ppermute(
                mine[d * span:(d + 1) * span], "ctx", pairs
            ).astype(jnp.float32)
        sums.append((total + loc).reshape(nb, HD, 2, BLK))
    stacked = jnp.stack([s[:, :, 0] for s in sums] + [s[:, :, 1] for s in sums], axis=2)
    kv_grad = jnp.transpose(stacked, (0, 3, 2, 1)).reshape(span, 2 * kv_here * HD).astype(jnp.bfloat16)
    width = 2 * kv_here * HD

    query_out = lax.all_to_all(dq, "uly", split_axis=0, concat_axis=1, tiled=True)
    query_out, kv_grad = lax.optimization_barrier((query_out, kv_grad))
    kv_seq = lax.all_to_all(kv_grad, "uly", split_axis=0, concat_axis=1, tiled=True)
    rows_here = kv_seq.shape[0]
    lane_count = kv_seq.shape[1] // width
    spread = kv_seq.reshape(rows_here, lane_count, 2, kv_here * HD)

    def gather_heads(part):
        if heads_here >= GROUP:
            return part.reshape(rows_here, KVH * HD)
        lanes_per = GROUP // heads_here
        merged = part.astype(jnp.float32).reshape(rows_here, KVH, lanes_per, HD).sum(axis=2)
        return merged.reshape(rows_here, KVH * HD).astype(jnp.bfloat16)

    return (query_out, gather_heads(spread[:, :, 0]), gather_heads(spread[:, :, 1]))


def solution(mesh):
    return jax.shard_map(
        shards,
        mesh=mesh,
        in_specs=(P("ctx", "uly"), P("ctx", None), P("ctx", None), P("ctx", "uly"), P()),
        out_specs=(P(("ctx", "uly"), None), P(("ctx", "uly"), None), P(("ctx", "uly"), None)),
        check_vma=False,
    )
```

```python
import functools
import math

import jax
import jax.numpy as jnp
from jax import lax
from jax.experimental import pallas as pl
from jax.experimental.pallas import tpu as pltpu
from jax.sharding import PartitionSpec as P

HD = 128
KVH = 8
BLK = 128
GROUP = 6
SLOTS = 8


def attention_kernel(
    tbl_ref,
    q_ref, do_ref, k_ref, v_ref, ko_ref, vo_ref, dq_in,
    dq_ref, loc_ref, far_ref, fo_ref,
    kc_ref, vc_ref, loc_acc, far_acc, fo_acc, s_ref, p_ref, pb_ref, ds_ref, dl_ref,
    *, hpk, kv_here, nb,
):
    g = pl.program_id(0)
    b = pl.program_id(1)
    scale = 1.0 / math.sqrt(HD)
    count = nb * SLOTS

    def blk_ref(i):
        return tbl_ref[i]

    def side_ref(i):
        return tbl_ref[count + i]

    def dst_ref(i):
        return tbl_ref[2 * count + i]

    def kind_ref(i):
        return tbl_ref[3 * count + i]

    @pl.when((g == 0) & (b == 0))
    def _():
        loc_acc[...] = jnp.zeros_like(loc_acc)
        far_acc[...] = jnp.zeros_like(far_acc)
        fo_acc[...] = jnp.zeros_like(fo_acc)

    for s in range(SLOTS):
        row = pl.multiple_of(blk_ref(b * SLOTS + s) * BLK, BLK)
        side = side_ref(b * SLOTS + s)
        for code, tk, tv in ((0, k_ref, v_ref), (1, ko_ref, vo_ref)):
            @pl.when(side == code)
            def _():
                kc_ref[s * BLK:(s + 1) * BLK, :] = tk[pl.ds(row, BLK), :]
                vc_ref[s * BLK:(s + 1) * BLK, :] = tv[pl.ds(row, BLK), :]

    kc = kc_ref[...]
    vc = vc_ref[...]
    qs = jnp.concatenate([q_ref[:, h * HD:(h + 1) * HD] for h in range(hpk)], axis=0)
    dos = jnp.concatenate([do_ref[:, h * HD:(h + 1) * HD] for h in range(hpk)], axis=0)
    nt = (((1,), (1,)), ((), ()))
    tn = (((0,), (0,)), ((), ()))
    rows = hpk * BLK
    chunk = BLK
    s_ref[...] = lax.dot_general(qs, kc, nt, preferred_element_type=jnp.float32)

    def softmax_rows(i, carry):
        r0 = pl.multiple_of(i * chunk, chunk)
        scores = s_ref[pl.ds(r0, chunk), :] * scale
        peak = jnp.max(scores, axis=1, keepdims=True)
        lifted = jnp.exp(scores - peak)
        probs = lifted * (1.0 / jnp.sum(lifted, axis=1, keepdims=True))
        p_ref[pl.ds(r0, chunk), :] = probs
        pb_ref[pl.ds(r0, chunk), :] = probs.astype(jnp.bfloat16)
        return carry

    lax.fori_loop(0, rows // chunk, softmax_rows, 0, unroll=True)
    probs_b = pb_ref[...]
    attended = jnp.dot(probs_b, vc, preferred_element_type=jnp.float32)
    dl_ref[...] = jnp.sum(dos.astype(jnp.float32) * attended, axis=1, keepdims=True)
    s_ref[...] = lax.dot_general(dos, vc, nt, preferred_element_type=jnp.float32)

    def score_grad_rows(i, carry):
        r0 = pl.multiple_of(i * chunk, chunk)
        probs = p_ref[pl.ds(r0, chunk), :]
        dprobs = s_ref[pl.ds(r0, chunk), :]
        delta = dl_ref[pl.ds(r0, chunk), :]
        ds_ref[pl.ds(r0, chunk), :] = (probs * (dprobs - delta) * scale).astype(jnp.bfloat16)
        return carry

    lax.fori_loop(0, rows // chunk, score_grad_rows, 0, unroll=True)
    dscores = ds_ref[...]
    dq = jnp.dot(dscores, kc, preferred_element_type=jnp.float32)
    for h in range(hpk):
        dq_ref[:, h * HD:(h + 1) * HD] = dq[h * BLK:(h + 1) * BLK].astype(jnp.bfloat16)
    kterm = lax.dot_general(qs, dscores, tn, preferred_element_type=jnp.float32)
    vterm = lax.dot_general(dos, probs_b, tn, preferred_element_type=jnp.float32)

    for s in range(SLOTS):
        kind = kind_ref(b * SLOTS + s)
        row = pl.multiple_of(dst_ref(b * SLOTS + s) * BLK, BLK)
        kt = kterm[:, s * BLK:(s + 1) * BLK]
        vt = vterm[:, s * BLK:(s + 1) * BLK]
        rounded = kind == 0
        kt = jnp.where(rounded, kt.astype(jnp.bfloat16).astype(jnp.float32), kt)
        vt = jnp.where(rounded, vt.astype(jnp.bfloat16).astype(jnp.float32), vt)

        @pl.when(kind == 2)
        def _():
            loc_acc[g, pl.ds(row, BLK), :] += kt
            loc_acc[kv_here + g, pl.ds(row, BLK), :] += vt

        side = side_ref(b * SLOTS + s)

        @pl.when((kind != 2) & (side == 0))
        def _():
            far_acc[g, pl.ds(row, BLK), :] += kt
            far_acc[kv_here + g, pl.ds(row, BLK), :] += vt

        @pl.when((kind != 2) & (side == 1))
        def _():
            fo_acc[g, pl.ds(row, BLK), :] += kt
            fo_acc[kv_here + g, pl.ds(row, BLK), :] += vt

    @pl.when((g == kv_here - 1) & (b == nb - 1))
    def _():
        for j in range(2 * kv_here):
            loc_ref[:, j * HD:(j + 1) * HD] = loc_acc[j]
            far_ref[:, j * HD:(j + 1) * HD] = far_acc[j].astype(jnp.bfloat16)
            fo_ref[:, j * HD:(j + 1) * HD] = fo_acc[j].astype(jnp.bfloat16)


def shards(query_rows, key_rows, value_rows, out_grad, block_list):
    shard_index = lax.axis_index("ctx")
    lane_index = lax.axis_index("uly")
    nb = key_rows.shape[0] // BLK
    seq = block_list.shape[0] * BLK
    heads_here = query_rows.shape[1] // HD
    kv_here = max(1, heads_here // GROUP)
    hpk = heads_here // kv_here
    width = 2 * kv_here * HD
    first_kv = lane_index * heads_here // GROUP
    shard_count = lax.axis_size("ctx")
    partner = [(i, i ^ 1) for i in range(shard_count)]
    core = shard_index % 2
    members = shard_count // 2
    member = shard_index // 2
    half = seq // 2
    span = nb * BLK

    rows = lax.dynamic_slice_in_dim(block_list, shard_index * nb, nb, axis=0).astype(jnp.int32)
    owner = rows // nb
    cols = jnp.arange(SLOTS)[None, :]
    is_global = (cols == 3) | (cols == 4)
    local = owner == shard_index
    remote = jnp.logical_not(local) & jnp.logical_not(is_global)
    kind = jnp.where(local, 2, jnp.where(remote, 0, 1)).astype(jnp.int32).reshape(-1)
    owner_side = (owner % 2 != core).astype(jnp.int32)
    half_row = ((member - owner // 2) % members) * nb + rows % nb
    dst = jnp.where(local, rows - shard_index * nb, half_row).astype(jnp.int32).reshape(-1)
    blk = half_row.astype(jnp.int32).reshape(-1)
    side = owner_side.reshape(-1)
    table = jnp.concatenate([blk, side, dst, kind]).astype(jnp.int32)

    kernel = functools.partial(attention_kernel, hpk=hpk, kv_here=1, nb=nb)
    dq = jnp.zeros((nb * BLK, heads_here * HD), jnp.bfloat16)
    sums = []
    for g in range(kv_here):
        col = (first_kv + g) * HD
        kv_own = jnp.concatenate(
            [
                lax.dynamic_slice_in_dim(key_rows, col, HD, axis=1),
                lax.dynamic_slice_in_dim(value_rows, col, HD, axis=1),
            ],
            axis=1,
        )
        gathered = [kv_own]
        for d in range(1, members):
            pairs = [(i, (i + 2 * d) % shard_count) for i in range(shard_count)]
            gathered.append(lax.ppermute(kv_own, "ctx", pairs))
        kv_half = jnp.concatenate(gathered, axis=0)
        kv_other = lax.ppermute(kv_half, "ctx", partner)
        if g > 0:
            kv_half, kv_other, dq = lax.optimization_barrier((kv_half, kv_other, dq))
        grid_spec = pltpu.PrefetchScalarGridSpec(
            num_scalar_prefetch=1,
            grid=(1, nb),
            in_specs=[
                pl.BlockSpec((BLK, hpk * HD), lambda z, b, *_, g=g: (b, g)),
                pl.BlockSpec((BLK, hpk * HD), lambda z, b, *_, g=g: (b, g)),
                pl.BlockSpec((half, HD), lambda z, b, *_: (0, 0)),
                pl.BlockSpec((half, HD), lambda z, b, *_: (0, 1)),
                pl.BlockSpec((half, HD), lambda z, b, *_: (0, 0)),
                pl.BlockSpec((half, HD), lambda z, b, *_: (0, 1)),
                pl.BlockSpec(memory_space=pl.ANY),
            ],
            out_specs=[
                pl.BlockSpec((BLK, hpk * HD), lambda z, b, *_, g=g: (b, g)),
                pl.BlockSpec((span, 2 * HD), lambda z, b, *_: (0, 0)),
                pl.BlockSpec((half, 2 * HD), lambda z, b, *_: (0, 0)),
                pl.BlockSpec((half, 2 * HD), lambda z, b, *_: (0, 0)),
            ],
            scratch_shapes=[
                pltpu.VMEM((SLOTS * BLK, HD), jnp.bfloat16),
                pltpu.VMEM((SLOTS * BLK, HD), jnp.bfloat16),
                pltpu.VMEM((2, span, HD), jnp.float32),
                pltpu.VMEM((2, half, HD), jnp.float32),
                pltpu.VMEM((2, half, HD), jnp.float32),
                pltpu.VMEM((hpk * BLK, SLOTS * BLK), jnp.float32),
                pltpu.VMEM((hpk * BLK, SLOTS * BLK), jnp.float32),
                pltpu.VMEM((hpk * BLK, SLOTS * BLK), jnp.bfloat16),
                pltpu.VMEM((hpk * BLK, SLOTS * BLK), jnp.bfloat16),
                pltpu.VMEM((hpk * BLK, 1), jnp.float32),
            ],
        )
        dq, loc, far, far_other = pl.pallas_call(
            kernel,
            grid_spec=grid_spec,
            out_shape=[
                jax.ShapeDtypeStruct((nb * BLK, heads_here * HD), jnp.bfloat16),
                jax.ShapeDtypeStruct((span, 2 * HD), jnp.float32),
                jax.ShapeDtypeStruct((half, 2 * HD), jnp.bfloat16),
                jax.ShapeDtypeStruct((half, 2 * HD), jnp.bfloat16),
            ],
            input_output_aliases={7: 0},
            cost_estimate=pl.CostEstimate(
                flops=12 * nb * hpk * BLK * SLOTS * BLK * HD,
                transcendentals=nb * hpk * BLK * SLOTS * BLK,
                bytes_accessed=4 * nb * BLK * hpk * HD + 4 * half * HD * 2 + 12 * half * HD,
            ),
            compiler_params=pltpu.CompilerParams(dimension_semantics=("arbitrary", "arbitrary")),
        )(table, query_rows, out_grad, kv_half, kv_half, kv_other, kv_other, dq)
        from_partner = lax.ppermute(far_other, "ctx", partner)
        mine = (far.astype(jnp.float32) + from_partner.astype(jnp.float32)).astype(jnp.bfloat16)
        total = far[0:span].astype(jnp.float32) + from_partner[0:span].astype(jnp.float32)
        for d in range(1, members):
            pairs = [(i, (i - 2 * d) % shard_count) for i in range(shard_count)]
            total = total + lax.ppermute(
                mine[d * span:(d + 1) * span], "ctx", pairs
            ).astype(jnp.float32)
        sums.append((total + loc).reshape(nb, HD, 2, BLK))
    stacked = jnp.stack([s[:, :, 0] for s in sums] + [s[:, :, 1] for s in sums], axis=2)
    kv_grad = jnp.transpose(stacked, (0, 3, 2, 1)).reshape(span, 2 * kv_here * HD).astype(jnp.bfloat16)
    width = 2 * kv_here * HD

    query_out = lax.all_to_all(dq, "uly", split_axis=0, concat_axis=1, tiled=True)
    query_out, kv_grad = lax.optimization_barrier((query_out, kv_grad))
    kv_seq = lax.all_to_all(kv_grad, "uly", split_axis=0, concat_axis=1, tiled=True)
    rows_here = kv_seq.shape[0]
    lane_count = kv_seq.shape[1] // width
    spread = kv_seq.reshape(rows_here, lane_count, 2, kv_here * HD)

    def gather_heads(part):
        if heads_here >= GROUP:
            return part.reshape(rows_here, KVH * HD)
        lanes_per = GROUP // heads_here
        merged = part.astype(jnp.float32).reshape(rows_here, KVH, lanes_per, HD).sum(axis=2)
        return merged.reshape(rows_here, KVH * HD).astype(jnp.bfloat16)

    return (query_out, gather_heads(spread[:, :, 0]), gather_heads(spread[:, :, 1]))


def solution(mesh):
    return jax.shard_map(
        shards,
        mesh=mesh,
        in_specs=(P("ctx", "uly"), P("ctx", None), P("ctx", None), P("ctx", "uly"), P()),
        out_specs=(P(("ctx", "uly"), None), P(("ctx", "uly"), None), P(("ctx", "uly"), None)),
        check_vma=False,
    )
```

```python
import functools
import math

import jax
import jax.numpy as jnp
from jax import lax
from jax.experimental import pallas as pl
from jax.experimental.pallas import tpu as pltpu
from jax.sharding import PartitionSpec as P

HD = 128
KVH = 8
BLK = 128
GROUP = 6
SLOTS = 8


def attention_kernel(
    tbl_ref,
    q_ref, do_ref, k_ref, v_ref, ko_ref, vo_ref, dq_in,
    dq_ref, loc_ref, far_ref, fo_ref,
    kc_ref, vc_ref,
    *, hpk, kv_here, nb,
):
    g = pl.program_id(0)
    b = pl.program_id(1)
    scale = 1.0 / math.sqrt(HD)
    count = nb * SLOTS

    def blk_ref(i):
        return tbl_ref[i]

    def side_ref(i):
        return tbl_ref[count + i]

    def dst_ref(i):
        return tbl_ref[2 * count + i]

    def kind_ref(i):
        return tbl_ref[3 * count + i]

    @pl.when(b == 0)
    def _():
        loc_ref[...] = jnp.zeros_like(loc_ref)
        far_ref[...] = jnp.zeros_like(far_ref)
        fo_ref[...] = jnp.zeros_like(fo_ref)

    for s in range(SLOTS):
        row = pl.multiple_of(blk_ref(b * SLOTS + s) * BLK, BLK)
        side = side_ref(b * SLOTS + s)
        for code, tk, tv in ((0, k_ref, v_ref), (1, ko_ref, vo_ref)):
            @pl.when(side == code)
            def _():
                kc_ref[s * BLK:(s + 1) * BLK, :] = tk[pl.ds(row, BLK), :]
                vc_ref[s * BLK:(s + 1) * BLK, :] = tv[pl.ds(row, BLK), :]

    kc = kc_ref[...]
    vc = vc_ref[...]
    qs = jnp.concatenate([q_ref[:, h * HD:(h + 1) * HD] for h in range(hpk)], axis=0)
    dos = jnp.concatenate([do_ref[:, h * HD:(h + 1) * HD] for h in range(hpk)], axis=0)
    nt = (((1,), (1,)), ((), ()))
    tn = (((0,), (0,)), ((), ()))
    scores = lax.dot_general(qs, kc, nt, preferred_element_type=jnp.float32) * scale
    peak = jnp.max(scores, axis=1, keepdims=True)
    lifted = jnp.exp(scores - peak)
    probs = lifted * (1.0 / jnp.sum(lifted, axis=1, keepdims=True))
    probs_b = probs.astype(jnp.bfloat16)
    attended = jnp.dot(probs_b, vc, preferred_element_type=jnp.float32)
    delta = jnp.sum(dos.astype(jnp.float32) * attended, axis=1, keepdims=True)
    dprobs = lax.dot_general(dos, vc, nt, preferred_element_type=jnp.float32)
    dscores = (probs * (dprobs - delta) * scale).astype(jnp.bfloat16)
    dq = jnp.dot(dscores, kc, preferred_element_type=jnp.float32)
    for h in range(hpk):
        dq_ref[:, h * HD:(h + 1) * HD] = dq[h * BLK:(h + 1) * BLK].astype(jnp.bfloat16)
    kterm = lax.dot_general(qs, dscores, tn, preferred_element_type=jnp.float32)
    vterm = lax.dot_general(dos, probs_b, tn, preferred_element_type=jnp.float32)

    for s in range(SLOTS):
        kind = kind_ref(b * SLOTS + s)
        row = pl.multiple_of(dst_ref(b * SLOTS + s) * BLK, BLK)
        kt = kterm[:, s * BLK:(s + 1) * BLK]
        vt = vterm[:, s * BLK:(s + 1) * BLK]
        rounded = kind == 0
        kt = jnp.where(rounded, kt.astype(jnp.bfloat16).astype(jnp.float32), kt)
        vt = jnp.where(rounded, vt.astype(jnp.bfloat16).astype(jnp.float32), vt)

        side = side_ref(b * SLOTS + s)

        @pl.when(kind == 2)
        def _():
            loc_ref[pl.ds(row, BLK), 0:HD] += kt
            loc_ref[pl.ds(row, BLK), HD:2 * HD] += vt

        for code, out in ((0, far_ref), (1, fo_ref)):
            @pl.when((kind != 2) & (side == code))
            def _():
                kk = out[pl.ds(row, BLK), 0:HD].astype(jnp.float32) + kt
                out[pl.ds(row, BLK), 0:HD] = kk.astype(jnp.bfloat16)
                vv = out[pl.ds(row, BLK), HD:2 * HD].astype(jnp.float32) + vt
                out[pl.ds(row, BLK), HD:2 * HD] = vv.astype(jnp.bfloat16)


def shards(query_rows, key_rows, value_rows, out_grad, block_list):
    shard_index = lax.axis_index("ctx")
    lane_index = lax.axis_index("uly")
    nb = key_rows.shape[0] // BLK
    seq = block_list.shape[0] * BLK
    heads_here = query_rows.shape[1] // HD
    kv_here = max(1, heads_here // GROUP)
    hpk = heads_here // kv_here
    width = 2 * kv_here * HD
    first_kv = lane_index * heads_here // GROUP
    shard_count = lax.axis_size("ctx")
    partner = [(i, i ^ 1) for i in range(shard_count)]
    core = shard_index % 2
    members = shard_count // 2
    member = shard_index // 2
    half = seq // 2
    span = nb * BLK

    rows = lax.dynamic_slice_in_dim(block_list, shard_index * nb, nb, axis=0).astype(jnp.int32)
    owner = rows // nb
    cols = jnp.arange(SLOTS)[None, :]
    is_global = (cols == 3) | (cols == 4)
    local = owner == shard_index
    remote = jnp.logical_not(local) & jnp.logical_not(is_global)
    kind = jnp.where(local, 2, jnp.where(remote, 0, 1)).astype(jnp.int32).reshape(-1)
    owner_side = (owner % 2 != core).astype(jnp.int32)
    half_row = ((member - owner // 2) % members) * nb + rows % nb
    dst = jnp.where(local, rows - shard_index * nb, half_row).astype(jnp.int32).reshape(-1)
    blk = half_row.astype(jnp.int32).reshape(-1)
    side = owner_side.reshape(-1)
    table = jnp.concatenate([blk, side, dst, kind]).astype(jnp.int32)

    kernel = functools.partial(attention_kernel, hpk=hpk, kv_here=1, nb=nb)
    dq = jnp.zeros((nb * BLK, heads_here * HD), jnp.bfloat16)
    sums = []
    for g in range(kv_here):
        col = (first_kv + g) * HD
        kv_own = jnp.concatenate(
            [
                lax.dynamic_slice_in_dim(key_rows, col, HD, axis=1),
                lax.dynamic_slice_in_dim(value_rows, col, HD, axis=1),
            ],
            axis=1,
        )
        gathered = [kv_own]
        for d in range(1, members):
            pairs = [(i, (i + 2 * d) % shard_count) for i in range(shard_count)]
            gathered.append(lax.ppermute(kv_own, "ctx", pairs))
        kv_half = jnp.concatenate(gathered, axis=0)
        kv_other = lax.ppermute(kv_half, "ctx", partner)
        if g > 0:
            kv_half, kv_other, dq = lax.optimization_barrier((kv_half, kv_other, dq))
        grid_spec = pltpu.PrefetchScalarGridSpec(
            num_scalar_prefetch=1,
            grid=(1, nb),
            in_specs=[
                pl.BlockSpec((BLK, hpk * HD), lambda z, b, *_, g=g: (b, g)),
                pl.BlockSpec((BLK, hpk * HD), lambda z, b, *_, g=g: (b, g)),
                pl.BlockSpec((half, HD), lambda z, b, *_: (0, 0)),
                pl.BlockSpec((half, HD), lambda z, b, *_: (0, 1)),
                pl.BlockSpec((half, HD), lambda z, b, *_: (0, 0)),
                pl.BlockSpec((half, HD), lambda z, b, *_: (0, 1)),
                pl.BlockSpec(memory_space=pl.ANY),
            ],
            out_specs=[
                pl.BlockSpec((BLK, hpk * HD), lambda z, b, *_, g=g: (b, g)),
                pl.BlockSpec((span, 2 * HD), lambda z, b, *_: (0, 0)),
                pl.BlockSpec((half, 2 * HD), lambda z, b, *_: (0, 0)),
                pl.BlockSpec((half, 2 * HD), lambda z, b, *_: (0, 0)),
            ],
            scratch_shapes=[
                pltpu.VMEM((SLOTS * BLK, HD), jnp.bfloat16),
                pltpu.VMEM((SLOTS * BLK, HD), jnp.bfloat16),
            ],
        )
        dq, loc, far, far_other = pl.pallas_call(
            kernel,
            grid_spec=grid_spec,
            out_shape=[
                jax.ShapeDtypeStruct((nb * BLK, heads_here * HD), jnp.bfloat16),
                jax.ShapeDtypeStruct((span, 2 * HD), jnp.float32),
                jax.ShapeDtypeStruct((half, 2 * HD), jnp.bfloat16),
                jax.ShapeDtypeStruct((half, 2 * HD), jnp.bfloat16),
            ],
            input_output_aliases={7: 0},
            cost_estimate=pl.CostEstimate(
                flops=12 * nb * hpk * BLK * SLOTS * BLK * HD,
                transcendentals=nb * hpk * BLK * SLOTS * BLK,
                bytes_accessed=4 * nb * BLK * hpk * HD + 4 * half * HD * 2 + 12 * half * HD,
            ),
            compiler_params=pltpu.CompilerParams(dimension_semantics=("arbitrary", "arbitrary")),
        )(table, query_rows, out_grad, kv_half, kv_half, kv_other, kv_other, dq)
        from_partner = lax.ppermute(far_other, "ctx", partner)
        mine = (far.astype(jnp.float32) + from_partner.astype(jnp.float32)).astype(jnp.bfloat16)
        total = far[0:span].astype(jnp.float32) + from_partner[0:span].astype(jnp.float32)
        for d in range(1, members):
            pairs = [(i, (i - 2 * d) % shard_count) for i in range(shard_count)]
            total = total + lax.ppermute(
                mine[d * span:(d + 1) * span], "ctx", pairs
            ).astype(jnp.float32)
        sums.append((total + loc).reshape(nb, HD, 2, BLK))
    stacked = jnp.stack([s[:, :, 0] for s in sums] + [s[:, :, 1] for s in sums], axis=2)
    kv_grad = jnp.transpose(stacked, (0, 3, 2, 1)).reshape(span, 2 * kv_here * HD).astype(jnp.bfloat16)
    width = 2 * kv_here * HD

    query_out = lax.all_to_all(dq, "uly", split_axis=0, concat_axis=1, tiled=True)
    query_out, kv_grad = lax.optimization_barrier((query_out, kv_grad))
    kv_seq = lax.all_to_all(kv_grad, "uly", split_axis=0, concat_axis=1, tiled=True)
    rows_here = kv_seq.shape[0]
    lane_count = kv_seq.shape[1] // width
    spread = kv_seq.reshape(rows_here, lane_count, 2, kv_here * HD)

    def gather_heads(part):
        if heads_here >= GROUP:
            return part.reshape(rows_here, KVH * HD)
        lanes_per = GROUP // heads_here
        merged = part.astype(jnp.float32).reshape(rows_here, KVH, lanes_per, HD).sum(axis=2)
        return merged.reshape(rows_here, KVH * HD).astype(jnp.bfloat16)

    return (query_out, gather_heads(spread[:, :, 0]), gather_heads(spread[:, :, 1]))


def solution(mesh):
    return jax.shard_map(
        shards,
        mesh=mesh,
        in_specs=(P("ctx", "uly"), P("ctx", None), P("ctx", None), P("ctx", "uly"), P()),
        out_specs=(P(("ctx", "uly"), None), P(("ctx", "uly"), None), P(("ctx", "uly"), None)),
        check_vma=False,
    )
```

```python
import functools
import math

import jax
import jax.numpy as jnp
from jax import lax
from jax.experimental import pallas as pl
from jax.experimental.pallas import tpu as pltpu
from jax.sharding import PartitionSpec as P

HD = 128
KVH = 8
BLK = 128
GROUP = 6
SLOTS = 8


def attention_kernel(
    tbl_ref,
    q_ref, do_ref, k_ref, v_ref, ko_ref, vo_ref, *refs,
    hpk, kv_here, nb,
):
    dq_ref, loc_ref, far_ref, fo_ref, kc_ref, vc_ref = refs[-6:]
    g = pl.program_id(0)
    b = pl.program_id(1)
    scale = 1.0 / math.sqrt(HD)
    count = nb * SLOTS

    def blk_ref(i):
        return tbl_ref[i]

    def side_ref(i):
        return tbl_ref[count + i]

    def dst_ref(i):
        return tbl_ref[2 * count + i]

    def kind_ref(i):
        return tbl_ref[3 * count + i]

    @pl.when(b == 0)
    def _():
        loc_ref[...] = jnp.zeros_like(loc_ref)
        far_ref[...] = jnp.zeros_like(far_ref)
        fo_ref[...] = jnp.zeros_like(fo_ref)

    for s in range(SLOTS):
        row = pl.multiple_of(blk_ref(b * SLOTS + s) * BLK, BLK)
        side = side_ref(b * SLOTS + s)
        for code, tk, tv in ((0, k_ref, v_ref), (1, ko_ref, vo_ref)):
            @pl.when(side == code)
            def _():
                kc_ref[s * BLK:(s + 1) * BLK, :] = tk[pl.ds(row, BLK), :]
                vc_ref[s * BLK:(s + 1) * BLK, :] = tv[pl.ds(row, BLK), :]

    kc = kc_ref[...]
    vc = vc_ref[...]
    qs = jnp.concatenate([q_ref[:, h * HD:(h + 1) * HD] for h in range(hpk)], axis=0)
    dos = jnp.concatenate([do_ref[:, h * HD:(h + 1) * HD] for h in range(hpk)], axis=0)
    nt = (((1,), (1,)), ((), ()))
    tn = (((0,), (0,)), ((), ()))
    scores = lax.dot_general(qs, kc, nt, preferred_element_type=jnp.float32) * scale
    peak = jnp.max(scores, axis=1, keepdims=True)
    lifted = jnp.exp(scores - peak)
    probs = lifted * (1.0 / jnp.sum(lifted, axis=1, keepdims=True))
    probs_b = probs.astype(jnp.bfloat16)
    attended = jnp.dot(probs_b, vc, preferred_element_type=jnp.float32)
    delta = jnp.sum(dos.astype(jnp.float32) * attended, axis=1, keepdims=True)
    dprobs = lax.dot_general(dos, vc, nt, preferred_element_type=jnp.float32)
    dscores = (probs * (dprobs - delta) * scale).astype(jnp.bfloat16)
    dq = jnp.dot(dscores, kc, preferred_element_type=jnp.float32)
    for h in range(hpk):
        dq_ref[:, h * HD:(h + 1) * HD] = dq[h * BLK:(h + 1) * BLK].astype(jnp.bfloat16)
    kterm = lax.dot_general(qs, dscores, tn, preferred_element_type=jnp.float32)
    vterm = lax.dot_general(dos, probs_b, tn, preferred_element_type=jnp.float32)

    for s in range(SLOTS):
        kind = kind_ref(b * SLOTS + s)
        row = pl.multiple_of(dst_ref(b * SLOTS + s) * BLK, BLK)
        kt = kterm[:, s * BLK:(s + 1) * BLK]
        vt = vterm[:, s * BLK:(s + 1) * BLK]
        rounded = kind == 0
        kt = jnp.where(rounded, kt.astype(jnp.bfloat16).astype(jnp.float32), kt)
        vt = jnp.where(rounded, vt.astype(jnp.bfloat16).astype(jnp.float32), vt)

        side = side_ref(b * SLOTS + s)

        @pl.when(kind == 2)
        def _():
            loc_ref[pl.ds(row, BLK), 0:HD] += kt
            loc_ref[pl.ds(row, BLK), HD:2 * HD] += vt

        for code, out in ((0, far_ref), (1, fo_ref)):
            @pl.when((kind != 2) & (side == code))
            def _():
                kk = out[pl.ds(row, BLK), 0:HD].astype(jnp.float32) + kt
                out[pl.ds(row, BLK), 0:HD] = kk.astype(jnp.bfloat16)
                vv = out[pl.ds(row, BLK), HD:2 * HD].astype(jnp.float32) + vt
                out[pl.ds(row, BLK), HD:2 * HD] = vv.astype(jnp.bfloat16)


def shards(query_rows, key_rows, value_rows, out_grad, block_list):
    shard_index = lax.axis_index("ctx")
    lane_index = lax.axis_index("uly")
    nb = key_rows.shape[0] // BLK
    seq = block_list.shape[0] * BLK
    heads_here = query_rows.shape[1] // HD
    kv_here = max(1, heads_here // GROUP)
    hpk = heads_here // kv_here
    width = 2 * kv_here * HD
    first_kv = lane_index * heads_here // GROUP
    shard_count = lax.axis_size("ctx")
    partner = [(i, i ^ 1) for i in range(shard_count)]
    core = shard_index % 2
    members = shard_count // 2
    member = shard_index // 2
    half = seq // 2
    span = nb * BLK

    rows = lax.dynamic_slice_in_dim(block_list, shard_index * nb, nb, axis=0).astype(jnp.int32)
    owner = rows // nb
    cols = jnp.arange(SLOTS)[None, :]
    is_global = (cols == 3) | (cols == 4)
    local = owner == shard_index
    remote = jnp.logical_not(local) & jnp.logical_not(is_global)
    kind = jnp.where(local, 2, jnp.where(remote, 0, 1)).astype(jnp.int32).reshape(-1)
    owner_side = (owner % 2 != core).astype(jnp.int32)
    half_row = ((member - owner // 2) % members) * nb + rows % nb
    dst = jnp.where(local, rows - shard_index * nb, half_row).astype(jnp.int32).reshape(-1)
    blk = half_row.astype(jnp.int32).reshape(-1)
    side = owner_side.reshape(-1)
    table = jnp.concatenate([blk, side, dst, kind]).astype(jnp.int32)

    kernel = functools.partial(attention_kernel, hpk=hpk, kv_here=1, nb=nb)
    dq = None
    sums = []
    for g in range(kv_here):
        col = (first_kv + g) * HD
        kv_own = jnp.concatenate(
            [
                lax.dynamic_slice_in_dim(key_rows, col, HD, axis=1),
                lax.dynamic_slice_in_dim(value_rows, col, HD, axis=1),
            ],
            axis=1,
        )
        gathered = [kv_own]
        for d in range(1, members):
            pairs = [(i, (i + 2 * d) % shard_count) for i in range(shard_count)]
            gathered.append(lax.ppermute(kv_own, "ctx", pairs))
        kv_half = jnp.concatenate(gathered, axis=0)
        kv_other = lax.ppermute(kv_half, "ctx", partner)
        if g > 0:
            kv_half, kv_other, dq = lax.optimization_barrier((kv_half, kv_other, dq))
        grid_spec = pltpu.PrefetchScalarGridSpec(
            num_scalar_prefetch=1,
            grid=(1, nb),
            in_specs=[
                pl.BlockSpec((BLK, hpk * HD), lambda z, b, *_, g=g: (b, g)),
                pl.BlockSpec((BLK, hpk * HD), lambda z, b, *_, g=g: (b, g)),
                pl.BlockSpec((half, HD), lambda z, b, *_: (0, 0)),
                pl.BlockSpec((half, HD), lambda z, b, *_: (0, 1)),
                pl.BlockSpec((half, HD), lambda z, b, *_: (0, 0)),
                pl.BlockSpec((half, HD), lambda z, b, *_: (0, 1)),
            ] + ([] if dq is None else [pl.BlockSpec(memory_space=pl.ANY)]),
            out_specs=[
                pl.BlockSpec((BLK, hpk * HD), lambda z, b, *_, g=g: (b, g)),
                pl.BlockSpec((span, 2 * HD), lambda z, b, *_: (0, 0)),
                pl.BlockSpec((half, 2 * HD), lambda z, b, *_: (0, 0)),
                pl.BlockSpec((half, 2 * HD), lambda z, b, *_: (0, 0)),
            ],
            scratch_shapes=[
                pltpu.VMEM((SLOTS * BLK, HD), jnp.bfloat16),
                pltpu.VMEM((SLOTS * BLK, HD), jnp.bfloat16),
            ],
        )
        dq, loc, far, far_other = pl.pallas_call(
            kernel,
            grid_spec=grid_spec,
            out_shape=[
                jax.ShapeDtypeStruct((nb * BLK, heads_here * HD), jnp.bfloat16),
                jax.ShapeDtypeStruct((span, 2 * HD), jnp.float32),
                jax.ShapeDtypeStruct((half, 2 * HD), jnp.bfloat16),
                jax.ShapeDtypeStruct((half, 2 * HD), jnp.bfloat16),
            ],
            input_output_aliases={} if dq is None else {7: 0},
            cost_estimate=pl.CostEstimate(
                flops=12 * nb * hpk * BLK * SLOTS * BLK * HD,
                transcendentals=nb * hpk * BLK * SLOTS * BLK,
                bytes_accessed=4 * nb * BLK * hpk * HD + 4 * half * HD * 2 + 12 * half * HD,
            ),
            compiler_params=pltpu.CompilerParams(dimension_semantics=("arbitrary", "arbitrary")),
        )(table, query_rows, out_grad, kv_half, kv_half, kv_other, kv_other, *([] if dq is None else [dq]))
        from_partner = lax.ppermute(far_other, "ctx", partner)
        mine = (far.astype(jnp.float32) + from_partner.astype(jnp.float32)).astype(jnp.bfloat16)
        total = far[0:span].astype(jnp.float32) + from_partner[0:span].astype(jnp.float32)
        for d in range(1, members):
            pairs = [(i, (i - 2 * d) % shard_count) for i in range(shard_count)]
            total = total + lax.ppermute(
                mine[d * span:(d + 1) * span], "ctx", pairs
            ).astype(jnp.float32)
        sums.append((total + loc).reshape(nb, HD, 2, BLK))
    stacked = jnp.stack([s[:, :, 0] for s in sums] + [s[:, :, 1] for s in sums], axis=2)
    kv_grad = jnp.transpose(stacked, (0, 3, 2, 1)).reshape(span, 2 * kv_here * HD).astype(jnp.bfloat16)
    width = 2 * kv_here * HD

    query_out = lax.all_to_all(dq, "uly", split_axis=0, concat_axis=1, tiled=True)
    query_out, kv_grad = lax.optimization_barrier((query_out, kv_grad))
    kv_seq = lax.all_to_all(kv_grad, "uly", split_axis=0, concat_axis=1, tiled=True)
    rows_here = kv_seq.shape[0]
    lane_count = kv_seq.shape[1] // width
    spread = kv_seq.reshape(rows_here, lane_count, 2, kv_here * HD)

    def gather_heads(part):
        if heads_here >= GROUP:
            return part.reshape(rows_here, KVH * HD)
        lanes_per = GROUP // heads_here
        merged = part.astype(jnp.float32).reshape(rows_here, KVH, lanes_per, HD).sum(axis=2)
        return merged.reshape(rows_here, KVH * HD).astype(jnp.bfloat16)

    return (query_out, gather_heads(spread[:, :, 0]), gather_heads(spread[:, :, 1]))


def solution(mesh):
    return jax.shard_map(
        shards,
        mesh=mesh,
        in_specs=(P("ctx", "uly"), P("ctx", None), P("ctx", None), P("ctx", "uly"), P()),
        out_specs=(P(("ctx", "uly"), None), P(("ctx", "uly"), None), P(("ctx", "uly"), None)),
        check_vma=False,
    )
```

```python
import functools
import math

import jax
import jax.numpy as jnp
from jax import lax
from jax.experimental import pallas as pl
from jax.experimental.pallas import tpu as pltpu
from jax.sharding import PartitionSpec as P

HD = 128
KVH = 8
BLK = 128
GROUP = 6
SLOTS = 8


def attention_kernel(
    tbl_ref,
    q_ref, do_ref, k_ref, v_ref, ko_ref, vo_ref, *refs,
    hpk, kv_here, nb,
):
    dq_ref, loc_ref, far_ref, fo_ref, kc_ref, vc_ref = refs[-6:]
    g = pl.program_id(0)
    b = pl.program_id(1)
    scale = 1.0 / math.sqrt(HD)
    count = nb * SLOTS

    def blk_ref(i):
        return tbl_ref[i]

    def side_ref(i):
        return tbl_ref[count + i]

    def dst_ref(i):
        return tbl_ref[2 * count + i]

    def kind_ref(i):
        return tbl_ref[3 * count + i]

    @pl.when(b == 0)
    def _():
        loc_ref[...] = jnp.zeros_like(loc_ref)
        far_ref[...] = jnp.zeros_like(far_ref)
        fo_ref[...] = jnp.zeros_like(fo_ref)

    for s in range(SLOTS):
        row = pl.multiple_of(blk_ref(b * SLOTS + s) * BLK, BLK)
        side = side_ref(b * SLOTS + s)
        for code, tk, tv in ((0, k_ref, v_ref), (1, ko_ref, vo_ref)):
            @pl.when(side == code)
            def _():
                kc_ref[s * BLK:(s + 1) * BLK, :] = tk[pl.ds(row, BLK), :]
                vc_ref[s * BLK:(s + 1) * BLK, :] = tv[pl.ds(row, BLK), :]

    kc = kc_ref[...]
    vc = vc_ref[...]
    qs = jnp.concatenate([q_ref[:, h * HD:(h + 1) * HD] for h in range(hpk)], axis=0)
    dos = jnp.concatenate([do_ref[:, h * HD:(h + 1) * HD] for h in range(hpk)], axis=0)
    nt = (((1,), (1,)), ((), ()))
    tn = (((0,), (0,)), ((), ()))
    scores = lax.dot_general(qs, kc, nt, preferred_element_type=jnp.float32) * scale
    peak = jnp.max(scores, axis=1, keepdims=True)
    lifted = jnp.exp(scores - peak)
    probs = lifted * (1.0 / jnp.sum(lifted, axis=1, keepdims=True))
    probs_b = probs.astype(jnp.bfloat16)
    attended = jnp.dot(probs_b, vc, preferred_element_type=jnp.float32)
    delta = jnp.sum(dos.astype(jnp.float32) * attended, axis=1, keepdims=True)
    dprobs = lax.dot_general(dos, vc, nt, preferred_element_type=jnp.float32)
    dscores = (probs * (dprobs - delta) * scale).astype(jnp.bfloat16)
    dq = jnp.dot(dscores, kc, preferred_element_type=jnp.float32)
    for h in range(hpk):
        dq_ref[:, h * HD:(h + 1) * HD] = dq[h * BLK:(h + 1) * BLK].astype(jnp.bfloat16)
    kterm = lax.dot_general(qs, dscores, tn, preferred_element_type=jnp.float32)
    vterm = lax.dot_general(dos, probs_b, tn, preferred_element_type=jnp.float32)

    for s in range(SLOTS):
        kind = kind_ref(b * SLOTS + s)
        row = pl.multiple_of(dst_ref(b * SLOTS + s) * BLK, BLK)
        kt = kterm[:, s * BLK:(s + 1) * BLK]
        vt = vterm[:, s * BLK:(s + 1) * BLK]
        rounded = kind == 0
        kt = jnp.where(rounded, kt.astype(jnp.bfloat16).astype(jnp.float32), kt)
        vt = jnp.where(rounded, vt.astype(jnp.bfloat16).astype(jnp.float32), vt)

        side = side_ref(b * SLOTS + s)

        @pl.when(kind == 2)
        def _():
            loc_ref[pl.ds(row, BLK), 0:HD] += kt
            loc_ref[pl.ds(row, BLK), HD:2 * HD] += vt

        for code, out in ((0, far_ref), (1, fo_ref)):
            @pl.when((kind != 2) & (side == code))
            def _():
                kk = out[pl.ds(row, BLK), 0:HD].astype(jnp.float32) + kt
                out[pl.ds(row, BLK), 0:HD] = kk.astype(jnp.bfloat16)
                vv = out[pl.ds(row, BLK), HD:2 * HD].astype(jnp.float32) + vt
                out[pl.ds(row, BLK), HD:2 * HD] = vv.astype(jnp.bfloat16)


def shards(query_rows, key_rows, value_rows, out_grad, block_list):
    shard_index = lax.axis_index("ctx")
    lane_index = lax.axis_index("uly")
    nb = key_rows.shape[0] // BLK
    seq = block_list.shape[0] * BLK
    heads_here = query_rows.shape[1] // HD
    kv_here = max(1, heads_here // GROUP)
    hpk = heads_here // kv_here
    width = 2 * kv_here * HD
    first_kv = lane_index * heads_here // GROUP
    shard_count = lax.axis_size("ctx")
    partner = [(i, i ^ 1) for i in range(shard_count)]
    core = shard_index % 2
    members = shard_count // 2
    member = shard_index // 2
    half = seq // 2
    span = nb * BLK

    rows = lax.dynamic_slice_in_dim(block_list, shard_index * nb, nb, axis=0).astype(jnp.int32)
    owner = rows // nb
    cols = jnp.arange(SLOTS)[None, :]
    is_global = (cols == 3) | (cols == 4)
    local = owner == shard_index
    remote = jnp.logical_not(local) & jnp.logical_not(is_global)
    kind = jnp.where(local, 2, jnp.where(remote, 0, 1)).astype(jnp.int32).reshape(-1)
    owner_side = (owner % 2 != core).astype(jnp.int32)
    half_row = ((member - owner // 2) % members) * nb + rows % nb
    dst = jnp.where(local, rows - shard_index * nb, half_row).astype(jnp.int32).reshape(-1)
    blk = half_row.astype(jnp.int32).reshape(-1)
    side = owner_side.reshape(-1)
    table = jnp.concatenate([blk, side, dst, kind]).astype(jnp.int32)

    kernel = functools.partial(attention_kernel, hpk=hpk, kv_here=1, nb=nb)
    dq = None
    sums = []
    for g in range(kv_here):
        col = (first_kv + g) * HD
        kv_own = jnp.concatenate(
            [
                lax.dynamic_slice_in_dim(key_rows, col, HD, axis=1),
                lax.dynamic_slice_in_dim(value_rows, col, HD, axis=1),
            ],
            axis=1,
        )
        gathered = [kv_own]
        for d in range(1, members):
            pairs = [(i, (i + 2 * d) % shard_count) for i in range(shard_count)]
            gathered.append(lax.ppermute(kv_own, "ctx", pairs))
        kv_half = jnp.concatenate(gathered, axis=0)
        kv_other = lax.ppermute(kv_half, "ctx", partner)
        if g > 0:
            kv_half, kv_other, dq = lax.optimization_barrier((kv_half, kv_other, dq))
        grid_spec = pltpu.PrefetchScalarGridSpec(
            num_scalar_prefetch=1,
            grid=(1, nb),
            in_specs=[
                pl.BlockSpec((BLK, hpk * HD), lambda z, b, *_, g=g: (b, g)),
                pl.BlockSpec((BLK, hpk * HD), lambda z, b, *_, g=g: (b, g)),
                pl.BlockSpec((half, HD), lambda z, b, *_: (0, 0)),
                pl.BlockSpec((half, HD), lambda z, b, *_: (0, 1)),
                pl.BlockSpec((half, HD), lambda z, b, *_: (0, 0)),
                pl.BlockSpec((half, HD), lambda z, b, *_: (0, 1)),
            ] + ([] if dq is None else [pl.BlockSpec(memory_space=pl.ANY)]),
            out_specs=[
                pl.BlockSpec((BLK, hpk * HD), lambda z, b, *_, g=g: (b, g)),
                pl.BlockSpec((span, 2 * HD), lambda z, b, *_: (0, 0)),
                pl.BlockSpec((half, 2 * HD), lambda z, b, *_: (0, 0)),
                pl.BlockSpec((half, 2 * HD), lambda z, b, *_: (0, 0)),
            ],
            scratch_shapes=[
                pltpu.VMEM((SLOTS * BLK, HD), jnp.bfloat16),
                pltpu.VMEM((SLOTS * BLK, HD), jnp.bfloat16),
            ],
        )
        dq, loc, far, far_other = pl.pallas_call(
            kernel,
            grid_spec=grid_spec,
            out_shape=[
                jax.ShapeDtypeStruct((nb * BLK, heads_here * HD), jnp.bfloat16),
                jax.ShapeDtypeStruct((span, 2 * HD), jnp.float32),
                jax.ShapeDtypeStruct((half, 2 * HD), jnp.bfloat16),
                jax.ShapeDtypeStruct((half, 2 * HD), jnp.bfloat16),
            ],
            input_output_aliases={} if dq is None else {7: 0},
            cost_estimate=pl.CostEstimate(
                flops=12 * nb * hpk * BLK * SLOTS * BLK * HD,
                transcendentals=nb * hpk * BLK * SLOTS * BLK,
                bytes_accessed=4 * nb * BLK * hpk * HD + 4 * half * HD * 2 + 12 * half * HD,
            ),
            compiler_params=pltpu.CompilerParams(dimension_semantics=("arbitrary", "arbitrary")),
        )(table, query_rows, out_grad, kv_half, kv_half, kv_other, kv_other, *([] if dq is None else [dq]))
        from_partner = lax.ppermute(far_other, "ctx", partner)
        if g == kv_here - 1:
            dq, from_partner = lax.optimization_barrier((dq, from_partner))
        mine = (far.astype(jnp.float32) + from_partner.astype(jnp.float32)).astype(jnp.bfloat16)
        total = far[0:span].astype(jnp.float32) + from_partner[0:span].astype(jnp.float32)
        for d in range(1, members):
            pairs = [(i, (i - 2 * d) % shard_count) for i in range(shard_count)]
            total = total + lax.ppermute(
                mine[d * span:(d + 1) * span], "ctx", pairs
            ).astype(jnp.float32)
        sums.append((total + loc).reshape(nb, HD, 2, BLK))
    stacked = jnp.stack([s[:, :, 0] for s in sums] + [s[:, :, 1] for s in sums], axis=2)
    kv_grad = jnp.transpose(stacked, (0, 3, 2, 1)).reshape(span, 2 * kv_here * HD).astype(jnp.bfloat16)
    width = 2 * kv_here * HD

    query_out = lax.all_to_all(dq, "uly", split_axis=0, concat_axis=1, tiled=True)
    query_out, kv_grad = lax.optimization_barrier((query_out, kv_grad))
    kv_seq = lax.all_to_all(kv_grad, "uly", split_axis=0, concat_axis=1, tiled=True)
    rows_here = kv_seq.shape[0]
    lane_count = kv_seq.shape[1] // width
    spread = kv_seq.reshape(rows_here, lane_count, 2, kv_here * HD)

    def gather_heads(part):
        if heads_here >= GROUP:
            return part.reshape(rows_here, KVH * HD)
        lanes_per = GROUP // heads_here
        merged = part.astype(jnp.float32).reshape(rows_here, KVH, lanes_per, HD).sum(axis=2)
        return merged.reshape(rows_here, KVH * HD).astype(jnp.bfloat16)

    return (query_out, gather_heads(spread[:, :, 0]), gather_heads(spread[:, :, 1]))


def solution(mesh):
    return jax.shard_map(
        shards,
        mesh=mesh,
        in_specs=(P("ctx", "uly"), P("ctx", None), P("ctx", None), P("ctx", "uly"), P()),
        out_specs=(P(("ctx", "uly"), None), P(("ctx", "uly"), None), P(("ctx", "uly"), None)),
        check_vma=False,
    )
```

```python
import functools
import math

import jax
import jax.numpy as jnp
from jax import lax
from jax.experimental import pallas as pl
from jax.experimental.pallas import tpu as pltpu
from jax.sharding import PartitionSpec as P

HD = 128
KVH = 8
BLK = 128
GROUP = 6
SLOTS = 8


def attention_kernel(
    tbl_ref,
    q_ref, do_ref, k_ref, v_ref, ko_ref, vo_ref, dq_in,
    dq_ref, loc_ref, far_ref, fo_ref,
    kc_ref, vc_ref,
    *, hpk, kv_here, nb,
):
    g = pl.program_id(0)
    b = pl.program_id(1)
    scale = 1.0 / math.sqrt(HD)
    count = nb * SLOTS

    def blk_ref(i):
        return tbl_ref[i]

    def side_ref(i):
        return tbl_ref[count + i]

    def dst_ref(i):
        return tbl_ref[2 * count + i]

    def kind_ref(i):
        return tbl_ref[3 * count + i]

    @pl.when(b == 0)
    def _():
        loc_ref[...] = jnp.zeros_like(loc_ref)
        far_ref[...] = jnp.zeros_like(far_ref)
        fo_ref[...] = jnp.zeros_like(fo_ref)

    for s in range(SLOTS):
        row = pl.multiple_of(blk_ref(b * SLOTS + s) * BLK, BLK)
        side = side_ref(b * SLOTS + s)
        for code, tk, tv in ((0, k_ref, v_ref), (1, ko_ref, vo_ref)):
            @pl.when(side == code)
            def _():
                kc_ref[s * BLK:(s + 1) * BLK, :] = tk[pl.ds(row, BLK), :]
                vc_ref[s * BLK:(s + 1) * BLK, :] = tv[pl.ds(row, BLK), :]

    kc = kc_ref[...]
    vc = vc_ref[...]
    qs = jnp.concatenate([q_ref[:, h * HD:(h + 1) * HD] for h in range(hpk)], axis=0)
    dos = jnp.concatenate([do_ref[:, h * HD:(h + 1) * HD] for h in range(hpk)], axis=0)
    nt = (((1,), (1,)), ((), ()))
    tn = (((0,), (0,)), ((), ()))
    scores = lax.dot_general(qs, kc, nt, preferred_element_type=jnp.float32) * scale
    peak = jnp.max(scores, axis=1, keepdims=True)
    lifted = jnp.exp(scores - peak)
    probs = lifted * (1.0 / jnp.sum(lifted, axis=1, keepdims=True))
    probs_b = probs.astype(jnp.bfloat16)
    attended = jnp.dot(probs_b, vc, preferred_element_type=jnp.float32)
    delta = jnp.sum(dos.astype(jnp.float32) * attended, axis=1, keepdims=True)
    dprobs = lax.dot_general(dos, vc, nt, preferred_element_type=jnp.float32)
    dscores = (probs * (dprobs - delta) * scale).astype(jnp.bfloat16)
    dq = jnp.dot(dscores, kc, preferred_element_type=jnp.float32)
    for h in range(hpk):
        dq_ref[:, h * HD:(h + 1) * HD] = dq[h * BLK:(h + 1) * BLK].astype(jnp.bfloat16)
    kterm = lax.dot_general(qs, dscores, tn, preferred_element_type=jnp.float32)
    vterm = lax.dot_general(dos, probs_b, tn, preferred_element_type=jnp.float32)

    for s in range(SLOTS):
        kind = kind_ref(b * SLOTS + s)
        row = pl.multiple_of(dst_ref(b * SLOTS + s) * BLK, BLK)
        kt = kterm[:, s * BLK:(s + 1) * BLK]
        vt = vterm[:, s * BLK:(s + 1) * BLK]
        rounded = kind == 0
        kt = jnp.where(rounded, kt.astype(jnp.bfloat16).astype(jnp.float32), kt)
        vt = jnp.where(rounded, vt.astype(jnp.bfloat16).astype(jnp.float32), vt)

        side = side_ref(b * SLOTS + s)

        @pl.when(kind == 2)
        def _():
            loc_ref[pl.ds(row, BLK), 0:HD] += kt
            loc_ref[pl.ds(row, BLK), HD:2 * HD] += vt

        for code, out in ((0, far_ref), (1, fo_ref)):
            @pl.when((kind != 2) & (side == code))
            def _():
                kk = out[pl.ds(row, BLK), 0:HD].astype(jnp.float32) + kt
                out[pl.ds(row, BLK), 0:HD] = kk.astype(jnp.bfloat16)
                vv = out[pl.ds(row, BLK), HD:2 * HD].astype(jnp.float32) + vt
                out[pl.ds(row, BLK), HD:2 * HD] = vv.astype(jnp.bfloat16)


def shards(query_rows, key_rows, value_rows, out_grad, block_list):
    shard_index = lax.axis_index("ctx")
    lane_index = lax.axis_index("uly")
    nb = key_rows.shape[0] // BLK
    seq = block_list.shape[0] * BLK
    heads_here = query_rows.shape[1] // HD
    kv_here = max(1, heads_here // GROUP)
    hpk = heads_here // kv_here
    width = 2 * kv_here * HD
    first_kv = lane_index * heads_here // GROUP
    shard_count = lax.axis_size("ctx")
    partner = [(i, i ^ 1) for i in range(shard_count)]
    core = shard_index % 2
    members = shard_count // 2
    member = shard_index // 2
    half = seq // 2
    span = nb * BLK

    rows = lax.dynamic_slice_in_dim(block_list, shard_index * nb, nb, axis=0).astype(jnp.int32)
    owner = rows // nb
    cols = jnp.arange(SLOTS)[None, :]
    is_global = (cols == 3) | (cols == 4)
    local = owner == shard_index
    remote = jnp.logical_not(local) & jnp.logical_not(is_global)
    kind = jnp.where(local, 2, jnp.where(remote, 0, 1)).astype(jnp.int32).reshape(-1)
    owner_side = (owner % 2 != core).astype(jnp.int32)
    half_row = jnp.bitwise_xor(member, owner // 2) * nb + rows % nb
    dst = jnp.where(local, rows - shard_index * nb, half_row).astype(jnp.int32).reshape(-1)
    blk = half_row.astype(jnp.int32).reshape(-1)
    side = owner_side.reshape(-1)
    table = jnp.concatenate([blk, side, dst, kind]).astype(jnp.int32)

    kernel = functools.partial(attention_kernel, hpk=hpk, kv_here=1, nb=nb)
    dq = jnp.zeros((nb * BLK, heads_here * HD), jnp.bfloat16)
    sums = []
    for g in range(kv_here):
        col = (first_kv + g) * HD
        kv_own = jnp.concatenate(
            [
                lax.dynamic_slice_in_dim(key_rows, col, HD, axis=1),
                lax.dynamic_slice_in_dim(value_rows, col, HD, axis=1),
            ],
            axis=1,
        )
        gathered = [kv_own]
        for d in range(1, members):
            pairs = [(i, i ^ (2 * d)) for i in range(shard_count)]
            gathered.append(lax.ppermute(kv_own, "ctx", pairs))
        kv_half = jnp.concatenate(gathered, axis=0)
        kv_other = lax.ppermute(kv_half, "ctx", partner)
        if g > 0:
            kv_half, kv_other, dq = lax.optimization_barrier((kv_half, kv_other, dq))
        grid_spec = pltpu.PrefetchScalarGridSpec(
            num_scalar_prefetch=1,
            grid=(1, nb),
            in_specs=[
                pl.BlockSpec((BLK, hpk * HD), lambda z, b, *_, g=g: (b, g)),
                pl.BlockSpec((BLK, hpk * HD), lambda z, b, *_, g=g: (b, g)),
                pl.BlockSpec((half, HD), lambda z, b, *_: (0, 0)),
                pl.BlockSpec((half, HD), lambda z, b, *_: (0, 1)),
                pl.BlockSpec((half, HD), lambda z, b, *_: (0, 0)),
                pl.BlockSpec((half, HD), lambda z, b, *_: (0, 1)),
                pl.BlockSpec(memory_space=pl.ANY),
            ],
            out_specs=[
                pl.BlockSpec((BLK, hpk * HD), lambda z, b, *_, g=g: (b, g)),
                pl.BlockSpec((span, 2 * HD), lambda z, b, *_: (0, 0)),
                pl.BlockSpec((half, 2 * HD), lambda z, b, *_: (0, 0)),
                pl.BlockSpec((half, 2 * HD), lambda z, b, *_: (0, 0)),
            ],
            scratch_shapes=[
                pltpu.VMEM((SLOTS * BLK, HD), jnp.bfloat16),
                pltpu.VMEM((SLOTS * BLK, HD), jnp.bfloat16),
            ],
        )
        dq, loc, far, far_other = pl.pallas_call(
            kernel,
            grid_spec=grid_spec,
            out_shape=[
                jax.ShapeDtypeStruct((nb * BLK, heads_here * HD), jnp.bfloat16),
                jax.ShapeDtypeStruct((span, 2 * HD), jnp.float32),
                jax.ShapeDtypeStruct((half, 2 * HD), jnp.bfloat16),
                jax.ShapeDtypeStruct((half, 2 * HD), jnp.bfloat16),
            ],
            input_output_aliases={7: 0},
            cost_estimate=pl.CostEstimate(
                flops=12 * nb * hpk * BLK * SLOTS * BLK * HD,
                transcendentals=nb * hpk * BLK * SLOTS * BLK,
                bytes_accessed=4 * nb * BLK * hpk * HD + 4 * half * HD * 2 + 12 * half * HD,
            ),
            compiler_params=pltpu.CompilerParams(dimension_semantics=("arbitrary", "arbitrary")),
        )(table, query_rows, out_grad, kv_half, kv_half, kv_other, kv_other, dq)
        from_partner = lax.ppermute(far_other, "ctx", partner)
        mine = (far.astype(jnp.float32) + from_partner.astype(jnp.float32)).astype(jnp.bfloat16)
        total = far[0:span].astype(jnp.float32) + from_partner[0:span].astype(jnp.float32)
        for d in range(1, members):
            pairs = [(i, i ^ (2 * d)) for i in range(shard_count)]
            total = total + lax.ppermute(
                mine[d * span:(d + 1) * span], "ctx", pairs
            ).astype(jnp.float32)
        sums.append((total + loc).reshape(nb, HD, 2, BLK))
    stacked = jnp.stack([s[:, :, 0] for s in sums] + [s[:, :, 1] for s in sums], axis=2)
    kv_grad = jnp.transpose(stacked, (0, 3, 2, 1)).reshape(span, 2 * kv_here * HD).astype(jnp.bfloat16)
    width = 2 * kv_here * HD

    query_out = lax.all_to_all(dq, "uly", split_axis=0, concat_axis=1, tiled=True)
    query_out, kv_grad = lax.optimization_barrier((query_out, kv_grad))
    kv_seq = lax.all_to_all(kv_grad, "uly", split_axis=0, concat_axis=1, tiled=True)
    rows_here = kv_seq.shape[0]
    lane_count = kv_seq.shape[1] // width
    spread = kv_seq.reshape(rows_here, lane_count, 2, kv_here * HD)

    def gather_heads(part):
        if heads_here >= GROUP:
            return part.reshape(rows_here, KVH * HD)
        lanes_per = GROUP // heads_here
        merged = part.astype(jnp.float32).reshape(rows_here, KVH, lanes_per, HD).sum(axis=2)
        return merged.reshape(rows_here, KVH * HD).astype(jnp.bfloat16)

    return (query_out, gather_heads(spread[:, :, 0]), gather_heads(spread[:, :, 1]))


def solution(mesh):
    return jax.shard_map(
        shards,
        mesh=mesh,
        in_specs=(P("ctx", "uly"), P("ctx", None), P("ctx", None), P("ctx", "uly"), P()),
        out_specs=(P(("ctx", "uly"), None), P(("ctx", "uly"), None), P(("ctx", "uly"), None)),
        check_vma=False,
    )
```

```python
import functools
import math

import jax
import jax.numpy as jnp
from jax import lax
from jax.experimental import pallas as pl
from jax.experimental.pallas import tpu as pltpu
from jax.sharding import PartitionSpec as P

HD = 128
KVH = 8
BLK = 128
GROUP = 6
SLOTS = 8


def attention_kernel(
    tbl_ref,
    q_ref, do_ref, k_ref, v_ref, ko_ref, vo_ref, dq_in,
    dq_ref, loc_ref, far_ref, fo_ref,
    kc_ref, vc_ref,
    *, hpk, kv_here, nb,
):
    g = pl.program_id(0)
    b = pl.program_id(1)
    scale = 1.0 / math.sqrt(HD)
    count = nb * SLOTS

    def blk_ref(i):
        return tbl_ref[i]

    def side_ref(i):
        return tbl_ref[count + i]

    def dst_ref(i):
        return tbl_ref[2 * count + i]

    def kind_ref(i):
        return tbl_ref[3 * count + i]

    @pl.when(b == 0)
    def _():
        loc_ref[...] = jnp.zeros_like(loc_ref)
        far_ref[...] = jnp.zeros_like(far_ref)
        fo_ref[...] = jnp.zeros_like(fo_ref)

    for s in range(SLOTS):
        row = pl.multiple_of(blk_ref(b * SLOTS + s) * BLK, BLK)
        side = side_ref(b * SLOTS + s)
        for code, tk, tv in ((0, k_ref, v_ref), (1, ko_ref, vo_ref)):
            @pl.when(side == code)
            def _():
                kc_ref[s * BLK:(s + 1) * BLK, :] = tk[pl.ds(row, BLK), :]
                vc_ref[s * BLK:(s + 1) * BLK, :] = tv[pl.ds(row, BLK), :]

    kc = kc_ref[...]
    vc = vc_ref[...]
    qs = jnp.concatenate([q_ref[:, h * HD:(h + 1) * HD] for h in range(hpk)], axis=0)
    dos = jnp.concatenate([do_ref[:, h * HD:(h + 1) * HD] for h in range(hpk)], axis=0)
    nt = (((1,), (1,)), ((), ()))
    tn = (((0,), (0,)), ((), ()))
    scores = lax.dot_general(qs, kc, nt, preferred_element_type=jnp.float32) * scale
    peak = jnp.max(scores, axis=1, keepdims=True)
    lifted = jnp.exp(scores - peak)
    probs = lifted * (1.0 / jnp.sum(lifted, axis=1, keepdims=True))
    probs_b = probs.astype(jnp.bfloat16)
    attended = jnp.dot(probs_b, vc, preferred_element_type=jnp.float32)
    delta = jnp.sum(dos.astype(jnp.float32) * attended, axis=1, keepdims=True)
    dprobs = lax.dot_general(dos, vc, nt, preferred_element_type=jnp.float32)
    dscores = (probs * (dprobs - delta) * scale).astype(jnp.bfloat16)
    dq = jnp.dot(dscores, kc, preferred_element_type=jnp.float32)
    for h in range(hpk):
        dq_ref[:, h * HD:(h + 1) * HD] = dq[h * BLK:(h + 1) * BLK].astype(jnp.bfloat16)
    kterm = lax.dot_general(qs, dscores, tn, preferred_element_type=jnp.float32)
    vterm = lax.dot_general(dos, probs_b, tn, preferred_element_type=jnp.float32)

    for s in range(SLOTS):
        kind = kind_ref(b * SLOTS + s)
        row = pl.multiple_of(dst_ref(b * SLOTS + s) * BLK, BLK)
        kt = kterm[:, s * BLK:(s + 1) * BLK]
        vt = vterm[:, s * BLK:(s + 1) * BLK]
        rounded = kind == 0
        kt = jnp.where(rounded, kt.astype(jnp.bfloat16).astype(jnp.float32), kt)
        vt = jnp.where(rounded, vt.astype(jnp.bfloat16).astype(jnp.float32), vt)

        side = side_ref(b * SLOTS + s)

        @pl.when(kind == 2)
        def _():
            loc_ref[pl.ds(row, BLK), 0:HD] += kt
            loc_ref[pl.ds(row, BLK), HD:2 * HD] += vt

        for code, out in ((0, far_ref), (1, fo_ref)):
            @pl.when((kind != 2) & (side == code))
            def _():
                kk = out[pl.ds(row, BLK), 0:HD].astype(jnp.float32) + kt
                out[pl.ds(row, BLK), 0:HD] = kk.astype(jnp.bfloat16)
                vv = out[pl.ds(row, BLK), HD:2 * HD].astype(jnp.float32) + vt
                out[pl.ds(row, BLK), HD:2 * HD] = vv.astype(jnp.bfloat16)


def shards(query_rows, key_rows, value_rows, out_grad, block_list):
    shard_index = lax.axis_index("ctx")
    lane_index = lax.axis_index("uly")
    nb = key_rows.shape[0] // BLK
    seq = block_list.shape[0] * BLK
    heads_here = query_rows.shape[1] // HD
    kv_here = max(1, heads_here // GROUP)
    hpk = heads_here // kv_here
    width = 2 * kv_here * HD
    first_kv = lane_index * heads_here // GROUP
    shard_count = lax.axis_size("ctx")
    partner = [(i, i ^ 1) for i in range(shard_count)]
    core = shard_index % 2
    members = shard_count // 2
    member = shard_index // 2
    half = seq // 2
    span = nb * BLK

    rows = lax.dynamic_slice_in_dim(block_list, shard_index * nb, nb, axis=0).astype(jnp.int32)
    owner = rows // nb
    cols = jnp.arange(SLOTS)[None, :]
    is_global = (cols == 3) | (cols == 4)
    local = owner == shard_index
    remote = jnp.logical_not(local) & jnp.logical_not(is_global)
    kind = jnp.where(local, 2, jnp.where(remote, 0, 1)).astype(jnp.int32).reshape(-1)
    owner_side = (owner % 2 != core).astype(jnp.int32)
    half_row = ((member - owner // 2) % members) * nb + rows % nb
    dst = jnp.where(local, rows - shard_index * nb, half_row).astype(jnp.int32).reshape(-1)
    blk = half_row.astype(jnp.int32).reshape(-1)
    side = owner_side.reshape(-1)
    table = jnp.concatenate([blk, side, dst, kind]).astype(jnp.int32)

    kernel = functools.partial(attention_kernel, hpk=hpk, kv_here=1, nb=nb)
    dq = jnp.zeros((nb * BLK, heads_here * HD), jnp.bfloat16)
    sums = []
    kv_own = jnp.concatenate(
        [
            lax.dynamic_slice_in_dim(key_rows, first_kv * HD, kv_here * HD, axis=1),
            lax.dynamic_slice_in_dim(value_rows, first_kv * HD, kv_here * HD, axis=1),
        ],
        axis=1,
    )
    gathered = [kv_own]
    for d in range(1, members):
        pairs = [(i, (i + 2 * d) % shard_count) for i in range(shard_count)]
        gathered.append(lax.ppermute(kv_own, "ctx", pairs))
    kv_half = jnp.concatenate(gathered, axis=0)
    kv_other = lax.ppermute(kv_half, "ctx", partner)
    for g in range(kv_here):
        grid_spec = pltpu.PrefetchScalarGridSpec(
            num_scalar_prefetch=1,
            grid=(1, nb),
            in_specs=[
                pl.BlockSpec((BLK, hpk * HD), lambda z, b, *_, g=g: (b, g)),
                pl.BlockSpec((BLK, hpk * HD), lambda z, b, *_, g=g: (b, g)),
                pl.BlockSpec((half, HD), lambda z, b, *_, g=g: (0, g)),
                pl.BlockSpec((half, HD), lambda z, b, *_, g=g: (0, kv_here + g)),
                pl.BlockSpec((half, HD), lambda z, b, *_, g=g: (0, g)),
                pl.BlockSpec((half, HD), lambda z, b, *_, g=g: (0, kv_here + g)),
                pl.BlockSpec(memory_space=pl.ANY),
            ],
            out_specs=[
                pl.BlockSpec((BLK, hpk * HD), lambda z, b, *_, g=g: (b, g)),
                pl.BlockSpec((span, 2 * HD), lambda z, b, *_: (0, 0)),
                pl.BlockSpec((half, 2 * HD), lambda z, b, *_: (0, 0)),
                pl.BlockSpec((half, 2 * HD), lambda z, b, *_: (0, 0)),
            ],
            scratch_shapes=[
                pltpu.VMEM((SLOTS * BLK, HD), jnp.bfloat16),
                pltpu.VMEM((SLOTS * BLK, HD), jnp.bfloat16),
            ],
        )
        dq, loc, far, far_other = pl.pallas_call(
            kernel,
            grid_spec=grid_spec,
            out_shape=[
                jax.ShapeDtypeStruct((nb * BLK, heads_here * HD), jnp.bfloat16),
                jax.ShapeDtypeStruct((span, 2 * HD), jnp.float32),
                jax.ShapeDtypeStruct((half, 2 * HD), jnp.bfloat16),
                jax.ShapeDtypeStruct((half, 2 * HD), jnp.bfloat16),
            ],
            input_output_aliases={7: 0},
            cost_estimate=pl.CostEstimate(
                flops=12 * nb * hpk * BLK * SLOTS * BLK * HD,
                transcendentals=nb * hpk * BLK * SLOTS * BLK,
                bytes_accessed=4 * nb * BLK * hpk * HD + 4 * half * HD * 2 + 12 * half * HD,
            ),
            compiler_params=pltpu.CompilerParams(dimension_semantics=("arbitrary", "arbitrary")),
        )(table, query_rows, out_grad, kv_half, kv_half, kv_other, kv_other, dq)
        from_partner = lax.ppermute(far_other, "ctx", partner)
        mine = (far.astype(jnp.float32) + from_partner.astype(jnp.float32)).astype(jnp.bfloat16)
        total = far[0:span].astype(jnp.float32) + from_partner[0:span].astype(jnp.float32)
        for d in range(1, members):
            pairs = [(i, (i - 2 * d) % shard_count) for i in range(shard_count)]
            total = total + lax.ppermute(
                mine[d * span:(d + 1) * span], "ctx", pairs
            ).astype(jnp.float32)
        sums.append((total + loc).reshape(nb, HD, 2, BLK))
    stacked = jnp.stack([s[:, :, 0] for s in sums] + [s[:, :, 1] for s in sums], axis=2)
    kv_grad = jnp.transpose(stacked, (0, 3, 2, 1)).reshape(span, 2 * kv_here * HD).astype(jnp.bfloat16)
    width = 2 * kv_here * HD

    query_out = lax.all_to_all(dq, "uly", split_axis=0, concat_axis=1, tiled=True)
    query_out, kv_grad = lax.optimization_barrier((query_out, kv_grad))
    kv_seq = lax.all_to_all(kv_grad, "uly", split_axis=0, concat_axis=1, tiled=True)
    rows_here = kv_seq.shape[0]
    lane_count = kv_seq.shape[1] // width
    spread = kv_seq.reshape(rows_here, lane_count, 2, kv_here * HD)

    def gather_heads(part):
        if heads_here >= GROUP:
            return part.reshape(rows_here, KVH * HD)
        lanes_per = GROUP // heads_here
        merged = part.astype(jnp.float32).reshape(rows_here, KVH, lanes_per, HD).sum(axis=2)
        return merged.reshape(rows_here, KVH * HD).astype(jnp.bfloat16)

    return (query_out, gather_heads(spread[:, :, 0]), gather_heads(spread[:, :, 1]))


def solution(mesh):
    return jax.shard_map(
        shards,
        mesh=mesh,
        in_specs=(P("ctx", "uly"), P("ctx", None), P("ctx", None), P("ctx", "uly"), P()),
        out_specs=(P(("ctx", "uly"), None), P(("ctx", "uly"), None), P(("ctx", "uly"), None)),
        check_vma=False,
    )
```

```python
import functools
import math

import jax
import jax.numpy as jnp
from jax import lax
from jax.experimental import pallas as pl
from jax.experimental.pallas import tpu as pltpu
from jax.sharding import PartitionSpec as P

HD = 128
KVH = 8
BLK = 128
GROUP = 6
SLOTS = 8


def attention_kernel(
    tbl_ref,
    q_ref, do_ref, k_ref, v_ref, ko_ref, vo_ref, dq_in,
    dq_ref, loc_ref, far_ref, fo_ref,
    kc_ref, vc_ref,
    *, hpk, kv_here, nb,
):
    g = pl.program_id(0)
    b = pl.program_id(1)
    scale = 1.0 / math.sqrt(HD)
    count = nb * SLOTS

    def blk_ref(i):
        return tbl_ref[i]

    def side_ref(i):
        return tbl_ref[count + i]

    def dst_ref(i):
        return tbl_ref[2 * count + i]

    def kind_ref(i):
        return tbl_ref[3 * count + i]

    @pl.when(b == 0)
    def _():
        loc_ref[...] = jnp.zeros_like(loc_ref)
        far_ref[...] = jnp.zeros_like(far_ref)
        fo_ref[...] = jnp.zeros_like(fo_ref)

    for s in range(SLOTS):
        row = pl.multiple_of(blk_ref(b * SLOTS + s) * BLK, BLK)
        side = side_ref(b * SLOTS + s)
        for code, tk, tv in ((0, k_ref, v_ref), (1, ko_ref, vo_ref)):
            @pl.when(side == code)
            def _():
                kc_ref[s * BLK:(s + 1) * BLK, :] = tk[pl.ds(row, BLK), :]
                vc_ref[s * BLK:(s + 1) * BLK, :] = tv[pl.ds(row, BLK), :]

    kc = kc_ref[...]
    vc = vc_ref[...]
    qs = jnp.concatenate([q_ref[:, h * HD:(h + 1) * HD] for h in range(hpk)], axis=0)
    dos = jnp.concatenate([do_ref[:, h * HD:(h + 1) * HD] for h in range(hpk)], axis=0)
    nt = (((1,), (1,)), ((), ()))
    tn = (((0,), (0,)), ((), ()))
    scores = lax.dot_general(qs, kc, nt, preferred_element_type=jnp.float32) * scale
    peak = jnp.max(scores, axis=1, keepdims=True)
    lifted = jnp.exp(scores - peak)
    probs = lifted * (1.0 / jnp.sum(lifted, axis=1, keepdims=True))
    probs_b = probs.astype(jnp.bfloat16)
    attended = jnp.dot(probs_b, vc, preferred_element_type=jnp.float32)
    delta = jnp.sum(dos.astype(jnp.float32) * attended, axis=1, keepdims=True)
    dprobs = lax.dot_general(dos, vc, nt, preferred_element_type=jnp.float32)
    dscores = (probs * (dprobs - delta) * scale).astype(jnp.bfloat16)
    dq = jnp.dot(dscores, kc, preferred_element_type=jnp.float32)
    for h in range(hpk):
        dq_ref[:, h * HD:(h + 1) * HD] = dq[h * BLK:(h + 1) * BLK].astype(jnp.bfloat16)
    kterm = lax.dot_general(qs, dscores, tn, preferred_element_type=jnp.float32)
    vterm = lax.dot_general(dos, probs_b, tn, preferred_element_type=jnp.float32)

    for s in range(SLOTS):
        kind = kind_ref(b * SLOTS + s)
        row = pl.multiple_of(dst_ref(b * SLOTS + s) * BLK, BLK)
        kt = kterm[:, s * BLK:(s + 1) * BLK]
        vt = vterm[:, s * BLK:(s + 1) * BLK]

        side = side_ref(b * SLOTS + s)

        @pl.when(kind == 2)
        def _():
            loc_ref[pl.ds(row, BLK), 0:HD] += kt
            loc_ref[pl.ds(row, BLK), HD:2 * HD] += vt

        for code, out in ((0, far_ref), (1, fo_ref)):
            for round_it in (True, False):
                @pl.when((kind == (0 if round_it else 1)) & (side == code))
                def _():
                    ka, va = kt, vt
                    if round_it:
                        ka = ka.astype(jnp.bfloat16).astype(jnp.float32)
                        va = va.astype(jnp.bfloat16).astype(jnp.float32)
                    kk = out[pl.ds(row, BLK), 0:HD].astype(jnp.float32) + ka
                    out[pl.ds(row, BLK), 0:HD] = kk.astype(jnp.bfloat16)
                    vv = out[pl.ds(row, BLK), HD:2 * HD].astype(jnp.float32) + va
                    out[pl.ds(row, BLK), HD:2 * HD] = vv.astype(jnp.bfloat16)


def shards(query_rows, key_rows, value_rows, out_grad, block_list):
    shard_index = lax.axis_index("ctx")
    lane_index = lax.axis_index("uly")
    nb = key_rows.shape[0] // BLK
    seq = block_list.shape[0] * BLK
    heads_here = query_rows.shape[1] // HD
    kv_here = max(1, heads_here // GROUP)
    hpk = heads_here // kv_here
    width = 2 * kv_here * HD
    first_kv = lane_index * heads_here // GROUP
    shard_count = lax.axis_size("ctx")
    partner = [(i, i ^ 1) for i in range(shard_count)]
    core = shard_index % 2
    members = shard_count // 2
    member = shard_index // 2
    half = seq // 2
    span = nb * BLK

    rows = lax.dynamic_slice_in_dim(block_list, shard_index * nb, nb, axis=0).astype(jnp.int32)
    owner = rows // nb
    cols = jnp.arange(SLOTS)[None, :]
    is_global = (cols == 3) | (cols == 4)
    local = owner == shard_index
    remote = jnp.logical_not(local) & jnp.logical_not(is_global)
    kind = jnp.where(local, 2, jnp.where(remote, 0, 1)).astype(jnp.int32).reshape(-1)
    owner_side = (owner % 2 != core).astype(jnp.int32)
    half_row = ((member - owner // 2) % members) * nb + rows % nb
    dst = jnp.where(local, rows - shard_index * nb, half_row).astype(jnp.int32).reshape(-1)
    blk = half_row.astype(jnp.int32).reshape(-1)
    side = owner_side.reshape(-1)
    table = jnp.concatenate([blk, side, dst, kind]).astype(jnp.int32)

    kernel = functools.partial(attention_kernel, hpk=hpk, kv_here=1, nb=nb)
    dq = jnp.zeros((nb * BLK, heads_here * HD), jnp.bfloat16)
    sums = []
    for g in range(kv_here):
        col = (first_kv + g) * HD
        kv_own = jnp.concatenate(
            [
                lax.dynamic_slice_in_dim(key_rows, col, HD, axis=1),
                lax.dynamic_slice_in_dim(value_rows, col, HD, axis=1),
            ],
            axis=1,
        )
        gathered = [kv_own]
        for d in range(1, members):
            pairs = [(i, (i + 2 * d) % shard_count) for i in range(shard_count)]
            gathered.append(lax.ppermute(kv_own, "ctx", pairs))
        kv_half = jnp.concatenate(gathered, axis=0)
        kv_other = lax.ppermute(kv_half, "ctx", partner)
        if g > 0:
            kv_half, kv_other, dq = lax.optimization_barrier((kv_half, kv_other, dq))
        grid_spec = pltpu.PrefetchScalarGridSpec(
            num_scalar_prefetch=1,
            grid=(1, nb),
            in_specs=[
                pl.BlockSpec((BLK, hpk * HD), lambda z, b, *_, g=g: (b, g)),
                pl.BlockSpec((BLK, hpk * HD), lambda z, b, *_, g=g: (b, g)),
                pl.BlockSpec((half, HD), lambda z, b, *_: (0, 0)),
                pl.BlockSpec((half, HD), lambda z, b, *_: (0, 1)),
                pl.BlockSpec((half, HD), lambda z, b, *_: (0, 0)),
                pl.BlockSpec((half, HD), lambda z, b, *_: (0, 1)),
                pl.BlockSpec(memory_space=pl.ANY),
            ],
            out_specs=[
                pl.BlockSpec((BLK, hpk * HD), lambda z, b, *_, g=g: (b, g)),
                pl.BlockSpec((span, 2 * HD), lambda z, b, *_: (0, 0)),
                pl.BlockSpec((half, 2 * HD), lambda z, b, *_: (0, 0)),
                pl.BlockSpec((half, 2 * HD), lambda z, b, *_: (0, 0)),
            ],
            scratch_shapes=[
                pltpu.VMEM((SLOTS * BLK, HD), jnp.bfloat16),
                pltpu.VMEM((SLOTS * BLK, HD), jnp.bfloat16),
            ],
        )
        dq, loc, far, far_other = pl.pallas_call(
            kernel,
            grid_spec=grid_spec,
            out_shape=[
                jax.ShapeDtypeStruct((nb * BLK, heads_here * HD), jnp.bfloat16),
                jax.ShapeDtypeStruct((span, 2 * HD), jnp.float32),
                jax.ShapeDtypeStruct((half, 2 * HD), jnp.bfloat16),
                jax.ShapeDtypeStruct((half, 2 * HD), jnp.bfloat16),
            ],
            input_output_aliases={7: 0},
            cost_estimate=pl.CostEstimate(
                flops=12 * nb * hpk * BLK * SLOTS * BLK * HD,
                transcendentals=nb * hpk * BLK * SLOTS * BLK,
                bytes_accessed=4 * nb * BLK * hpk * HD + 4 * half * HD * 2 + 12 * half * HD,
            ),
            compiler_params=pltpu.CompilerParams(dimension_semantics=("arbitrary", "arbitrary")),
        )(table, query_rows, out_grad, kv_half, kv_half, kv_other, kv_other, dq)
        from_partner = lax.ppermute(far_other, "ctx", partner)
        mine = (far.astype(jnp.float32) + from_partner.astype(jnp.float32)).astype(jnp.bfloat16)
        total = far[0:span].astype(jnp.float32) + from_partner[0:span].astype(jnp.float32)
        for d in range(1, members):
            pairs = [(i, (i - 2 * d) % shard_count) for i in range(shard_count)]
            total = total + lax.ppermute(
                mine[d * span:(d + 1) * span], "ctx", pairs
            ).astype(jnp.float32)
        sums.append((total + loc).reshape(nb, HD, 2, BLK))
    stacked = jnp.stack([s[:, :, 0] for s in sums] + [s[:, :, 1] for s in sums], axis=2)
    kv_grad = jnp.transpose(stacked, (0, 3, 2, 1)).reshape(span, 2 * kv_here * HD).astype(jnp.bfloat16)
    width = 2 * kv_here * HD

    query_out = lax.all_to_all(dq, "uly", split_axis=0, concat_axis=1, tiled=True)
    query_out, kv_grad = lax.optimization_barrier((query_out, kv_grad))
    kv_seq = lax.all_to_all(kv_grad, "uly", split_axis=0, concat_axis=1, tiled=True)
    rows_here = kv_seq.shape[0]
    lane_count = kv_seq.shape[1] // width
    spread = kv_seq.reshape(rows_here, lane_count, 2, kv_here * HD)

    def gather_heads(part):
        if heads_here >= GROUP:
            return part.reshape(rows_here, KVH * HD)
        lanes_per = GROUP // heads_here
        merged = part.astype(jnp.float32).reshape(rows_here, KVH, lanes_per, HD).sum(axis=2)
        return merged.reshape(rows_here, KVH * HD).astype(jnp.bfloat16)

    return (query_out, gather_heads(spread[:, :, 0]), gather_heads(spread[:, :, 1]))


def solution(mesh):
    return jax.shard_map(
        shards,
        mesh=mesh,
        in_specs=(P("ctx", "uly"), P("ctx", None), P("ctx", None), P("ctx", "uly"), P()),
        out_specs=(P(("ctx", "uly"), None), P(("ctx", "uly"), None), P(("ctx", "uly"), None)),
        check_vma=False,
    )
```
